32 devices in a mesh: groups: 2 (over y), ctx: 4 (over z), head: 2 (over x), dp: 2 (over core).
Axes of the slice: x: 2, y: 2, z: 4, core: 2. Of those that a mesh axis runs over, the one named last changes fastest.
Arguments:
- query_rows: bfloat16 [8192, 4096], P(('groups', 'ctx', 'dp'), 'head'), parts along dimension 0, may hold values from -6 to 6
- key_rows: bfloat16 [8192, 4096], P(('groups', 'ctx', 'dp'), 'head'), parts along dimension 0, may hold values from -6 to 6
- value_rows: bfloat16 [8192, 4096], P(('groups', 'ctx', 'dp'), 'head'), parts along dimension 0, may hold values from -6 to 6
- cotangent: bfloat16 [8192, 4096], P(('groups', 'ctx', 'dp'), 'head'), parts along dimension 0, may hold values from -6 to 6
- log_decay: float32 [8192, 32], P(('groups', 'ctx', 'dp'), 'head'), parts along dimension 0, may hold values from -0.7 to 0, as said below
- norm_gain: float32 [4096], P('head'), may hold values from 0.1 to 1.9
Outputs:
- query_grad: bfloat16 [8192, 4096], P(('groups', 'ctx', 'dp'), 'head'), parts along dimension 0
- key_grad: bfloat16 [8192, 4096], P(('groups', 'ctx', 'dp'), 'head'), parts along dimension 0
- value_grad: bfloat16 [8192, 4096], P(('groups', 'ctx', 'dp'), 'head'), parts along dimension 0
- gain_grad: float32 [8192], P(('groups', 'head')), parts along dimension 0
The draws below stay inside these ranges and needn't reach their ends.
There are 2 independent parts, one for each index of `groups`. The reference program is written for one: setup_inputs(seed, part) draws one part's arguments, and reference() takes and returns one part's arrays. A program takes and returns all parts, laid end to end along the dimension named above; an argument that names none is the same for every part. Nothing has to cross between parts.
Inputs may be any that keep to these rules, and one draw needn't show every extreme that they name: `log_decay`: every entry is negative.
All inputs are finite; a program needn't handle non-finite values.
Results may differ from the reference program's by a relative error of at most 0.0062.
Values sent between devices are 32-bit elements; how exact they have to be, the bound alone decides.
No kernel may reach another device: no remote copies, remote signals or barrier semaphores. Data moves between devices by JAX's collectives and lax.ppermute only.
A program may use at most 128 MiB of HBM per device.

```python
import math
import jax
import jax.numpy as jnp
from jax import lax

LOCAL_HEADS = 32
DH = 128
T_DEV = 512
SEQUENCE_LENGTH = 4096


def draw_log_decay(key, part):
    random_subkeys = jax.random.split(key, 8)
    ranking = jax.random.permutation(random_subkeys[0], LOCAL_HEADS)
    fast_count = max(LOCAL_HEADS // 8, 1)
    slow_count = max(3 * LOCAL_HEADS // 8, 1)
    middle_rate = jax.random.uniform(random_subkeys[7], (LOCAL_HEADS,), jnp.float32, 2.3, 3.0) / T_DEV
    middle_count = LOCAL_HEADS - fast_count - slow_count
    fast_head = ranking < fast_count
    middle_head = (ranking >= fast_count) & (ranking < fast_count + middle_count)
    slow_rate = jax.random.uniform(random_subkeys[1], (LOCAL_HEADS,), jnp.float32, 0.05, 0.4) * (math.log(10.0) / SEQUENCE_LENGTH)
    fast_rate = jax.random.uniform(random_subkeys[2], (LOCAL_HEADS,), jnp.float32, 1.0 / 50.0, 1.0 / 30.0)
    decay_rate = jnp.where(fast_head, fast_rate, jnp.where(middle_head, middle_rate, slow_rate))
    block_count = SEQUENCE_LENGTH // T_DEV
    block_factor = jnp.exp(jax.random.uniform(random_subkeys[3], (block_count, 1, LOCAL_HEADS), jnp.float32, -0.7, 0.7))
    cell_factor = jnp.exp(jax.random.uniform(random_subkeys[4], (block_count, T_DEV, LOCAL_HEADS), jnp.float32, -0.5, 0.5))
    stable_decay = -(decay_rate[None, None, :] * block_factor * cell_factor).reshape(SEQUENCE_LENGTH, LOCAL_HEADS)
    stable_decay = jnp.maximum(stable_decay, -0.7)
    surge_position = jax.random.randint(random_subkeys[5], (2,), 0, SEQUENCE_LENGTH)
    surging_flag = jnp.any(jnp.arange(SEQUENCE_LENGTH)[:, None] == surge_position[None, :], axis=1)
    surge_log_value = jnp.log(jax.random.uniform(random_subkeys[6], (SEQUENCE_LENGTH, LOCAL_HEADS), jnp.float32, 0.55, 0.8))
    sluggish_head = jnp.logical_not(fast_head)
    return jnp.where(surging_flag[:, None] & sluggish_head[None, :], surge_log_value, stable_decay)


def shard_levels(own_key, shape, shards, smallest, top_value):
    def one(position, blocks):
        heights = jax.random.uniform(jax.random.fold_in(jax.random.fold_in(own_key, 6), position), (blocks,), jnp.float32, smallest / len(shards), top_value / len(shards))
        return jnp.repeat(jnp.exp(heights), shape[position] // blocks).reshape((-1,) + (1,) * (len(shape) - position - 1))

    loudness = one(*shards[0])
    for cut in shards[1:]:
        loudness = loudness * one(*cut)
    return loudness


def noise(key, shape, deviation, bound, cuts=(), kind=jnp.bfloat16):
    array = deviation * jax.random.normal(key, shape, jnp.float32)
    if cuts:
        array = array * shard_levels(key, shape, cuts, -0.22, 0.18)
    return jnp.clip(array, -bound, bound).astype(kind)


def setup_inputs(seed: int = 0, part: int = 0) -> dict:
    streams_of = jax.random.split(jax.random.key(seed), 7)
    own_keys = jax.random.split(jax.random.fold_in(streams_of[6], part), 7)
    return {
        "query_rows": noise(own_keys[0], (SEQUENCE_LENGTH, LOCAL_HEADS * DH), 1.0, 6.0, ((0, 8), (1, 2))),
        "key_rows": noise(own_keys[1], (SEQUENCE_LENGTH, LOCAL_HEADS * DH), 1.0, 6.0, ((0, 8), (1, 2))),
        "value_rows": noise(own_keys[2], (SEQUENCE_LENGTH, LOCAL_HEADS * DH), 1.0, 6.0, ((0, 8), (1, 2))),
        "cotangent": noise(own_keys[3], (SEQUENCE_LENGTH, LOCAL_HEADS * DH), 1.0, 6.0, ((0, 8), (1, 2))),
        "log_decay": draw_log_decay(jax.random.fold_in(jax.random.fold_in(streams_of[6], part), 71), part),
        "norm_gain": jnp.clip(1.0 + 0.18 * jax.random.normal(streams_of[5], (LOCAL_HEADS * DH,), jnp.float32), 0.1, 1.9),
    }


epsilon = 1e-06

def decay_parts(decay_log):
    cumulated = jnp.cumsum(decay_log, axis=0)
    final_log = cumulated[-1]
    by_head = cumulated.T
    spread = by_head[:, :, None] - by_head[:, None, :]
    length = decay_log.shape[0]
    causal = (jnp.arange(length)[:, None] >= jnp.arange(length)[None, :])[None]
    decay_mat = jnp.where(causal, jnp.exp(jnp.where(causal, spread, 0.0)), 0.0)
    return (cumulated, final_log, decay_mat)

def forward_block(query_blk, key_blk, value_blk, decay_log, state_in):
    cumulated, final_log, decay_mat = decay_parts(decay_log)
    to_end = jnp.exp(final_log[None, :] - cumulated)
    query_f = query_blk.astype(jnp.float32)
    key_f = key_blk.astype(jnp.float32)
    value_f = value_blk.astype(jnp.float32)
    scores = jnp.einsum('thd,shd->hts', query_f, key_f)
    masked = (scores * decay_mat).astype(jnp.bfloat16)
    intra = jnp.einsum('hts,she->the', masked.astype(jnp.float32), value_f)
    state_low = state_in.astype(jnp.bfloat16)
    attended = intra + jnp.exp(cumulated)[:, :, None] * jnp.einsum('thd,hde->the', query_f, state_low.astype(jnp.float32))
    key_scaled = (key_f * to_end[:, :, None]).astype(jnp.bfloat16)
    local_state = jnp.einsum('shd,she->hde', key_scaled.astype(jnp.float32), value_f)
    return (attended, local_state, jnp.exp(final_log), masked, decay_mat, cumulated, to_end, state_low)

def norm_backward(attended, grad_blk, gain_heads):
    root_mean = jnp.sqrt(lax.optimization_barrier(jnp.mean(attended * attended, axis=-1, keepdims=True)) + epsilon)
    normed = attended / root_mean
    grad_f = grad_blk.astype(jnp.float32)
    scaled = gain_heads[None] * grad_f
    projected = lax.optimization_barrier(jnp.sum(scaled * attended, axis=-1, keepdims=True))
    width = attended.shape[-1]
    out_grad = ((scaled - attended * projected / (width * root_mean * root_mean)) / root_mean).astype(jnp.bfloat16)
    gain_part = lax.optimization_barrier(jnp.sum(grad_f * normed, axis=0))
    return (out_grad, gain_part)

def reference(query_rows, key_rows, value_rows, cotangent, log_decay, norm_gain):
    block_count = SEQUENCE_LENGTH // T_DEV
    shaped = (block_count, T_DEV, LOCAL_HEADS, DH)
    query_b = query_rows.reshape(shaped)
    key_b = key_rows.reshape(shaped)
    value_b = value_rows.reshape(shaped)
    grad_b = cotangent.reshape(shaped)
    decay_b = log_decay.reshape(block_count, T_DEV, LOCAL_HEADS)
    gain_heads = norm_gain.reshape(LOCAL_HEADS, DH)
    zero_state = jnp.zeros((LOCAL_HEADS, DH, DH), jnp.float32)

    def forward_step(state, pieces):
        query_blk, key_blk, value_blk, decay_log = pieces
        result = forward_block(query_blk, key_blk, value_blk, decay_log, state)
        return (result[2][:, None, None] * state + result[1], state)
    _, states_in = lax.scan(forward_step, zero_state, (query_b, key_b, value_b, decay_b))

    def middle(pieces):
        query_blk, key_blk, value_blk, decay_log, grad_blk, state_in = pieces
        result = forward_block(query_blk, key_blk, value_blk, decay_log, state_in)
        out_grad, gain_part = norm_backward(result[0], grad_blk, gain_heads)
        query_scaled = (query_blk.astype(jnp.float32) * jnp.exp(result[5])[:, :, None]).astype(jnp.bfloat16)
        moment = jnp.einsum('thd,the->hde', query_scaled.astype(jnp.float32), out_grad.astype(jnp.float32))
        return (out_grad, gain_part, moment, result[2])
    out_grads, gain_parts, moments, totals = lax.map(middle, (query_b, key_b, value_b, decay_b, grad_b, states_in))

    def backward_step(grad_state, pieces):
        moment, total = pieces
        return (total[:, None, None] * grad_state + moment, grad_state)
    _, grad_states = lax.scan(backward_step, zero_state, (moments, totals), reverse=True)

    def gradients(pieces):
        query_blk, key_blk, value_blk, decay_log, out_grad, state_in, grad_state = pieces
        result = forward_block(query_blk, key_blk, value_blk, decay_log, state_in)
        masked, decay_mat, cumulated, to_end, state_low = (result[3], result[4], result[5], result[6], result[7])
        query_f = query_blk.astype(jnp.float32)
        key_f = key_blk.astype(jnp.float32)
        value_f = value_blk.astype(jnp.float32)
        out_f = out_grad.astype(jnp.float32)
        grad_low = grad_state.astype(jnp.bfloat16).astype(jnp.float32)
        dots = jnp.einsum('the,she->hts', out_f, value_f)
        rgrad = (dots * decay_mat).astype(jnp.bfloat16).astype(jnp.float32)
        query_grad = jnp.einsum('hts,shd->thd', rgrad, key_f) + jnp.exp(cumulated)[:, :, None] * jnp.einsum('the,hde->thd', out_f, state_low.astype(jnp.float32))
        key_grad = jnp.einsum('hts,thd->shd', rgrad, query_f) + to_end[:, :, None] * jnp.einsum('she,hde->shd', value_f, grad_low)
        value_grad = jnp.einsum('hts,the->she', masked.astype(jnp.float32), out_f) + to_end[:, :, None] * jnp.einsum('shd,hde->she', key_f, grad_low)
        return (query_grad.astype(jnp.bfloat16), key_grad.astype(jnp.bfloat16), value_grad.astype(jnp.bfloat16))
    query_grad, key_grad, value_grad = lax.map(gradients, (query_b, key_b, value_b, decay_b, out_grads, states_in, grad_states))
    gain_grad = lax.optimization_barrier(jnp.sum(gain_parts, axis=0)).reshape(LOCAL_HEADS * DH) * (1.0 / math.sqrt(SEQUENCE_LENGTH))
    return (query_grad.reshape(SEQUENCE_LENGTH, LOCAL_HEADS * DH), key_grad.reshape(SEQUENCE_LENGTH, LOCAL_HEADS * DH), value_grad.reshape(SEQUENCE_LENGTH, LOCAL_HEADS * DH), gain_grad)
```

```python
import math

import jax
import jax.numpy as jnp
from jax import lax
from jax.sharding import PartitionSpec as P

DH = 128
PAD = 8


epsilon = 1e-06


def decay_parts(decay_log):
    cumulated = jnp.cumsum(decay_log, axis=0)
    final_log = cumulated[-1]
    by_head = cumulated.T
    spread = by_head[:, :, None] - by_head[:, None, :]
    length = decay_log.shape[0]
    causal = (jnp.arange(length)[:, None] >= jnp.arange(length)[None, :])[None]
    decay_mat = jnp.where(causal, jnp.exp(jnp.where(causal, spread, 0.0)), 0.0)
    return (cumulated, final_log, decay_mat)


def swap_dp(x):
    return lax.ppermute(x, "dp", perm=[(0, 1), (1, 0)])


def pack_rows(core, *rows):
    heads = core.shape[0]
    pad = [jnp.broadcast_to(r.reshape(heads, 1, -1), (heads, 1, DH)) for r in rows]
    fill = jnp.zeros((heads, PAD - len(rows), DH), jnp.float32)
    return jnp.concatenate([core] + pad + [fill], axis=1)


def chip_prefix(message, later):
    gathered = lax.all_gather(message, "ctx")
    chips = gathered.shape[0]
    z = lax.axis_index("ctx")
    decay = gathered[:, :, DH, 0]
    before = jnp.cumsum(decay, axis=0) - decay
    index = jnp.arange(chips)[:, None]
    mine = jnp.sum(jnp.where(index == z, before, 0.0), axis=0)
    mine_decay = jnp.sum(jnp.where(index == z, decay, 0.0), axis=0)
    if later:
        valid = index > z
        spread = before - mine[None] - mine_decay[None]
    else:
        valid = index < z
        spread = mine[None] - before - decay
    weight = jnp.where(valid, jnp.exp(jnp.where(valid, spread, 0.0)), 0.0)
    total = jnp.sum(weight[:, :, None, None] * gathered[:, :, :DH, :], axis=0)
    return total, gathered


def halves(x, c):
    half = x.shape[0] // 2
    return lax.dynamic_slice_in_dim(x, c * half, half, axis=0)


def join_halves(mine, other, c):
    first = jnp.where(c == 0, mine, other)
    second = jnp.where(c == 0, other, mine)
    return jnp.concatenate([first, second], axis=0)


def forward_states(local_state, final_log):
    c = lax.axis_index("dp")
    message = pack_rows(local_state, final_log)
    other = swap_dp(message)
    own_state, other_state = local_state, other[:, :DH, :]
    own_fin, other_fin = final_log, other[:, DH, 0]
    first = jnp.where(c == 0, own_state, other_state)
    second = jnp.where(c == 0, other_state, own_state)
    fin_first = jnp.where(c == 0, own_fin, other_fin)
    fin_second = jnp.where(c == 0, other_fin, own_fin)
    chip_state = jnp.exp(fin_second)[:, None, None] * first + second
    chip_decay = fin_first + fin_second
    prefix_half, _ = chip_prefix(pack_rows(halves(chip_state, c), halves(chip_decay, c)), later=False)
    prefix = join_halves(prefix_half, swap_dp(prefix_half), c)
    core_one = jnp.exp(fin_first)[:, None, None] * prefix + first
    return jnp.where(c == 0, prefix, core_one)


def backward_states(moment, final_log, gain_part):
    c = lax.axis_index("dp")
    heads = moment.shape[0]
    gain_rows = gain_part.reshape(heads, DH)
    message = pack_rows(moment, final_log, gain_rows)
    other = swap_dp(message)
    own_m, other_m = moment, other[:, :DH, :]
    own_fin, other_fin = final_log, other[:, DH, 0]
    first = jnp.where(c == 0, own_m, other_m)
    second = jnp.where(c == 0, other_m, own_m)
    fin_first = jnp.where(c == 0, own_fin, other_fin)
    fin_second = jnp.where(c == 0, other_fin, own_fin)
    chip_gain = gain_rows + other[:, DH + 1, :]
    chip_state = first + jnp.exp(fin_first)[:, None, None] * second
    chip_decay = fin_first + fin_second
    suffix_half, gathered = chip_prefix(
        pack_rows(halves(chip_state, c), halves(chip_decay, c), halves(chip_gain, c)), later=True
    )
    gain_half = jnp.sum(gathered[:, :, DH + 1, :], axis=0)
    back = swap_dp(pack_rows(suffix_half, gain_half))
    suffix = join_halves(suffix_half, back[:, :DH, :], c)
    gain_total = join_halves(gain_half, back[:, DH, :], c)
    core_zero = second + jnp.exp(fin_second)[:, None, None] * suffix
    return jnp.where(c == 0, core_zero, suffix), gain_total.reshape(heads * DH)


def on_device(query_rows, key_rows, value_rows, cotangent, log_decay, norm_gain):
    length = query_rows.shape[0]
    heads = log_decay.shape[1]
    shaped = (length, heads, DH)
    query_blk = query_rows.reshape(shaped)
    key_blk = key_rows.reshape(shaped)
    value_blk = value_rows.reshape(shaped)
    grad_blk = cotangent.reshape(shaped)
    gain_heads = norm_gain.reshape(heads, DH)
    f32 = jnp.float32
    bf16 = jnp.bfloat16
    cumulated, final_log, decay_mat = decay_parts(log_decay)
    to_end = jnp.exp(final_log[None, :] - cumulated)
    grow_from = jnp.exp(cumulated)
    scores = jnp.einsum("thd,shd->hts", query_blk, key_blk, preferred_element_type=f32)
    masked = (scores * decay_mat).astype(bf16)
    intra = jnp.einsum("hts,she->the", masked, value_blk, preferred_element_type=f32)
    key_scaled = (key_blk.astype(f32) * to_end[:, :, None]).astype(bf16)
    local_state = jnp.einsum("shd,she->hde", key_scaled, value_blk, preferred_element_type=f32)
    state_in = forward_states(local_state, final_log)
    state_low = state_in.astype(bf16)
    attended = intra + grow_from[:, :, None] * jnp.einsum(
        "thd,hde->the", query_blk, state_low, preferred_element_type=f32
    )
    root_mean = jnp.sqrt(jnp.mean(attended * attended, axis=-1, keepdims=True) + epsilon)
    normed = attended / root_mean
    grad_f = grad_blk.astype(f32)
    scaled = gain_heads[None] * grad_f
    projected = jnp.sum(scaled * attended, axis=-1, keepdims=True)
    out_grad = ((scaled - attended * projected / (DH * root_mean * root_mean)) / root_mean).astype(
        bf16
    )
    gain_part = jnp.sum(grad_f * normed, axis=0).reshape(heads * DH)
    query_scaled = (query_blk.astype(f32) * grow_from[:, :, None]).astype(bf16)
    moment = jnp.einsum("thd,the->hde", query_scaled, out_grad, preferred_element_type=f32)
    grad_state, gain_sum = backward_states(moment, final_log, gain_part)
    grad_low = grad_state.astype(bf16)
    seq_total = length * lax.axis_size(("ctx", "dp"))
    gain_grad = gain_sum * (1.0 / math.sqrt(seq_total))
    dots = jnp.einsum("the,she->hts", out_grad, value_blk, preferred_element_type=f32)
    rgrad = (dots * decay_mat).astype(bf16)
    query_grad = jnp.einsum("hts,shd->thd", rgrad, key_blk, preferred_element_type=f32) + grow_from[
        :, :, None
    ] * jnp.einsum("the,hde->thd", out_grad, state_low, preferred_element_type=f32)
    key_grad = jnp.einsum("hts,thd->shd", rgrad, query_blk, preferred_element_type=f32) + to_end[
        :, :, None
    ] * jnp.einsum("she,hde->shd", value_blk, grad_low, preferred_element_type=f32)
    value_grad = jnp.einsum("hts,the->she", masked, out_grad, preferred_element_type=f32) + to_end[
        :, :, None
    ] * jnp.einsum("shd,hde->she", key_blk, grad_low, preferred_element_type=f32)
    flat = (length, heads * DH)
    return (
        query_grad.astype(bf16).reshape(flat),
        key_grad.astype(bf16).reshape(flat),
        value_grad.astype(bf16).reshape(flat),
        gain_grad,
    )


def solution(mesh):
    return jax.shard_map(
        on_device,
        mesh=mesh,
        in_specs=(
            P(("groups", "ctx", "dp"), "head"),
            P(("groups", "ctx", "dp"), "head"),
            P(("groups", "ctx", "dp"), "head"),
            P(("groups", "ctx", "dp"), "head"),
            P(("groups", "ctx", "dp"), "head"),
            P("head"),
        ),
        out_specs=(
            P(("groups", "ctx", "dp"), "head"),
            P(("groups", "ctx", "dp"), "head"),
            P(("groups", "ctx", "dp"), "head"),
            P(("groups", "head")),
        ),
        check_vma=False,
    )
```

```python
import math

import jax
import jax.numpy as jnp
from jax import lax
from jax.experimental import pallas as pl
from jax.sharding import PartitionSpec as P

DH = 128
PAD = 8


epsilon = 1e-06


def swap_dp(x):
    return lax.ppermute(x, "dp", perm=[(0, 1), (1, 0)])


def pack_rows(core, *rows):
    heads = core.shape[0]
    pad = [jnp.broadcast_to(r.reshape(heads, 1, -1), (heads, 1, DH)) for r in rows]
    fill = jnp.zeros((heads, PAD - len(rows), DH), jnp.float32)
    return jnp.concatenate([core] + pad + [fill], axis=1)


def chip_prefix(message, later):
    gathered = lax.all_gather(message, "ctx")
    chips = gathered.shape[0]
    z = lax.axis_index("ctx")
    decay = gathered[:, :, DH, 0]
    before = jnp.cumsum(decay, axis=0) - decay
    index = jnp.arange(chips)[:, None]
    mine = jnp.sum(jnp.where(index == z, before, 0.0), axis=0)
    mine_decay = jnp.sum(jnp.where(index == z, decay, 0.0), axis=0)
    if later:
        valid = index > z
        spread = before - mine[None] - mine_decay[None]
    else:
        valid = index < z
        spread = mine[None] - before - decay
    weight = jnp.where(valid, jnp.exp(jnp.where(valid, spread, 0.0)), 0.0)
    total = jnp.sum(weight[:, :, None, None] * gathered[:, :, :DH, :], axis=0)
    return total, gathered


def halves(x, c):
    half = x.shape[0] // 2
    return lax.dynamic_slice_in_dim(x, c * half, half, axis=0)


def join_halves(mine, other, c):
    first = jnp.where(c == 0, mine, other)
    second = jnp.where(c == 0, other, mine)
    return jnp.concatenate([first, second], axis=0)


def forward_states(local_state, final_log):
    c = lax.axis_index("dp")
    message = pack_rows(local_state, final_log)
    other = swap_dp(message)
    own_state, other_state = local_state, other[:, :DH, :]
    own_fin, other_fin = final_log, other[:, DH, 0]
    first = jnp.where(c == 0, own_state, other_state)
    second = jnp.where(c == 0, other_state, own_state)
    fin_first = jnp.where(c == 0, own_fin, other_fin)
    fin_second = jnp.where(c == 0, other_fin, own_fin)
    chip_state = jnp.exp(fin_second)[:, None, None] * first + second
    chip_decay = fin_first + fin_second
    prefix_half, _ = chip_prefix(pack_rows(halves(chip_state, c), halves(chip_decay, c)), later=False)
    prefix = join_halves(prefix_half, swap_dp(prefix_half), c)
    core_one = jnp.exp(fin_first)[:, None, None] * prefix + first
    return jnp.where(c == 0, prefix, core_one)


def backward_states(moment, final_log, gain_part):
    c = lax.axis_index("dp")
    heads = moment.shape[0]
    gain_rows = gain_part.reshape(heads, DH)
    message = pack_rows(moment, final_log, gain_rows)
    other = swap_dp(message)
    own_m, other_m = moment, other[:, :DH, :]
    own_fin, other_fin = final_log, other[:, DH, 0]
    first = jnp.where(c == 0, own_m, other_m)
    second = jnp.where(c == 0, other_m, own_m)
    fin_first = jnp.where(c == 0, own_fin, other_fin)
    fin_second = jnp.where(c == 0, other_fin, own_fin)
    chip_gain = gain_rows + other[:, DH + 1, :]
    chip_state = first + jnp.exp(fin_first)[:, None, None] * second
    chip_decay = fin_first + fin_second
    suffix_half, gathered = chip_prefix(
        pack_rows(halves(chip_state, c), halves(chip_decay, c), halves(chip_gain, c)), later=True
    )
    gain_half = jnp.sum(gathered[:, :, DH + 1, :], axis=0)
    back = swap_dp(pack_rows(suffix_half, gain_half))
    suffix = join_halves(suffix_half, back[:, :DH, :], c)
    gain_total = join_halves(gain_half, back[:, DH, :], c)
    core_zero = second + jnp.exp(fin_second)[:, None, None] * suffix
    return jnp.where(c == 0, core_zero, suffix), gain_total.reshape(heads * DH)


def _dot(a, b, contract):
    return lax.dot_general(a, b, (contract, ((), ())), preferred_element_type=jnp.float32)


def _nn(a, b):
    return _dot(a, b, ((1,), (0,)))


def _nt(a, b):
    return _dot(a, b, ((1,), (1,)))


def _tn(a, b):
    return _dot(a, b, ((0,), (0,)))


def _decay(cum_col, cum_row):
    length = cum_col.shape[0]
    t = lax.broadcasted_iota(jnp.int32, (length, length), 0)
    s = lax.broadcasted_iota(jnp.int32, (length, length), 1)
    causal = t >= s
    spread = cum_col - cum_row
    return jnp.where(causal, jnp.exp(jnp.where(causal, spread, 0.0)), 0.0)


def _masked(q, k, decay):
    return (_nt(q, k) * decay).astype(jnp.bfloat16)


def local_state_kernel(k_ref, v_ref, toend_ref, s_ref):
    scaled = (k_ref[...].astype(jnp.float32) * toend_ref[0]).astype(jnp.bfloat16)
    s_ref[0] = _tn(scaled, v_ref[...])


def intra_kernel(q_ref, k_ref, v_ref, col_ref, row_ref, out_ref):
    decay = _decay(col_ref[0], row_ref[0])
    out_ref[...] = _nn(_masked(q_ref[...], k_ref[...], decay), v_ref[...])


def norm_kernel(q_ref, g_ref, intra_ref, st_ref, grow_ref, gain_ref, og_ref, m_ref, gp_ref):
    grow = grow_ref[0]
    q = q_ref[...]
    attended = intra_ref[...] + grow * _nn(q, st_ref[0])
    width = attended.shape[-1]
    root_mean = jnp.sqrt(jnp.sum(attended * attended, axis=-1, keepdims=True) / width + epsilon)
    normed = attended / root_mean
    grad_f = g_ref[...].astype(jnp.float32)
    scaled = gain_ref[0] * grad_f
    projected = jnp.sum(scaled * attended, axis=-1, keepdims=True)
    out_grad = ((scaled - attended * projected / (width * root_mean * root_mean)) / root_mean).astype(
        jnp.bfloat16
    )
    og_ref[...] = out_grad
    gp_ref[0] = jnp.sum(grad_f * normed, axis=0, keepdims=True)
    q_scaled = (q.astype(jnp.float32) * grow).astype(jnp.bfloat16)
    m_ref[0] = _tn(q_scaled, out_grad)


def grads_kernel(q_ref, k_ref, v_ref, og_ref, col_ref, row_ref, grow_ref, st_ref, qg_ref, kg_ref, vg_ref):
    decay = _decay(col_ref[0], row_ref[0])
    q, k, v, og = q_ref[...], k_ref[...], v_ref[...], og_ref[...]
    masked = _masked(q, k, decay)
    rgrad = (_nt(og, v) * decay).astype(jnp.bfloat16)
    qg_ref[...] = (_nn(rgrad, k) + grow_ref[0] * _nt(og, st_ref[0])).astype(jnp.bfloat16)
    kg_ref[...] = _tn(rgrad, q)
    vg_ref[...] = _tn(masked, og)


def finish_kernel(k_ref, v_ref, kg_ref, vg_ref, gl_ref, toend_ref, ko_ref, vo_ref):
    toend = toend_ref[0]
    grad_low = gl_ref[0]
    ko_ref[...] = (kg_ref[...] + toend * _nt(v_ref[...], grad_low)).astype(jnp.bfloat16)
    vo_ref[...] = (vg_ref[...] + toend * _nn(k_ref[...], grad_low)).astype(jnp.bfloat16)


def _per_head(kernel, ins, outs, heads, length, flops, nbytes, exps=0):
    def spec(kind):
        if kind == "rows":
            return pl.BlockSpec((length, DH), lambda h: (0, h))
        if kind == "col":
            return pl.BlockSpec((1, length, 1), lambda h: (h, 0, 0))
        if kind == "row":
            return pl.BlockSpec((1, 1, length), lambda h: (h, 0, 0))
        if kind == "gain":
            return pl.BlockSpec((1, 1, DH), lambda h: (h, 0, 0))
        return pl.BlockSpec((1, DH, DH), lambda h: (h, 0, 0))

    shapes = {
        "rows": (length, heads * DH),
        "gain": (heads, 1, DH),
        "square": (heads, DH, DH),
    }
    out_shape = [jax.ShapeDtypeStruct(shapes[kind], dtype) for kind, dtype in outs]
    return pl.pallas_call(
        kernel,
        grid=(heads,),
        in_specs=[spec(kind) for kind, _ in ins],
        out_specs=[spec(kind) for kind, _ in outs],
        out_shape=out_shape,
        cost_estimate=pl.CostEstimate(flops=flops, transcendentals=exps, bytes_accessed=nbytes),
    )(*[x for _, x in ins])


def on_device(query_rows, key_rows, value_rows, cotangent, log_decay, norm_gain):
    length = query_rows.shape[0]
    heads = log_decay.shape[1]
    f32 = jnp.float32
    bf16 = jnp.bfloat16
    cumulated = jnp.cumsum(log_decay, axis=0)
    final_log = cumulated[-1]
    by_head = cumulated.T
    cum_col = by_head[:, :, None]
    cum_row = by_head[:, None, :]
    grow_col = jnp.exp(cum_col)
    toend_col = jnp.exp(final_log[:, None, None] - cum_col)
    gain_rows = norm_gain.reshape(heads, 1, DH)
    q, k, v, g = query_rows, key_rows, value_rows, cotangent
    big = length * length * DH * 2 * heads
    small = length * DH * DH * 2 * heads
    rows_bytes = length * heads * DH * 2
    (local_state,) = _per_head(
        local_state_kernel,
        [("rows", k), ("rows", v), ("col", toend_col)],
        [("square", f32)],
        heads, length, small, 2 * rows_bytes,
    )
    state_in = forward_states(local_state, final_log)
    (intra,) = _per_head(
        intra_kernel,
        [("rows", q), ("rows", k), ("rows", v), ("col", cum_col), ("row", cum_row)],
        [("rows", f32)],
        heads, length, 2 * big, 5 * rows_bytes, heads * length * length,
    )
    state_low = state_in.astype(bf16)
    out_grad, moment, gain_part = _per_head(
        norm_kernel,
        [("rows", q), ("rows", g), ("rows", intra), ("square", state_low), ("col", grow_col), ("gain", gain_rows)],
        [("rows", bf16), ("square", f32), ("gain", f32)],
        heads, length, 2 * small, 5 * rows_bytes,
    )
    grad_state, gain_sum = backward_states(moment, final_log, gain_part.reshape(heads * DH))
    query_grad, key_part, value_part = _per_head(
        grads_kernel,
        [("rows", q), ("rows", k), ("rows", v), ("rows", out_grad), ("col", cum_col), ("row", cum_row),
         ("col", grow_col), ("square", state_low)],
        [("rows", bf16), ("rows", f32), ("rows", f32)],
        heads, length, 5 * big + small, 9 * rows_bytes, heads * length * length,
    )
    grad_low = grad_state.astype(bf16)
    key_grad, value_grad = _per_head(
        finish_kernel,
        [("rows", k), ("rows", v), ("rows", key_part), ("rows", value_part), ("square", grad_low),
         ("col", toend_col)],
        [("rows", bf16), ("rows", bf16)],
        heads, length, 2 * small, 8 * rows_bytes,
    )
    seq_total = length * lax.axis_size(("ctx", "dp"))
    gain_grad = gain_sum * (1.0 / math.sqrt(seq_total))
    return (query_grad, key_grad, value_grad, gain_grad)


def solution(mesh):
    return jax.shard_map(
        on_device,
        mesh=mesh,
        in_specs=(
            P(("groups", "ctx", "dp"), "head"),
            P(("groups", "ctx", "dp"), "head"),
            P(("groups", "ctx", "dp"), "head"),
            P(("groups", "ctx", "dp"), "head"),
            P(("groups", "ctx", "dp"), "head"),
            P("head"),
        ),
        out_specs=(
            P(("groups", "ctx", "dp"), "head"),
            P(("groups", "ctx", "dp"), "head"),
            P(("groups", "ctx", "dp"), "head"),
            P(("groups", "head")),
        ),
        check_vma=False,
    )
```

```python
import math

import jax
import jax.numpy as jnp
from jax import lax
from jax.experimental import pallas as pl
from jax.sharding import PartitionSpec as P

DH = 128
PAD = 8
CHUNKS = 4


epsilon = 1e-06


def swap_dp(x):
    return lax.ppermute(x, "dp", perm=[(0, 1), (1, 0)])


def pack_rows(core, *rows):
    heads = core.shape[0]
    pad = [jnp.broadcast_to(r.reshape(heads, 1, -1), (heads, 1, DH)) for r in rows]
    fill = jnp.zeros((heads, PAD - len(rows), DH), jnp.float32)
    return jnp.concatenate([core] + pad + [fill], axis=1)


def halves(x, c):
    half = x.shape[0] // 2
    return lax.dynamic_slice_in_dim(x, c * half, half, axis=0)


def join_halves(mine, other, c):
    first = jnp.where(c == 0, mine, other)
    second = jnp.where(c == 0, other, mine)
    return jnp.concatenate([first, second], axis=0)


def chain_scan(chip_state, chip_decay, later):
    chips = lax.axis_size("ctx")
    z = lax.axis_index("ctx")
    heads = chip_state.shape[0]
    count = min(CHUNKS, heads)
    size = heads // count
    pieces = chip_state.reshape(count, size, DH, DH)
    factor = jnp.exp(chip_decay).reshape(count, size, 1, 1)
    rank = (chips - 1 - z) if later else z
    if later:
        perm = [(i, i - 1) for i in range(1, chips)]
    else:
        perm = [(i, i + 1) for i in range(chips - 1)]
    prefix = jnp.zeros_like(pieces)
    for step in range(count + chips - 2):
        send = jnp.clip(step - rank, 0, count - 1)
        outgoing = factor[send] * prefix[send] + pieces[send]
        arrived = lax.ppermute(outgoing, "ctx", perm=perm)
        where_to = step - rank + 1
        valid = (where_to >= 0) & (where_to < count) & (rank >= 1)
        slot = jnp.clip(where_to, 0, count - 1)
        prefix = prefix.at[slot].set(jnp.where(valid, arrived, prefix[slot]))
    return prefix.reshape(heads, DH, DH)


def forward_states(local_state, final_log):
    c = lax.axis_index("dp")
    message = pack_rows(local_state, final_log)
    other = swap_dp(message)
    own_state, other_state = local_state, other[:, :DH, :]
    own_fin, other_fin = final_log, other[:, DH, 0]
    first = jnp.where(c == 0, own_state, other_state)
    second = jnp.where(c == 0, other_state, own_state)
    fin_first = jnp.where(c == 0, own_fin, other_fin)
    fin_second = jnp.where(c == 0, other_fin, own_fin)
    chip_state = jnp.exp(fin_second)[:, None, None] * first + second
    chip_decay = fin_first + fin_second
    prefix_half = chain_scan(halves(chip_state, c), halves(chip_decay, c), later=False)
    prefix = join_halves(prefix_half, swap_dp(prefix_half), c)
    core_one = jnp.exp(fin_first)[:, None, None] * prefix + first
    return jnp.where(c == 0, prefix, core_one)


def backward_states(moment, final_log, gain_part):
    c = lax.axis_index("dp")
    heads = moment.shape[0]
    gain_rows = gain_part.reshape(heads, DH)
    message = pack_rows(moment, final_log, gain_rows)
    other = swap_dp(message)
    own_m, other_m = moment, other[:, :DH, :]
    own_fin, other_fin = final_log, other[:, DH, 0]
    first = jnp.where(c == 0, own_m, other_m)
    second = jnp.where(c == 0, other_m, own_m)
    fin_first = jnp.where(c == 0, own_fin, other_fin)
    fin_second = jnp.where(c == 0, other_fin, own_fin)
    chip_gain = gain_rows + other[:, DH + 1, :]
    chip_state = first + jnp.exp(fin_first)[:, None, None] * second
    chip_decay = fin_first + fin_second
    gain_half = jnp.sum(lax.all_gather(halves(chip_gain, c), "ctx"), axis=0)
    suffix_half = chain_scan(halves(chip_state, c), halves(chip_decay, c), later=True)
    back = swap_dp(pack_rows(suffix_half, gain_half))
    suffix = join_halves(suffix_half, back[:, :DH, :], c)
    gain_total = join_halves(gain_half, back[:, DH, :], c)
    core_zero = second + jnp.exp(fin_second)[:, None, None] * suffix
    return jnp.where(c == 0, core_zero, suffix), gain_total.reshape(heads * DH)


def _dot(a, b, contract):
    return lax.dot_general(a, b, (contract, ((), ())), preferred_element_type=jnp.float32)


def _nn(a, b):
    return _dot(a, b, ((1,), (0,)))


def _nt(a, b):
    return _dot(a, b, ((1,), (1,)))


def _tn(a, b):
    return _dot(a, b, ((0,), (0,)))


def _decay(cum_col, cum_row):
    length = cum_col.shape[0]
    t = lax.broadcasted_iota(jnp.int32, (length, length), 0)
    s = lax.broadcasted_iota(jnp.int32, (length, length), 1)
    causal = t >= s
    spread = cum_col - cum_row
    return jnp.where(causal, jnp.exp(jnp.where(causal, spread, 0.0)), 0.0)


def _masked(q, k, decay):
    return (_nt(q, k) * decay).astype(jnp.bfloat16)


def local_state_kernel(k_ref, v_ref, toend_ref, s_ref):
    scaled = (k_ref[...].astype(jnp.float32) * toend_ref[0]).astype(jnp.bfloat16)
    s_ref[0] = _tn(scaled, v_ref[...])


def intra_kernel(q_ref, k_ref, v_ref, col_ref, row_ref, out_ref):
    decay = _decay(col_ref[0], row_ref[0])
    out_ref[...] = _nn(_masked(q_ref[...], k_ref[...], decay), v_ref[...])


def norm_kernel(q_ref, g_ref, intra_ref, st_ref, grow_ref, gain_ref, og_ref, m_ref, gp_ref):
    grow = grow_ref[0]
    q = q_ref[...]
    attended = intra_ref[...] + grow * _nn(q, st_ref[0])
    width = attended.shape[-1]
    root_mean = jnp.sqrt(jnp.sum(attended * attended, axis=-1, keepdims=True) / width + epsilon)
    normed = attended / root_mean
    grad_f = g_ref[...].astype(jnp.float32)
    scaled = gain_ref[0] * grad_f
    projected = jnp.sum(scaled * attended, axis=-1, keepdims=True)
    out_grad = ((scaled - attended * projected / (width * root_mean * root_mean)) / root_mean).astype(
        jnp.bfloat16
    )
    og_ref[...] = out_grad
    gp_ref[0] = jnp.sum(grad_f * normed, axis=0, keepdims=True)
    q_scaled = (q.astype(jnp.float32) * grow).astype(jnp.bfloat16)
    m_ref[0] = _tn(q_scaled, out_grad)


def grads_kernel(q_ref, k_ref, v_ref, og_ref, col_ref, row_ref, grow_ref, st_ref, qg_ref, kg_ref, vg_ref):
    decay = _decay(col_ref[0], row_ref[0])
    q, k, v, og = q_ref[...], k_ref[...], v_ref[...], og_ref[...]
    masked = _masked(q, k, decay)
    rgrad = (_nt(og, v) * decay).astype(jnp.bfloat16)
    qg_ref[...] = (_nn(rgrad, k) + grow_ref[0] * _nt(og, st_ref[0])).astype(jnp.bfloat16)
    kg_ref[...] = _tn(rgrad, q)
    vg_ref[...] = _tn(masked, og)


def finish_kernel(k_ref, v_ref, kg_ref, vg_ref, gl_ref, toend_ref, ko_ref, vo_ref):
    toend = toend_ref[0]
    grad_low = gl_ref[0]
    ko_ref[...] = (kg_ref[...] + toend * _nt(v_ref[...], grad_low)).astype(jnp.bfloat16)
    vo_ref[...] = (vg_ref[...] + toend * _nn(k_ref[...], grad_low)).astype(jnp.bfloat16)


def _per_head(kernel, ins, outs, heads, length, flops, nbytes, exps=0):
    def spec(kind):
        if kind == "rows":
            return pl.BlockSpec((length, DH), lambda h: (0, h))
        if kind == "col":
            return pl.BlockSpec((1, length, 1), lambda h: (h, 0, 0))
        if kind == "row":
            return pl.BlockSpec((1, 1, length), lambda h: (h, 0, 0))
        if kind == "gain":
            return pl.BlockSpec((1, 1, DH), lambda h: (h, 0, 0))
        return pl.BlockSpec((1, DH, DH), lambda h: (h, 0, 0))

    shapes = {
        "rows": (length, heads * DH),
        "gain": (heads, 1, DH),
        "square": (heads, DH, DH),
    }
    out_shape = [jax.ShapeDtypeStruct(shapes[kind], dtype) for kind, dtype in outs]
    return pl.pallas_call(
        kernel,
        grid=(heads,),
        in_specs=[spec(kind) for kind, _ in ins],
        out_specs=[spec(kind) for kind, _ in outs],
        out_shape=out_shape,
        cost_estimate=pl.CostEstimate(flops=flops, transcendentals=exps, bytes_accessed=nbytes),
    )(*[x for _, x in ins])


def on_device(query_rows, key_rows, value_rows, cotangent, log_decay, norm_gain):
    length = query_rows.shape[0]
    heads = log_decay.shape[1]
    f32 = jnp.float32
    bf16 = jnp.bfloat16
    cumulated = jnp.cumsum(log_decay, axis=0)
    final_log = cumulated[-1]
    by_head = cumulated.T
    cum_col = by_head[:, :, None]
    cum_row = by_head[:, None, :]
    grow_col = jnp.exp(cum_col)
    toend_col = jnp.exp(final_log[:, None, None] - cum_col)
    gain_rows = norm_gain.reshape(heads, 1, DH)
    q, k, v, g = query_rows, key_rows, value_rows, cotangent
    big = length * length * DH * 2 * heads
    small = length * DH * DH * 2 * heads
    rows_bytes = length * heads * DH * 2
    (local_state,) = _per_head(
        local_state_kernel,
        [("rows", k), ("rows", v), ("col", toend_col)],
        [("square", f32)],
        heads, length, small, 2 * rows_bytes,
    )
    state_in = forward_states(local_state, final_log)
    (intra,) = _per_head(
        intra_kernel,
        [("rows", q), ("rows", k), ("rows", v), ("col", cum_col), ("row", cum_row)],
        [("rows", f32)],
        heads, length, 2 * big, 5 * rows_bytes, heads * length * length,
    )
    state_low = state_in.astype(bf16)
    out_grad, moment, gain_part = _per_head(
        norm_kernel,
        [("rows", q), ("rows", g), ("rows", intra), ("square", state_low), ("col", grow_col), ("gain", gain_rows)],
        [("rows", bf16), ("square", f32), ("gain", f32)],
        heads, length, 2 * small, 5 * rows_bytes,
    )
    grad_state, gain_sum = backward_states(moment, final_log, gain_part.reshape(heads * DH))
    query_grad, key_part, value_part = _per_head(
        grads_kernel,
        [("rows", q), ("rows", k), ("rows", v), ("rows", out_grad), ("col", cum_col), ("row", cum_row),
         ("col", grow_col), ("square", state_low)],
        [("rows", bf16), ("rows", f32), ("rows", f32)],
        heads, length, 5 * big + small, 9 * rows_bytes, heads * length * length,
    )
    grad_low = grad_state.astype(bf16)
    key_grad, value_grad = _per_head(
        finish_kernel,
        [("rows", k), ("rows", v), ("rows", key_part), ("rows", value_part), ("square", grad_low),
         ("col", toend_col)],
        [("rows", bf16), ("rows", bf16)],
        heads, length, 2 * small, 8 * rows_bytes,
    )
    seq_total = length * lax.axis_size(("ctx", "dp"))
    gain_grad = gain_sum * (1.0 / math.sqrt(seq_total))
    return (query_grad, key_grad, value_grad, gain_grad)


def solution(mesh):
    return jax.shard_map(
        on_device,
        mesh=mesh,
        in_specs=(
            P(("groups", "ctx", "dp"), "head"),
            P(("groups", "ctx", "dp"), "head"),
            P(("groups", "ctx", "dp"), "head"),
            P(("groups", "ctx", "dp"), "head"),
            P(("groups", "ctx", "dp"), "head"),
            P("head"),
        ),
        out_specs=(
            P(("groups", "ctx", "dp"), "head"),
            P(("groups", "ctx", "dp"), "head"),
            P(("groups", "ctx", "dp"), "head"),
            P(("groups", "head")),
        ),
        check_vma=False,
    )
```

```python
import math

import jax
import jax.numpy as jnp
from jax import lax
from jax.experimental import pallas as pl
from jax.sharding import PartitionSpec as P

DH = 128
PAD = 8
CHUNKS = 4


epsilon = 1e-06


def swap_dp(x):
    return lax.ppermute(x, "dp", perm=[(0, 1), (1, 0)])


def pack_rows(core, *rows):
    heads = core.shape[0]
    pad = [jnp.broadcast_to(r.reshape(heads, 1, -1), (heads, 1, DH)) for r in rows]
    fill = jnp.zeros((heads, PAD - len(rows), DH), jnp.float32)
    return jnp.concatenate([core] + pad + [fill], axis=1)


def halves(x, c):
    half = x.shape[0] // 2
    return lax.dynamic_slice_in_dim(x, c * half, half, axis=0)


def join_halves(mine, other, c):
    first = jnp.where(c == 0, mine, other)
    second = jnp.where(c == 0, other, mine)
    return jnp.concatenate([first, second], axis=0)


def chain_scan(chip_state, chip_decay, later):
    chips = lax.axis_size("ctx")
    z = lax.axis_index("ctx")
    heads = chip_state.shape[0]
    count = min(CHUNKS, heads)
    size = heads // count
    pieces = chip_state.reshape(count, size, DH, DH)
    factor = jnp.exp(chip_decay).reshape(count, size, 1, 1)
    rank = (chips - 1 - z) if later else z
    if later:
        perm = [(i, i - 1) for i in range(1, chips)]
    else:
        perm = [(i, i + 1) for i in range(chips - 1)]
    prefix = jnp.zeros_like(pieces)
    for step in range(count + chips - 2):
        send = jnp.clip(step - rank, 0, count - 1)
        outgoing = factor[send] * prefix[send] + pieces[send]
        arrived = lax.ppermute(outgoing, "ctx", perm=perm)
        where_to = step - rank + 1
        valid = (where_to >= 0) & (where_to < count) & (rank >= 1)
        slot = jnp.clip(where_to, 0, count - 1)
        prefix = prefix.at[slot].set(jnp.where(valid, arrived, prefix[slot]))
    return prefix.reshape(heads, DH, DH)


def forward_states(local_state, final_log):
    c = lax.axis_index("dp")
    message = pack_rows(local_state, final_log)
    other = swap_dp(message)
    own_state, other_state = local_state, other[:, :DH, :]
    own_fin, other_fin = final_log, other[:, DH, 0]
    first = jnp.where(c == 0, own_state, other_state)
    second = jnp.where(c == 0, other_state, own_state)
    fin_first = jnp.where(c == 0, own_fin, other_fin)
    fin_second = jnp.where(c == 0, other_fin, own_fin)
    chip_state = jnp.exp(fin_second)[:, None, None] * first + second
    chip_decay = fin_first + fin_second
    prefix_half = chain_scan(halves(chip_state, c), halves(chip_decay, c), later=False)
    prefix = join_halves(prefix_half, swap_dp(prefix_half), c)
    core_one = jnp.exp(fin_first)[:, None, None] * prefix + first
    return jnp.where(c == 0, prefix, core_one)


def backward_states(moment, final_log, gain_part):
    c = lax.axis_index("dp")
    heads = moment.shape[0]
    gain_rows = gain_part.reshape(heads, DH)
    message = pack_rows(moment, final_log, gain_rows)
    other = swap_dp(message)
    own_m, other_m = moment, other[:, :DH, :]
    own_fin, other_fin = final_log, other[:, DH, 0]
    first = jnp.where(c == 0, own_m, other_m)
    second = jnp.where(c == 0, other_m, own_m)
    fin_first = jnp.where(c == 0, own_fin, other_fin)
    fin_second = jnp.where(c == 0, other_fin, own_fin)
    chip_gain = gain_rows + other[:, DH + 1, :]
    chip_state = first + jnp.exp(fin_first)[:, None, None] * second
    chip_decay = fin_first + fin_second
    chips = lax.axis_size("ctx")
    gain_total = chip_gain
    distance = 1
    while distance < chips:
        partners = [(i, i ^ distance) for i in range(chips)]
        gain_total = gain_total + lax.ppermute(gain_total, "ctx", perm=partners)
        distance *= 2
    suffix_half = chain_scan(halves(chip_state, c), halves(chip_decay, c), later=True)
    suffix = join_halves(suffix_half, swap_dp(suffix_half), c)
    core_zero = second + jnp.exp(fin_second)[:, None, None] * suffix
    return jnp.where(c == 0, core_zero, suffix), gain_total.reshape(heads * DH)


def _dot(a, b, contract):
    return lax.dot_general(a, b, (contract, ((), ())), preferred_element_type=jnp.float32)


def _nn(a, b):
    return _dot(a, b, ((1,), (0,)))


def _nt(a, b):
    return _dot(a, b, ((1,), (1,)))


def _tn(a, b):
    return _dot(a, b, ((0,), (0,)))


def _decay(cum_col, cum_row):
    length = cum_col.shape[0]
    t = lax.broadcasted_iota(jnp.int32, (length, length), 0)
    s = lax.broadcasted_iota(jnp.int32, (length, length), 1)
    causal = t >= s
    spread = cum_col - cum_row
    return jnp.where(causal, jnp.exp(jnp.where(causal, spread, 0.0)), 0.0)


def _masked(q, k, decay):
    return (_nt(q, k) * decay).astype(jnp.bfloat16)


def _head_vectors(cum_ref, cumt_ref):
    h = pl.program_id(0)
    full = cum_ref[...]
    lane = lax.broadcasted_iota(jnp.int32, full.shape, 1)
    col = jnp.sum(jnp.where(lane == h, full, 0.0), axis=1, keepdims=True)
    row = cumt_ref[pl.ds(h, 1), :]
    fin = col[col.shape[0] - 1 :, :]
    return col, row, jnp.exp(col), jnp.exp(fin - col)


def local_state_kernel(k_ref, v_ref, cum_ref, cumt_ref, s_ref):
    _, _, _, toend = _head_vectors(cum_ref, cumt_ref)
    scaled = (k_ref[...].astype(jnp.float32) * toend).astype(jnp.bfloat16)
    s_ref[0] = _tn(scaled, v_ref[...])


def intra_kernel(q_ref, k_ref, v_ref, cum_ref, cumt_ref, out_ref):
    col, row, _, _ = _head_vectors(cum_ref, cumt_ref)
    decay = _decay(col, row)
    out_ref[...] = _nn(_masked(q_ref[...], k_ref[...], decay), v_ref[...])


def norm_kernel(q_ref, g_ref, intra_ref, st_ref, cum_ref, cumt_ref, gain_ref, og_ref, m_ref, gp_ref):
    _, _, grow, _ = _head_vectors(cum_ref, cumt_ref)
    q = q_ref[...]
    attended = intra_ref[...] + grow * _nn(q, st_ref[0])
    width = attended.shape[-1]
    root_mean = jnp.sqrt(jnp.sum(attended * attended, axis=-1, keepdims=True) / width + epsilon)
    normed = attended / root_mean
    grad_f = g_ref[...].astype(jnp.float32)
    scaled = gain_ref[0] * grad_f
    projected = jnp.sum(scaled * attended, axis=-1, keepdims=True)
    out_grad = ((scaled - attended * projected / (width * root_mean * root_mean)) / root_mean).astype(
        jnp.bfloat16
    )
    og_ref[...] = out_grad
    gp_ref[0] = jnp.sum(grad_f * normed, axis=0, keepdims=True)
    q_scaled = (q.astype(jnp.float32) * grow).astype(jnp.bfloat16)
    m_ref[0] = _tn(q_scaled, out_grad)


def grads_kernel(q_ref, k_ref, v_ref, og_ref, cum_ref, cumt_ref, st_ref, qg_ref, kg_ref, vg_ref):
    col, row, grow, _ = _head_vectors(cum_ref, cumt_ref)
    decay = _decay(col, row)
    q, k, v, og = q_ref[...], k_ref[...], v_ref[...], og_ref[...]
    masked = _masked(q, k, decay)
    rgrad = (_nt(og, v) * decay).astype(jnp.bfloat16)
    qg_ref[...] = (_nn(rgrad, k) + grow * _nt(og, st_ref[0])).astype(jnp.bfloat16)
    kg_ref[...] = _tn(rgrad, q)
    vg_ref[...] = _tn(masked, og)


def finish_kernel(k_ref, v_ref, kg_ref, vg_ref, gl_ref, cum_ref, cumt_ref, ko_ref, vo_ref):
    _, _, _, toend = _head_vectors(cum_ref, cumt_ref)
    grad_low = gl_ref[0]
    ko_ref[...] = (kg_ref[...] + toend * _nt(v_ref[...], grad_low)).astype(jnp.bfloat16)
    vo_ref[...] = (vg_ref[...] + toend * _nn(k_ref[...], grad_low)).astype(jnp.bfloat16)


def _per_head(kernel, ins, outs, heads, length, flops, nbytes, exps=0):
    def spec(kind):
        if kind == "rows":
            return pl.BlockSpec((length, DH), lambda h: (0, h))
        if kind == "cum":
            return pl.BlockSpec((length, heads), lambda h: (0, 0))
        if kind == "cumt":
            return pl.BlockSpec((heads, length), lambda h: (0, 0))
        if kind == "gain":
            return pl.BlockSpec((1, 1, DH), lambda h: (h, 0, 0))
        return pl.BlockSpec((1, DH, DH), lambda h: (h, 0, 0))

    shapes = {
        "rows": (length, heads * DH),
        "gain": (heads, 1, DH),
        "square": (heads, DH, DH),
    }
    out_shape = [jax.ShapeDtypeStruct(shapes[kind], dtype) for kind, dtype in outs]
    return pl.pallas_call(
        kernel,
        grid=(heads,),
        in_specs=[spec(kind) for kind, _ in ins],
        out_specs=[spec(kind) for kind, _ in outs],
        out_shape=out_shape,
        cost_estimate=pl.CostEstimate(flops=flops, transcendentals=exps, bytes_accessed=nbytes),
    )(*[x for _, x in ins])


def on_device(query_rows, key_rows, value_rows, cotangent, log_decay, norm_gain):
    length = query_rows.shape[0]
    heads = log_decay.shape[1]
    f32 = jnp.float32
    bf16 = jnp.bfloat16
    t = lax.broadcasted_iota(jnp.int32, (length, length), 0)
    s = lax.broadcasted_iota(jnp.int32, (length, length), 1)
    lower = (t >= s).astype(f32)
    exact = lax.Precision.HIGHEST
    cum = jnp.dot(lower, log_decay, precision=exact)
    cum_t = lax.dot_general(log_decay, lower, (((0,), (1,)), ((), ())), precision=exact)
    final_log = cum[-1]
    gain_rows = norm_gain.reshape(heads, 1, DH)
    q, k, v, g = query_rows, key_rows, value_rows, cotangent
    big = length * length * DH * 2 * heads
    small = length * DH * DH * 2 * heads
    rows_bytes = length * heads * DH * 2
    (local_state,) = _per_head(
        local_state_kernel,
        [("rows", k), ("rows", v), ("cum", cum), ("cumt", cum_t)],
        [("square", f32)],
        heads, length, small, 2 * rows_bytes,
    )
    state_in = forward_states(local_state, final_log)
    (intra,) = _per_head(
        intra_kernel,
        [("rows", q), ("rows", k), ("rows", v), ("cum", cum), ("cumt", cum_t)],
        [("rows", f32)],
        heads, length, 2 * big, 5 * rows_bytes, heads * length * length,
    )
    state_low = state_in.astype(bf16)
    out_grad, moment, gain_part = _per_head(
        norm_kernel,
        [("rows", q), ("rows", g), ("rows", intra), ("square", state_low), ("cum", cum), ("cumt", cum_t), ("gain", gain_rows)],
        [("rows", bf16), ("square", f32), ("gain", f32)],
        heads, length, 2 * small, 5 * rows_bytes,
    )
    grad_state, gain_sum = backward_states(moment, final_log, gain_part.reshape(heads * DH))
    query_grad, key_part, value_part = _per_head(
        grads_kernel,
        [("rows", q), ("rows", k), ("rows", v), ("rows", out_grad), ("cum", cum), ("cumt", cum_t),
         ("square", state_low)],
        [("rows", bf16), ("rows", f32), ("rows", f32)],
        heads, length, 5 * big + small, 9 * rows_bytes, heads * length * length,
    )
    grad_low = grad_state.astype(bf16)
    key_grad, value_grad = _per_head(
        finish_kernel,
        [("rows", k), ("rows", v), ("rows", key_part), ("rows", value_part), ("square", grad_low),
         ("cum", cum), ("cumt", cum_t)],
        [("rows", bf16), ("rows", bf16)],
        heads, length, 2 * small, 8 * rows_bytes,
    )
    seq_total = length * lax.axis_size(("ctx", "dp"))
    gain_grad = gain_sum * (1.0 / math.sqrt(seq_total))
    return (query_grad, key_grad, value_grad, gain_grad)


def solution(mesh):
    return jax.shard_map(
        on_device,
        mesh=mesh,
        in_specs=(
            P(("groups", "ctx", "dp"), "head"),
            P(("groups", "ctx", "dp"), "head"),
            P(("groups", "ctx", "dp"), "head"),
            P(("groups", "ctx", "dp"), "head"),
            P(("groups", "ctx", "dp"), "head"),
            P("head"),
        ),
        out_specs=(
            P(("groups", "ctx", "dp"), "head"),
            P(("groups", "ctx", "dp"), "head"),
            P(("groups", "ctx", "dp"), "head"),
            P(("groups", "head")),
        ),
        check_vma=False,
    )
```

```python
import math

import jax
import jax.numpy as jnp
from jax import lax
from jax.experimental import pallas as pl
from jax.sharding import PartitionSpec as P

DH = 128
PAD = 8
CHUNKS = 4
TIE_STEP = 1


epsilon = 1e-06


def swap_dp(x):
    return lax.ppermute(x, "dp", perm=[(0, 1), (1, 0)])


def pack_rows(core, *rows):
    heads = core.shape[0]
    pad = [jnp.broadcast_to(r.reshape(heads, 1, -1), (heads, 1, DH)) for r in rows]
    fill = jnp.zeros((heads, PAD - len(rows), DH), jnp.float32)
    return jnp.concatenate([core] + pad + [fill], axis=1)


def halves(x, c):
    half = x.shape[0] // 2
    return lax.dynamic_slice_in_dim(x, c * half, half, axis=0)


def join_halves(mine, other, c):
    first = jnp.where(c == 0, mine, other)
    second = jnp.where(c == 0, other, mine)
    return jnp.concatenate([first, second], axis=0)


def chain_scan(chip_state, chip_decay, later, cover):
    chips = lax.axis_size("ctx")
    z = lax.axis_index("ctx")
    heads = chip_state.shape[0]
    count = min(CHUNKS, heads)
    size = heads // count
    pieces = chip_state.reshape(count, size, DH, DH)
    factor = jnp.exp(chip_decay).reshape(count, size, 1, 1)
    rank = (chips - 1 - z) if later else z
    if later:
        perm = [(i, i - 1) for i in range(1, chips)]
    else:
        perm = [(i, i + 1) for i in range(chips - 1)]
    prefix = jnp.zeros_like(pieces)
    for step in range(count + chips - 2):
        send = jnp.clip(step - rank, 0, count - 1)
        outgoing = factor[send] * prefix[send] + pieces[send]
        arrived = lax.ppermute(outgoing, "ctx", perm=perm)
        where_to = step - rank + 1
        valid = (where_to >= 0) & (where_to < count) & (rank >= 1)
        slot = jnp.clip(where_to, 0, count - 1)
        prefix = prefix.at[slot].set(jnp.where(valid, arrived, prefix[slot]))
        if step == TIE_STEP:
            cover, prefix = lax.optimization_barrier((cover, prefix))
    return prefix.reshape(heads, DH, DH), cover


def forward_states(local_state, final_log, cover):
    c = lax.axis_index("dp")
    message = pack_rows(local_state, final_log)
    other = swap_dp(message)
    own_state, other_state = local_state, other[:, :DH, :]
    own_fin, other_fin = final_log, other[:, DH, 0]
    first = jnp.where(c == 0, own_state, other_state)
    second = jnp.where(c == 0, other_state, own_state)
    fin_first = jnp.where(c == 0, own_fin, other_fin)
    fin_second = jnp.where(c == 0, other_fin, own_fin)
    chip_state = jnp.exp(fin_second)[:, None, None] * first + second
    chip_decay = fin_first + fin_second
    prefix_half, cover = chain_scan(halves(chip_state, c), halves(chip_decay, c), False, cover)
    prefix = join_halves(prefix_half, swap_dp(prefix_half), c)
    core_one = jnp.exp(fin_first)[:, None, None] * prefix + first
    return jnp.where(c == 0, prefix, core_one), cover


def backward_states(moment, final_log, gain_part, cover):
    c = lax.axis_index("dp")
    heads = moment.shape[0]
    gain_rows = gain_part.reshape(heads, DH)
    message = pack_rows(moment, final_log, gain_rows)
    other = swap_dp(message)
    own_m, other_m = moment, other[:, :DH, :]
    own_fin, other_fin = final_log, other[:, DH, 0]
    first = jnp.where(c == 0, own_m, other_m)
    second = jnp.where(c == 0, other_m, own_m)
    fin_first = jnp.where(c == 0, own_fin, other_fin)
    fin_second = jnp.where(c == 0, other_fin, own_fin)
    chip_gain = gain_rows + other[:, DH + 1, :]
    chip_state = first + jnp.exp(fin_first)[:, None, None] * second
    chip_decay = fin_first + fin_second
    chips = lax.axis_size("ctx")
    gain_total = chip_gain
    distance = 1
    while distance < chips:
        partners = [(i, i ^ distance) for i in range(chips)]
        gain_total = gain_total + lax.ppermute(gain_total, "ctx", perm=partners)
        distance *= 2
    suffix_half, cover = chain_scan(halves(chip_state, c), halves(chip_decay, c), True, cover)
    suffix = join_halves(suffix_half, swap_dp(suffix_half), c)
    core_zero = second + jnp.exp(fin_second)[:, None, None] * suffix
    return jnp.where(c == 0, core_zero, suffix), gain_total.reshape(heads * DH), cover


def _dot(a, b, contract):
    return lax.dot_general(a, b, (contract, ((), ())), preferred_element_type=jnp.float32)


def _nn(a, b):
    return _dot(a, b, ((1,), (0,)))


def _nt(a, b):
    return _dot(a, b, ((1,), (1,)))


def _tn(a, b):
    return _dot(a, b, ((0,), (0,)))


def _decay(cum_col, cum_row):
    length = cum_col.shape[0]
    t = lax.broadcasted_iota(jnp.int32, (length, length), 0)
    s = lax.broadcasted_iota(jnp.int32, (length, length), 1)
    causal = t >= s
    spread = cum_col - cum_row
    return jnp.where(causal, jnp.exp(jnp.where(causal, spread, 0.0)), 0.0)


def _masked(q, k, decay):
    return (_nt(q, k) * decay).astype(jnp.bfloat16)


def _head_vectors(cum_ref, cumt_ref):
    h = pl.program_id(0)
    full = cum_ref[...]
    lane = lax.broadcasted_iota(jnp.int32, full.shape, 1)
    col = jnp.sum(jnp.where(lane == h, full, 0.0), axis=1, keepdims=True)
    row = cumt_ref[pl.ds(h, 1), :]
    fin = col[col.shape[0] - 1 :, :]
    return col, row, jnp.exp(col), jnp.exp(fin - col)


def local_state_kernel(k_ref, v_ref, cum_ref, cumt_ref, s_ref):
    _, _, _, toend = _head_vectors(cum_ref, cumt_ref)
    scaled = (k_ref[...].astype(jnp.float32) * toend).astype(jnp.bfloat16)
    s_ref[0] = _tn(scaled, v_ref[...])


def intra_kernel(q_ref, k_ref, v_ref, cum_ref, cumt_ref, out_ref):
    col, row, _, _ = _head_vectors(cum_ref, cumt_ref)
    decay = _decay(col, row)
    out_ref[...] = _nn(_masked(q_ref[...], k_ref[...], decay), v_ref[...])


def norm_kernel(q_ref, g_ref, intra_ref, st_ref, cum_ref, cumt_ref, gain_ref, og_ref, m_ref, gp_ref):
    _, _, grow, _ = _head_vectors(cum_ref, cumt_ref)
    q = q_ref[...]
    attended = intra_ref[...] + grow * _nn(q, st_ref[0])
    width = attended.shape[-1]
    root_mean = jnp.sqrt(jnp.sum(attended * attended, axis=-1, keepdims=True) / width + epsilon)
    normed = attended / root_mean
    grad_f = g_ref[...].astype(jnp.float32)
    scaled = gain_ref[0] * grad_f
    projected = jnp.sum(scaled * attended, axis=-1, keepdims=True)
    out_grad = ((scaled - attended * projected / (width * root_mean * root_mean)) / root_mean).astype(
        jnp.bfloat16
    )
    og_ref[...] = out_grad
    gp_ref[0] = jnp.sum(grad_f * normed, axis=0, keepdims=True)
    q_scaled = (q.astype(jnp.float32) * grow).astype(jnp.bfloat16)
    m_ref[0] = _tn(q_scaled, out_grad)


def grads_kernel(q_ref, k_ref, v_ref, og_ref, cum_ref, cumt_ref, st_ref, qg_ref, kg_ref, vg_ref):
    col, row, grow, _ = _head_vectors(cum_ref, cumt_ref)
    decay = _decay(col, row)
    q, k, v, og = q_ref[...], k_ref[...], v_ref[...], og_ref[...]
    masked = _masked(q, k, decay)
    rgrad = (_nt(og, v) * decay).astype(jnp.bfloat16)
    qg_ref[...] = (_nn(rgrad, k) + grow * _nt(og, st_ref[0])).astype(jnp.bfloat16)
    kg_ref[...] = _tn(rgrad, q)
    vg_ref[...] = _tn(masked, og)


def finish_kernel(k_ref, v_ref, kg_ref, vg_ref, gl_ref, cum_ref, cumt_ref, ko_ref, vo_ref):
    _, _, _, toend = _head_vectors(cum_ref, cumt_ref)
    grad_low = gl_ref[0]
    ko_ref[...] = (kg_ref[...] + toend * _nt(v_ref[...], grad_low)).astype(jnp.bfloat16)
    vo_ref[...] = (vg_ref[...] + toend * _nn(k_ref[...], grad_low)).astype(jnp.bfloat16)


def _per_head(kernel, ins, outs, heads, length, flops, nbytes, exps=0):
    def spec(kind):
        if kind == "rows":
            return pl.BlockSpec((length, DH), lambda h: (0, h))
        if kind == "cum":
            return pl.BlockSpec((length, heads), lambda h: (0, 0))
        if kind == "cumt":
            return pl.BlockSpec((heads, length), lambda h: (0, 0))
        if kind == "gain":
            return pl.BlockSpec((1, 1, DH), lambda h: (h, 0, 0))
        return pl.BlockSpec((1, DH, DH), lambda h: (h, 0, 0))

    shapes = {
        "rows": (length, heads * DH),
        "gain": (heads, 1, DH),
        "square": (heads, DH, DH),
    }
    out_shape = [jax.ShapeDtypeStruct(shapes[kind], dtype) for kind, dtype in outs]
    return pl.pallas_call(
        kernel,
        grid=(heads,),
        in_specs=[spec(kind) for kind, _ in ins],
        out_specs=[spec(kind) for kind, _ in outs],
        out_shape=out_shape,
        cost_estimate=pl.CostEstimate(flops=flops, transcendentals=exps, bytes_accessed=nbytes),
    )(*[x for _, x in ins])


def on_device(query_rows, key_rows, value_rows, cotangent, log_decay, norm_gain):
    length = query_rows.shape[0]
    heads = log_decay.shape[1]
    f32 = jnp.float32
    bf16 = jnp.bfloat16
    t = lax.broadcasted_iota(jnp.int32, (length, length), 0)
    s = lax.broadcasted_iota(jnp.int32, (length, length), 1)
    lower = (t >= s).astype(f32)
    exact = lax.Precision.HIGHEST
    cum = jnp.dot(lower, log_decay, precision=exact)
    cum_t = lax.dot_general(log_decay, lower, (((0,), (1,)), ((), ())), precision=exact)
    final_log = cum[-1]
    gain_rows = norm_gain.reshape(heads, 1, DH)
    q, k, v, g = query_rows, key_rows, value_rows, cotangent
    big = length * length * DH * 2 * heads
    small = length * DH * DH * 2 * heads
    rows_bytes = length * heads * DH * 2
    (local_state,) = _per_head(
        local_state_kernel,
        [("rows", k), ("rows", v), ("cum", cum), ("cumt", cum_t)],
        [("square", f32)],
        heads, length, small, 2 * rows_bytes,
    )
    (intra,) = _per_head(
        intra_kernel,
        [("rows", q), ("rows", k), ("rows", v), ("cum", cum), ("cumt", cum_t)],
        [("rows", f32)],
        heads, length, 2 * big, 5 * rows_bytes, heads * length * length,
    )
    state_in, intra = forward_states(local_state, final_log, intra)
    state_low = state_in.astype(bf16)
    out_grad, moment, gain_part = _per_head(
        norm_kernel,
        [("rows", q), ("rows", g), ("rows", intra), ("square", state_low), ("cum", cum), ("cumt", cum_t), ("gain", gain_rows)],
        [("rows", bf16), ("square", f32), ("gain", f32)],
        heads, length, 2 * small, 5 * rows_bytes,
    )
    query_grad, key_part, value_part = _per_head(
        grads_kernel,
        [("rows", q), ("rows", k), ("rows", v), ("rows", out_grad), ("cum", cum), ("cumt", cum_t),
         ("square", state_low)],
        [("rows", bf16), ("rows", f32), ("rows", f32)],
        heads, length, 5 * big + small, 9 * rows_bytes, heads * length * length,
    )
    grad_state, gain_sum, (query_grad, key_part, value_part) = backward_states(
        moment, final_log, gain_part.reshape(heads * DH), (query_grad, key_part, value_part)
    )
    grad_low = grad_state.astype(bf16)
    key_grad, value_grad = _per_head(
        finish_kernel,
        [("rows", k), ("rows", v), ("rows", key_part), ("rows", value_part), ("square", grad_low),
         ("cum", cum), ("cumt", cum_t)],
        [("rows", bf16), ("rows", bf16)],
        heads, length, 2 * small, 8 * rows_bytes,
    )
    seq_total = length * lax.axis_size(("ctx", "dp"))
    gain_grad = gain_sum * (1.0 / math.sqrt(seq_total))
    return (query_grad, key_grad, value_grad, gain_grad)


def solution(mesh):
    return jax.shard_map(
        on_device,
        mesh=mesh,
        in_specs=(
            P(("groups", "ctx", "dp"), "head"),
            P(("groups", "ctx", "dp"), "head"),
            P(("groups", "ctx", "dp"), "head"),
            P(("groups", "ctx", "dp"), "head"),
            P(("groups", "ctx", "dp"), "head"),
            P("head"),
        ),
        out_specs=(
            P(("groups", "ctx", "dp"), "head"),
            P(("groups", "ctx", "dp"), "head"),
            P(("groups", "ctx", "dp"), "head"),
            P(("groups", "head")),
        ),
        check_vma=False,
    )
```

```python
import math

import jax
import jax.numpy as jnp
from jax import lax
from jax.experimental import pallas as pl
from jax.sharding import PartitionSpec as P

DH = 128
PAD = 8
CHUNKS = 4
TIE_STEP = 1
HB = 4


epsilon = 1e-06


def swap_dp(x):
    return lax.ppermute(x, "dp", perm=[(0, 1), (1, 0)])


def pack_rows(core, *rows):
    heads = core.shape[0]
    pad = [jnp.broadcast_to(r.reshape(heads, 1, -1), (heads, 1, DH)) for r in rows]
    fill = jnp.zeros((heads, PAD - len(rows), DH), jnp.float32)
    return jnp.concatenate([core] + pad + [fill], axis=1)


def halves(x, c):
    half = x.shape[0] // 2
    return lax.dynamic_slice_in_dim(x, c * half, half, axis=0)


def join_halves(mine, other, c):
    first = jnp.where(c == 0, mine, other)
    second = jnp.where(c == 0, other, mine)
    return jnp.concatenate([first, second], axis=0)


def chain_scan(chip_state, chip_decay, later, cover):
    chips = lax.axis_size("ctx")
    z = lax.axis_index("ctx")
    heads = chip_state.shape[0]
    count = min(CHUNKS, heads)
    size = heads // count
    pieces = chip_state.reshape(count, size, DH, DH)
    factor = jnp.exp(chip_decay).reshape(count, size, 1, 1)
    rank = (chips - 1 - z) if later else z
    if later:
        perm = [(i, i - 1) for i in range(1, chips)]
    else:
        perm = [(i, i + 1) for i in range(chips - 1)]
    prefix = jnp.zeros_like(pieces)
    for step in range(count + chips - 2):
        send = jnp.clip(step - rank, 0, count - 1)
        outgoing = factor[send] * prefix[send] + pieces[send]
        arrived = lax.ppermute(outgoing, "ctx", perm=perm)
        where_to = step - rank + 1
        valid = (where_to >= 0) & (where_to < count) & (rank >= 1)
        slot = jnp.clip(where_to, 0, count - 1)
        prefix = prefix.at[slot].set(jnp.where(valid, arrived, prefix[slot]))
        if step == TIE_STEP:
            cover, prefix = lax.optimization_barrier((cover, prefix))
    return prefix.reshape(heads, DH, DH), cover


def forward_states(local_state, final_log, cover):
    c = lax.axis_index("dp")
    message = pack_rows(local_state, final_log)
    other = swap_dp(message)
    own_state, other_state = local_state, other[:, :DH, :]
    own_fin, other_fin = final_log, other[:, DH, 0]
    first = jnp.where(c == 0, own_state, other_state)
    second = jnp.where(c == 0, other_state, own_state)
    fin_first = jnp.where(c == 0, own_fin, other_fin)
    fin_second = jnp.where(c == 0, other_fin, own_fin)
    chip_state = jnp.exp(fin_second)[:, None, None] * first + second
    chip_decay = fin_first + fin_second
    prefix_half, cover = chain_scan(halves(chip_state, c), halves(chip_decay, c), False, cover)
    prefix = join_halves(prefix_half, swap_dp(prefix_half), c)
    core_one = jnp.exp(fin_first)[:, None, None] * prefix + first
    return jnp.where(c == 0, prefix, core_one), cover


def backward_states(moment, final_log, gain_part, cover):
    c = lax.axis_index("dp")
    heads = moment.shape[0]
    gain_rows = gain_part.reshape(heads, DH)
    message = pack_rows(moment, final_log, gain_rows)
    other = swap_dp(message)
    own_m, other_m = moment, other[:, :DH, :]
    own_fin, other_fin = final_log, other[:, DH, 0]
    first = jnp.where(c == 0, own_m, other_m)
    second = jnp.where(c == 0, other_m, own_m)
    fin_first = jnp.where(c == 0, own_fin, other_fin)
    fin_second = jnp.where(c == 0, other_fin, own_fin)
    chip_gain = gain_rows + other[:, DH + 1, :]
    chip_state = first + jnp.exp(fin_first)[:, None, None] * second
    chip_decay = fin_first + fin_second
    chips = lax.axis_size("ctx")
    gain_total = chip_gain
    distance = 1
    while distance < chips:
        partners = [(i, i ^ distance) for i in range(chips)]
        gain_total = gain_total + lax.ppermute(gain_total, "ctx", perm=partners)
        distance *= 2
    suffix_half, cover = chain_scan(halves(chip_state, c), halves(chip_decay, c), True, cover)
    suffix = join_halves(suffix_half, swap_dp(suffix_half), c)
    core_zero = second + jnp.exp(fin_second)[:, None, None] * suffix
    return jnp.where(c == 0, core_zero, suffix), gain_total.reshape(heads * DH), cover


def _dot(a, b, contract):
    return lax.dot_general(a, b, (contract, ((), ())), preferred_element_type=jnp.float32)


def _nn(a, b):
    return _dot(a, b, ((1,), (0,)))


def _nt(a, b):
    return _dot(a, b, ((1,), (1,)))


def _tn(a, b):
    return _dot(a, b, ((0,), (0,)))


def _decay(cum_col, cum_row):
    length = cum_col.shape[0]
    t = lax.broadcasted_iota(jnp.int32, (length, length), 0)
    s = lax.broadcasted_iota(jnp.int32, (length, length), 1)
    causal = t >= s
    spread = cum_col - cum_row
    return jnp.where(causal, jnp.exp(jnp.where(causal, spread, 0.0)), 0.0)


def _masked(q, k, decay):
    return (_nt(q, k) * decay).astype(jnp.bfloat16)


def _head_vectors(cum_ref, cumt_ref, j):
    h = pl.program_id(0) * HB + j
    full = cum_ref[...]
    lane = lax.broadcasted_iota(jnp.int32, full.shape, 1)
    col = jnp.sum(jnp.where(lane == h, full, 0.0), axis=1, keepdims=True)
    row = cumt_ref[pl.ds(h, 1), :]
    fin = col[col.shape[0] - 1 :, :]
    return col, row, jnp.exp(col), jnp.exp(fin - col)


def _lanes(j):
    return slice(j * DH, (j + 1) * DH)


def local_state_kernel(k_ref, v_ref, cum_ref, cumt_ref, s_ref):
    for j in range(HB):
        cols = _lanes(j)
        _, _, _, toend = _head_vectors(cum_ref, cumt_ref, j)
        scaled = (k_ref[:, cols].astype(jnp.float32) * toend).astype(jnp.bfloat16)
        s_ref[j] = _tn(scaled, v_ref[:, cols])


def intra_kernel(q_ref, k_ref, v_ref, cum_ref, cumt_ref, out_ref):
    for j in range(HB):
        cols = _lanes(j)
        col, row, _, _ = _head_vectors(cum_ref, cumt_ref, j)
        decay = _decay(col, row)
        out_ref[:, cols] = _nn(_masked(q_ref[:, cols], k_ref[:, cols], decay), v_ref[:, cols])


def norm_kernel(q_ref, g_ref, intra_ref, st_ref, cum_ref, cumt_ref, gain_ref, og_ref, m_ref, gp_ref):
    for j in range(HB):
        cols = _lanes(j)
        _, _, grow, _ = _head_vectors(cum_ref, cumt_ref, j)
        q = q_ref[:, cols]
        attended = intra_ref[:, cols] + grow * _nn(q, st_ref[j])
        width = attended.shape[-1]
        root_mean = jnp.sqrt(jnp.sum(attended * attended, axis=-1, keepdims=True) / width + epsilon)
        normed = attended / root_mean
        grad_f = g_ref[:, cols].astype(jnp.float32)
        scaled = gain_ref[j] * grad_f
        projected = jnp.sum(scaled * attended, axis=-1, keepdims=True)
        out_grad = ((scaled - attended * projected / (width * root_mean * root_mean)) / root_mean).astype(
            jnp.bfloat16
        )
        og_ref[:, cols] = out_grad
        gp_ref[j] = jnp.sum(grad_f * normed, axis=0, keepdims=True)
        q_scaled = (q.astype(jnp.float32) * grow).astype(jnp.bfloat16)
        m_ref[j] = _tn(q_scaled, out_grad)


def grads_kernel(q_ref, k_ref, v_ref, og_ref, cum_ref, cumt_ref, st_ref, qg_ref, kg_ref, vg_ref):
    for j in range(HB):
        cols = _lanes(j)
        col, row, grow, _ = _head_vectors(cum_ref, cumt_ref, j)
        decay = _decay(col, row)
        q, k, v, og = q_ref[:, cols], k_ref[:, cols], v_ref[:, cols], og_ref[:, cols]
        masked = _masked(q, k, decay)
        rgrad = (_nt(og, v) * decay).astype(jnp.bfloat16)
        qg_ref[:, cols] = (_nn(rgrad, k) + grow * _nt(og, st_ref[j])).astype(jnp.bfloat16)
        kg_ref[:, cols] = _tn(rgrad, q)
        vg_ref[:, cols] = _tn(masked, og)


def finish_kernel(k_ref, v_ref, kg_ref, vg_ref, gl_ref, cum_ref, cumt_ref, ko_ref, vo_ref):
    for j in range(HB):
        cols = _lanes(j)
        _, _, _, toend = _head_vectors(cum_ref, cumt_ref, j)
        grad_low = gl_ref[j]
        ko_ref[:, cols] = (kg_ref[:, cols] + toend * _nt(v_ref[:, cols], grad_low)).astype(jnp.bfloat16)
        vo_ref[:, cols] = (vg_ref[:, cols] + toend * _nn(k_ref[:, cols], grad_low)).astype(jnp.bfloat16)


def _per_head(kernel, ins, outs, heads, length, flops, nbytes, exps=0):
    def spec(kind):
        if kind == "rows":
            return pl.BlockSpec((length, HB * DH), lambda i: (0, i))
        if kind == "cum":
            return pl.BlockSpec((length, heads), lambda i: (0, 0))
        if kind == "cumt":
            return pl.BlockSpec((heads, length), lambda i: (0, 0))
        if kind == "gain":
            return pl.BlockSpec((HB, 1, DH), lambda i: (i, 0, 0))
        return pl.BlockSpec((HB, DH, DH), lambda i: (i, 0, 0))

    shapes = {
        "rows": (length, heads * DH),
        "gain": (heads, 1, DH),
        "square": (heads, DH, DH),
    }
    out_shape = [jax.ShapeDtypeStruct(shapes[kind], dtype) for kind, dtype in outs]
    return pl.pallas_call(
        kernel,
        grid=(heads // HB,),
        in_specs=[spec(kind) for kind, _ in ins],
        out_specs=[spec(kind) for kind, _ in outs],
        out_shape=out_shape,
        cost_estimate=pl.CostEstimate(flops=flops, transcendentals=exps, bytes_accessed=nbytes),
    )(*[x for _, x in ins])


def on_device(query_rows, key_rows, value_rows, cotangent, log_decay, norm_gain):
    length = query_rows.shape[0]
    heads = log_decay.shape[1]
    f32 = jnp.float32
    bf16 = jnp.bfloat16
    t = lax.broadcasted_iota(jnp.int32, (length, length), 0)
    s = lax.broadcasted_iota(jnp.int32, (length, length), 1)
    lower = (t >= s).astype(f32)
    exact = lax.Precision.HIGHEST
    cum = jnp.dot(lower, log_decay, precision=exact)
    cum_t = lax.dot_general(log_decay, lower, (((0,), (1,)), ((), ())), precision=exact)
    final_log = cum[-1]
    gain_rows = norm_gain.reshape(heads, 1, DH)
    q, k, v, g = query_rows, key_rows, value_rows, cotangent
    big = length * length * DH * 2 * heads
    small = length * DH * DH * 2 * heads
    rows_bytes = length * heads * DH * 2
    (local_state,) = _per_head(
        local_state_kernel,
        [("rows", k), ("rows", v), ("cum", cum), ("cumt", cum_t)],
        [("square", f32)],
        heads, length, small, 2 * rows_bytes,
    )
    (intra,) = _per_head(
        intra_kernel,
        [("rows", q), ("rows", k), ("rows", v), ("cum", cum), ("cumt", cum_t)],
        [("rows", f32)],
        heads, length, 2 * big, 5 * rows_bytes, heads * length * length,
    )
    state_in, intra = forward_states(local_state, final_log, intra)
    state_low = state_in.astype(bf16)
    out_grad, moment, gain_part = _per_head(
        norm_kernel,
        [("rows", q), ("rows", g), ("rows", intra), ("square", state_low), ("cum", cum), ("cumt", cum_t), ("gain", gain_rows)],
        [("rows", bf16), ("square", f32), ("gain", f32)],
        heads, length, 2 * small, 5 * rows_bytes,
    )
    query_grad, key_part, value_part = _per_head(
        grads_kernel,
        [("rows", q), ("rows", k), ("rows", v), ("rows", out_grad), ("cum", cum), ("cumt", cum_t),
         ("square", state_low)],
        [("rows", bf16), ("rows", f32), ("rows", f32)],
        heads, length, 5 * big + small, 9 * rows_bytes, heads * length * length,
    )
    grad_state, gain_sum, (query_grad, key_part, value_part) = backward_states(
        moment, final_log, gain_part.reshape(heads * DH), (query_grad, key_part, value_part)
    )
    grad_low = grad_state.astype(bf16)
    key_grad, value_grad = _per_head(
        finish_kernel,
        [("rows", k), ("rows", v), ("rows", key_part), ("rows", value_part), ("square", grad_low),
         ("cum", cum), ("cumt", cum_t)],
        [("rows", bf16), ("rows", bf16)],
        heads, length, 2 * small, 8 * rows_bytes,
    )
    seq_total = length * lax.axis_size(("ctx", "dp"))
    gain_grad = gain_sum * (1.0 / math.sqrt(seq_total))
    return (query_grad, key_grad, value_grad, gain_grad)


def solution(mesh):
    return jax.shard_map(
        on_device,
        mesh=mesh,
        in_specs=(
            P(("groups", "ctx", "dp"), "head"),
            P(("groups", "ctx", "dp"), "head"),
            P(("groups", "ctx", "dp"), "head"),
            P(("groups", "ctx", "dp"), "head"),
            P(("groups", "ctx", "dp"), "head"),
            P("head"),
        ),
        out_specs=(
            P(("groups", "ctx", "dp"), "head"),
            P(("groups", "ctx", "dp"), "head"),
            P(("groups", "ctx", "dp"), "head"),
            P(("groups", "head")),
        ),
        check_vma=False,
    )
```

```python
import math

import jax
import jax.numpy as jnp
from jax import lax
from jax.experimental import pallas as pl
from jax.sharding import PartitionSpec as P

DH = 128
PAD = 8
CHUNKS = 4
TIE_STEP = 1
HB = 8


epsilon = 1e-06


def swap_dp(x):
    return lax.ppermute(x, "dp", perm=[(0, 1), (1, 0)])


def pack_rows(core, *rows):
    heads = core.shape[0]
    pad = [jnp.broadcast_to(r.reshape(heads, 1, -1), (heads, 1, DH)) for r in rows]
    fill = jnp.zeros((heads, PAD - len(rows), DH), jnp.float32)
    return jnp.concatenate([core] + pad + [fill], axis=1)


def halves(x, c):
    half = x.shape[0] // 2
    return lax.dynamic_slice_in_dim(x, c * half, half, axis=0)


def join_halves(mine, other, c):
    first = jnp.where(c == 0, mine, other)
    second = jnp.where(c == 0, other, mine)
    return jnp.concatenate([first, second], axis=0)


def chain_scan(chip_state, chip_decay, later, cover):
    chips = lax.axis_size("ctx")
    z = lax.axis_index("ctx")
    heads = chip_state.shape[0]
    count = min(CHUNKS, heads)
    size = heads // count
    pieces = chip_state.reshape(count, size, DH, DH)
    factor = jnp.exp(chip_decay).reshape(count, size, 1, 1)
    rank = (chips - 1 - z) if later else z
    if later:
        perm = [(i, i - 1) for i in range(1, chips)]
    else:
        perm = [(i, i + 1) for i in range(chips - 1)]
    prefix = jnp.zeros_like(pieces)
    for step in range(count + chips - 2):
        send = jnp.clip(step - rank, 0, count - 1)
        outgoing = factor[send] * prefix[send] + pieces[send]
        arrived = lax.ppermute(outgoing, "ctx", perm=perm)
        where_to = step - rank + 1
        valid = (where_to >= 0) & (where_to < count) & (rank >= 1)
        slot = jnp.clip(where_to, 0, count - 1)
        prefix = prefix.at[slot].set(jnp.where(valid, arrived, prefix[slot]))
        if step == TIE_STEP:
            cover, prefix = lax.optimization_barrier((cover, prefix))
    return prefix.reshape(heads, DH, DH), cover


def forward_states(local_state, final_log, cover):
    c = lax.axis_index("dp")
    message = pack_rows(local_state, final_log)
    other = swap_dp(message)
    own_state, other_state = local_state, other[:, :DH, :]
    own_fin, other_fin = final_log, other[:, DH, 0]
    first = jnp.where(c == 0, own_state, other_state)
    second = jnp.where(c == 0, other_state, own_state)
    fin_first = jnp.where(c == 0, own_fin, other_fin)
    fin_second = jnp.where(c == 0, other_fin, own_fin)
    chip_state = jnp.exp(fin_second)[:, None, None] * first + second
    chip_decay = fin_first + fin_second
    prefix_half, cover = chain_scan(halves(chip_state, c), halves(chip_decay, c), False, cover)
    prefix = join_halves(prefix_half, swap_dp(prefix_half), c)
    core_one = jnp.exp(fin_first)[:, None, None] * prefix + first
    return jnp.where(c == 0, prefix, core_one), cover


def backward_states(moment, final_log, gain_part, cover):
    c = lax.axis_index("dp")
    heads = moment.shape[0]
    gain_rows = gain_part.reshape(heads, DH)
    message = pack_rows(moment, final_log, gain_rows)
    other = swap_dp(message)
    own_m, other_m = moment, other[:, :DH, :]
    own_fin, other_fin = final_log, other[:, DH, 0]
    first = jnp.where(c == 0, own_m, other_m)
    second = jnp.where(c == 0, other_m, own_m)
    fin_first = jnp.where(c == 0, own_fin, other_fin)
    fin_second = jnp.where(c == 0, other_fin, own_fin)
    chip_gain = gain_rows + other[:, DH + 1, :]
    chip_state = first + jnp.exp(fin_first)[:, None, None] * second
    chip_decay = fin_first + fin_second
    chips = lax.axis_size("ctx")
    gain_total = chip_gain
    distance = 1
    while distance < chips:
        partners = [(i, i ^ distance) for i in range(chips)]
        gain_total = gain_total + lax.ppermute(gain_total, "ctx", perm=partners)
        distance *= 2
    suffix_half, cover = chain_scan(halves(chip_state, c), halves(chip_decay, c), True, cover)
    suffix = join_halves(suffix_half, swap_dp(suffix_half), c)
    core_zero = second + jnp.exp(fin_second)[:, None, None] * suffix
    return jnp.where(c == 0, core_zero, suffix), gain_total.reshape(heads * DH), cover


def _dot(a, b, contract):
    return lax.dot_general(a, b, (contract, ((), ())), preferred_element_type=jnp.float32)


def _nn(a, b):
    return _dot(a, b, ((1,), (0,)))


def _nt(a, b):
    return _dot(a, b, ((1,), (1,)))


def _tn(a, b):
    return _dot(a, b, ((0,), (0,)))


def _decay(cum_col, cum_row):
    length = cum_col.shape[0]
    t = lax.broadcasted_iota(jnp.int32, (length, length), 0)
    s = lax.broadcasted_iota(jnp.int32, (length, length), 1)
    causal = t >= s
    spread = cum_col - cum_row
    return jnp.where(causal, jnp.exp(jnp.where(causal, spread, 0.0)), 0.0)


def _masked(q, k, decay):
    return (_nt(q, k) * decay).astype(jnp.bfloat16)


def _head_vectors(cum_ref, cumt_ref, j):
    h = pl.program_id(0) * HB + j
    full = cum_ref[...]
    lane = lax.broadcasted_iota(jnp.int32, full.shape, 1)
    col = jnp.sum(jnp.where(lane == h, full, 0.0), axis=1, keepdims=True)
    row = cumt_ref[pl.ds(h, 1), :]
    fin = col[col.shape[0] - 1 :, :]
    return col, row, jnp.exp(col), jnp.exp(fin - col)


def _lanes(j):
    return slice(j * DH, (j + 1) * DH)


def local_state_kernel(k_ref, v_ref, cum_ref, cumt_ref, s_ref):
    for j in range(HB):
        cols = _lanes(j)
        _, _, _, toend = _head_vectors(cum_ref, cumt_ref, j)
        scaled = (k_ref[:, cols].astype(jnp.float32) * toend).astype(jnp.bfloat16)
        s_ref[j] = _tn(scaled, v_ref[:, cols])


def intra_kernel(q_ref, k_ref, v_ref, cum_ref, cumt_ref, out_ref):
    for j in range(HB):
        cols = _lanes(j)
        col, row, _, _ = _head_vectors(cum_ref, cumt_ref, j)
        decay = _decay(col, row)
        out_ref[:, cols] = _nn(_masked(q_ref[:, cols], k_ref[:, cols], decay), v_ref[:, cols])


def norm_kernel(q_ref, g_ref, intra_ref, st_ref, cum_ref, cumt_ref, gain_ref, og_ref, m_ref, gp_ref):
    for j in range(HB):
        cols = _lanes(j)
        _, _, grow, _ = _head_vectors(cum_ref, cumt_ref, j)
        q = q_ref[:, cols]
        attended = intra_ref[:, cols] + grow * _nn(q, st_ref[j])
        width = attended.shape[-1]
        root_mean = jnp.sqrt(jnp.sum(attended * attended, axis=-1, keepdims=True) / width + epsilon)
        normed = attended / root_mean
        grad_f = g_ref[:, cols].astype(jnp.float32)
        scaled = gain_ref[j] * grad_f
        projected = jnp.sum(scaled * attended, axis=-1, keepdims=True)
        out_grad = ((scaled - attended * projected / (width * root_mean * root_mean)) / root_mean).astype(
            jnp.bfloat16
        )
        og_ref[:, cols] = out_grad
        gp_ref[j] = jnp.sum(grad_f * normed, axis=0, keepdims=True)
        q_scaled = (q.astype(jnp.float32) * grow).astype(jnp.bfloat16)
        m_ref[j] = _tn(q_scaled, out_grad)


def grads_kernel(q_ref, k_ref, v_ref, og_ref, cum_ref, cumt_ref, st_ref, qg_ref, kg_ref, vg_ref):
    for j in range(HB):
        cols = _lanes(j)
        col, row, grow, _ = _head_vectors(cum_ref, cumt_ref, j)
        decay = _decay(col, row)
        q, k, v, og = q_ref[:, cols], k_ref[:, cols], v_ref[:, cols], og_ref[:, cols]
        masked = _masked(q, k, decay)
        rgrad = (_nt(og, v) * decay).astype(jnp.bfloat16)
        qg_ref[:, cols] = (_nn(rgrad, k) + grow * _nt(og, st_ref[j])).astype(jnp.bfloat16)
        kg_ref[:, cols] = _tn(rgrad, q)
        vg_ref[:, cols] = _tn(masked, og)


def finish_kernel(k_ref, v_ref, kg_ref, vg_ref, gl_ref, cum_ref, cumt_ref, ko_ref, vo_ref):
    for j in range(HB):
        cols = _lanes(j)
        _, _, _, toend = _head_vectors(cum_ref, cumt_ref, j)
        grad_low = gl_ref[j]
        ko_ref[:, cols] = (kg_ref[:, cols] + toend * _nt(v_ref[:, cols], grad_low)).astype(jnp.bfloat16)
        vo_ref[:, cols] = (vg_ref[:, cols] + toend * _nn(k_ref[:, cols], grad_low)).astype(jnp.bfloat16)


def _per_head(kernel, ins, outs, heads, length, flops, nbytes, exps=0):
    def spec(kind):
        if kind == "rows":
            return pl.BlockSpec((length, HB * DH), lambda i: (0, i))
        if kind == "cum":
            return pl.BlockSpec((length, heads), lambda i: (0, 0))
        if kind == "cumt":
            return pl.BlockSpec((heads, length), lambda i: (0, 0))
        if kind == "gain":
            return pl.BlockSpec((HB, 1, DH), lambda i: (i, 0, 0))
        return pl.BlockSpec((HB, DH, DH), lambda i: (i, 0, 0))

    shapes = {
        "rows": (length, heads * DH),
        "gain": (heads, 1, DH),
        "square": (heads, DH, DH),
    }
    out_shape = [jax.ShapeDtypeStruct(shapes[kind], dtype) for kind, dtype in outs]
    return pl.pallas_call(
        kernel,
        grid=(heads // HB,),
        in_specs=[spec(kind) for kind, _ in ins],
        out_specs=[spec(kind) for kind, _ in outs],
        out_shape=out_shape,
        cost_estimate=pl.CostEstimate(flops=flops, transcendentals=exps, bytes_accessed=nbytes),
    )(*[x for _, x in ins])


def on_device(query_rows, key_rows, value_rows, cotangent, log_decay, norm_gain):
    length = query_rows.shape[0]
    heads = log_decay.shape[1]
    f32 = jnp.float32
    bf16 = jnp.bfloat16
    t = lax.broadcasted_iota(jnp.int32, (length, length), 0)
    s = lax.broadcasted_iota(jnp.int32, (length, length), 1)
    lower = (t >= s).astype(f32)
    exact = lax.Precision.HIGHEST
    cum = jnp.dot(lower, log_decay, precision=exact)
    cum_t = lax.dot_general(log_decay, lower, (((0,), (1,)), ((), ())), precision=exact)
    final_log = cum[-1]
    gain_rows = norm_gain.reshape(heads, 1, DH)
    q, k, v, g = query_rows, key_rows, value_rows, cotangent
    big = length * length * DH * 2 * heads
    small = length * DH * DH * 2 * heads
    rows_bytes = length * heads * DH * 2
    (local_state,) = _per_head(
        local_state_kernel,
        [("rows", k), ("rows", v), ("cum", cum), ("cumt", cum_t)],
        [("square", f32)],
        heads, length, small, 2 * rows_bytes,
    )
    (intra,) = _per_head(
        intra_kernel,
        [("rows", q), ("rows", k), ("rows", v), ("cum", cum), ("cumt", cum_t)],
        [("rows", f32)],
        heads, length, 2 * big, 5 * rows_bytes, heads * length * length,
    )
    state_in, intra = forward_states(local_state, final_log, intra)
    state_low = state_in.astype(bf16)
    out_grad, moment, gain_part = _per_head(
        norm_kernel,
        [("rows", q), ("rows", g), ("rows", intra), ("square", state_low), ("cum", cum), ("cumt", cum_t), ("gain", gain_rows)],
        [("rows", bf16), ("square", f32), ("gain", f32)],
        heads, length, 2 * small, 5 * rows_bytes,
    )
    query_grad, key_part, value_part = _per_head(
        grads_kernel,
        [("rows", q), ("rows", k), ("rows", v), ("rows", out_grad), ("cum", cum), ("cumt", cum_t),
         ("square", state_low)],
        [("rows", bf16), ("rows", f32), ("rows", f32)],
        heads, length, 5 * big + small, 9 * rows_bytes, heads * length * length,
    )
    grad_state, gain_sum, (query_grad, key_part, value_part) = backward_states(
        moment, final_log, gain_part.reshape(heads * DH), (query_grad, key_part, value_part)
    )
    grad_low = grad_state.astype(bf16)
    key_grad, value_grad = _per_head(
        finish_kernel,
        [("rows", k), ("rows", v), ("rows", key_part), ("rows", value_part), ("square", grad_low),
         ("cum", cum), ("cumt", cum_t)],
        [("rows", bf16), ("rows", bf16)],
        heads, length, 2 * small, 8 * rows_bytes,
    )
    seq_total = length * lax.axis_size(("ctx", "dp"))
    gain_grad = gain_sum * (1.0 / math.sqrt(seq_total))
    return (query_grad, key_grad, value_grad, gain_grad)


def solution(mesh):
    return jax.shard_map(
        on_device,
        mesh=mesh,
        in_specs=(
            P(("groups", "ctx", "dp"), "head"),
            P(("groups", "ctx", "dp"), "head"),
            P(("groups", "ctx", "dp"), "head"),
            P(("groups", "ctx", "dp"), "head"),
            P(("groups", "ctx", "dp"), "head"),
            P("head"),
        ),
        out_specs=(
            P(("groups", "ctx", "dp"), "head"),
            P(("groups", "ctx", "dp"), "head"),
            P(("groups", "ctx", "dp"), "head"),
            P(("groups", "head")),
        ),
        check_vma=False,
    )
```

```python
import functools
import math

import jax
import jax.numpy as jnp
from jax import lax
from jax.experimental import pallas as pl
from jax.sharding import PartitionSpec as P

DH = 128
PAD = 8
CHUNKS = 4
HB = 4


epsilon = 1e-06


def swap_dp(x):
    return lax.ppermute(x, "dp", perm=[(0, 1), (1, 0)])


def pack_rows(core, *rows):
    heads = core.shape[0]
    pad = [jnp.broadcast_to(r.reshape(heads, 1, -1), (heads, 1, DH)) for r in rows]
    fill = jnp.zeros((heads, PAD - len(rows), DH), jnp.float32)
    return jnp.concatenate([core] + pad + [fill], axis=1)


def halves(x, c):
    half = x.shape[0] // 2
    return lax.dynamic_slice_in_dim(x, c * half, half, axis=0)


def join_halves(mine, other, c):
    first = jnp.where(c == 0, mine, other)
    second = jnp.where(c == 0, other, mine)
    return jnp.concatenate([first, second], axis=0)


def chain_scan(chip_state, chip_decay, later, pieces_of_cover):
    chips = lax.axis_size("ctx")
    z = lax.axis_index("ctx")
    heads = chip_state.shape[0]
    count = min(CHUNKS, heads)
    size = heads // count
    pieces = chip_state.reshape(count, size, DH, DH)
    factor = jnp.exp(chip_decay).reshape(count, size, 1, 1)
    rank = (chips - 1 - z) if later else z
    if later:
        perm = [(i, i - 1) for i in range(1, chips)]
    else:
        perm = [(i, i + 1) for i in range(chips - 1)]
    prefix = jnp.zeros_like(pieces)
    cover = None
    steps = count + chips - 2
    for step in range(steps):
        send = jnp.clip(step - rank, 0, count - 1)
        outgoing = factor[send] * prefix[send] + pieces[send]
        arrived = lax.ppermute(outgoing, "ctx", perm=perm)
        where_to = step - rank + 1
        valid = (where_to >= 0) & (where_to < count) & (rank >= 1)
        slot = jnp.clip(where_to, 0, count - 1)
        prefix = prefix.at[slot].set(jnp.where(valid, arrived, prefix[slot]))
        if step < len(pieces_of_cover):
            cover = pieces_of_cover[step](cover)
            cover, prefix = lax.optimization_barrier((cover, prefix))
    for piece in pieces_of_cover[steps:]:
        cover = piece(cover)
    return prefix.reshape(heads, DH, DH), cover


def forward_states(local_state, final_log, cover):
    c = lax.axis_index("dp")
    message = pack_rows(local_state, final_log)
    other = swap_dp(message)
    own_state, other_state = local_state, other[:, :DH, :]
    own_fin, other_fin = final_log, other[:, DH, 0]
    first = jnp.where(c == 0, own_state, other_state)
    second = jnp.where(c == 0, other_state, own_state)
    fin_first = jnp.where(c == 0, own_fin, other_fin)
    fin_second = jnp.where(c == 0, other_fin, own_fin)
    chip_state = jnp.exp(fin_second)[:, None, None] * first + second
    chip_decay = fin_first + fin_second
    prefix_half, cover = chain_scan(halves(chip_state, c), halves(chip_decay, c), False, cover)
    prefix = join_halves(prefix_half, swap_dp(prefix_half), c)
    core_one = jnp.exp(fin_first)[:, None, None] * prefix + first
    return jnp.where(c == 0, prefix, core_one), cover


def backward_states(moment, final_log, gain_part, cover):
    c = lax.axis_index("dp")
    heads = moment.shape[0]
    gain_rows = gain_part.reshape(heads, DH)
    message = pack_rows(moment, final_log, gain_rows)
    other = swap_dp(message)
    own_m, other_m = moment, other[:, :DH, :]
    own_fin, other_fin = final_log, other[:, DH, 0]
    first = jnp.where(c == 0, own_m, other_m)
    second = jnp.where(c == 0, other_m, own_m)
    fin_first = jnp.where(c == 0, own_fin, other_fin)
    fin_second = jnp.where(c == 0, other_fin, own_fin)
    chip_gain = gain_rows + other[:, DH + 1, :]
    chip_state = first + jnp.exp(fin_first)[:, None, None] * second
    chip_decay = fin_first + fin_second
    chips = lax.axis_size("ctx")
    gain_total = chip_gain
    distance = 1
    while distance < chips:
        partners = [(i, i ^ distance) for i in range(chips)]
        gain_total = gain_total + lax.ppermute(gain_total, "ctx", perm=partners)
        distance *= 2
    suffix_half, cover = chain_scan(halves(chip_state, c), halves(chip_decay, c), True, cover)
    suffix = join_halves(suffix_half, swap_dp(suffix_half), c)
    core_zero = second + jnp.exp(fin_second)[:, None, None] * suffix
    return jnp.where(c == 0, core_zero, suffix), gain_total.reshape(heads * DH), cover


def _dot(a, b, contract):
    return lax.dot_general(a, b, (contract, ((), ())), preferred_element_type=jnp.float32)


def _nn(a, b):
    return _dot(a, b, ((1,), (0,)))


def _nt(a, b):
    return _dot(a, b, ((1,), (1,)))


def _tn(a, b):
    return _dot(a, b, ((0,), (0,)))


def _decay(cum_col, cum_row):
    length = cum_col.shape[0]
    t = lax.broadcasted_iota(jnp.int32, (length, length), 0)
    s = lax.broadcasted_iota(jnp.int32, (length, length), 1)
    causal = t >= s
    spread = cum_col - cum_row
    return jnp.where(causal, jnp.exp(jnp.where(causal, spread, 0.0)), 0.0)


def _masked(q, k, decay):
    return (_nt(q, k) * decay).astype(jnp.bfloat16)


def _head_vectors(cum_ref, cumt_ref, j, first=0):
    h = (pl.program_id(0) + first) * HB + j
    full = cum_ref[...]
    lane = lax.broadcasted_iota(jnp.int32, full.shape, 1)
    col = jnp.sum(jnp.where(lane == h, full, 0.0), axis=1, keepdims=True)
    row = cumt_ref[pl.ds(h, 1), :]
    fin = col[col.shape[0] - 1 :, :]
    return col, row, jnp.exp(col), jnp.exp(fin - col)


def _lanes(j):
    return slice(j * DH, (j + 1) * DH)


def local_state_kernel(k_ref, v_ref, cum_ref, cumt_ref, s_ref):
    for j in range(HB):
        cols = _lanes(j)
        _, _, _, toend = _head_vectors(cum_ref, cumt_ref, j)
        scaled = (k_ref[:, cols].astype(jnp.float32) * toend).astype(jnp.bfloat16)
        s_ref[j] = _tn(scaled, v_ref[:, cols])


def intra_kernel(first, q_ref, k_ref, v_ref, cum_ref, cumt_ref, out_ref):
    for j in range(HB):
        cols = _lanes(j)
        col, row, _, _ = _head_vectors(cum_ref, cumt_ref, j, first)
        decay = _decay(col, row)
        out_ref[:, cols] = _nn(_masked(q_ref[:, cols], k_ref[:, cols], decay), v_ref[:, cols])


def norm_kernel(q_ref, g_ref, intra_ref, st_ref, cum_ref, cumt_ref, gain_ref, og_ref, m_ref, gp_ref):
    for j in range(HB):
        cols = _lanes(j)
        _, _, grow, _ = _head_vectors(cum_ref, cumt_ref, j)
        q = q_ref[:, cols]
        attended = intra_ref[:, cols] + grow * _nn(q, st_ref[j])
        width = attended.shape[-1]
        root_mean = jnp.sqrt(jnp.sum(attended * attended, axis=-1, keepdims=True) / width + epsilon)
        normed = attended / root_mean
        grad_f = g_ref[:, cols].astype(jnp.float32)
        scaled = gain_ref[j] * grad_f
        projected = jnp.sum(scaled * attended, axis=-1, keepdims=True)
        out_grad = ((scaled - attended * projected / (width * root_mean * root_mean)) / root_mean).astype(
            jnp.bfloat16
        )
        og_ref[:, cols] = out_grad
        gp_ref[j] = jnp.sum(grad_f * normed, axis=0, keepdims=True)
        q_scaled = (q.astype(jnp.float32) * grow).astype(jnp.bfloat16)
        m_ref[j] = _tn(q_scaled, out_grad)


def grads_kernel(first, q_ref, k_ref, v_ref, og_ref, cum_ref, cumt_ref, st_ref, qg_ref, kg_ref, vg_ref):
    for j in range(HB):
        cols = _lanes(j)
        col, row, grow, _ = _head_vectors(cum_ref, cumt_ref, j, first)
        decay = _decay(col, row)
        q, k, v, og = q_ref[:, cols], k_ref[:, cols], v_ref[:, cols], og_ref[:, cols]
        masked = _masked(q, k, decay)
        rgrad = (_nt(og, v) * decay).astype(jnp.bfloat16)
        qg_ref[:, cols] = (_nn(rgrad, k) + grow * _nt(og, st_ref[j])).astype(jnp.bfloat16)
        kg_ref[:, cols] = _tn(rgrad, q)
        vg_ref[:, cols] = _tn(masked, og)


def finish_kernel(k_ref, v_ref, kg_ref, vg_ref, gl_ref, cum_ref, cumt_ref, ko_ref, vo_ref):
    for j in range(HB):
        cols = _lanes(j)
        _, _, _, toend = _head_vectors(cum_ref, cumt_ref, j)
        grad_low = gl_ref[j]
        ko_ref[:, cols] = (kg_ref[:, cols] + toend * _nt(v_ref[:, cols], grad_low)).astype(jnp.bfloat16)
        vo_ref[:, cols] = (vg_ref[:, cols] + toend * _nn(k_ref[:, cols], grad_low)).astype(jnp.bfloat16)


def _per_head(kernel, ins, outs, heads, length, flops, nbytes, exps=0, part=None, into=None):
    groups = heads // HB
    first, count = (0, groups) if part is None else (part, 1)
    if part is not None:
        kernel = functools.partial(kernel, first)

    def spec(kind):
        if kind == "rows":
            return pl.BlockSpec((length, HB * DH), lambda i: (0, i + first))
        if kind == "cum":
            return pl.BlockSpec((length, heads), lambda i: (0, 0))
        if kind == "cumt":
            return pl.BlockSpec((heads, length), lambda i: (0, 0))
        if kind == "gain":
            return pl.BlockSpec((HB, 1, DH), lambda i: (i + first, 0, 0))
        return pl.BlockSpec((HB, DH, DH), lambda i: (i + first, 0, 0))

    shapes = {
        "rows": (length, heads * DH),
        "gain": (heads, 1, DH),
        "square": (heads, DH, DH),
    }
    out_shape = [jax.ShapeDtypeStruct(shapes[kind], dtype) for kind, dtype in outs]
    in_specs = [spec(kind) for kind, _ in ins]
    operands = [x for _, x in ins]
    aliases = {}
    body = kernel
    if into is not None:
        given = len(ins)
        in_specs += [pl.BlockSpec(memory_space=pl.ANY) for _ in into]
        operands += list(into)
        aliases = {given + i: i for i in range(len(into))}

        def body(*refs):
            kernel(*refs[:given], *refs[given + len(into) :])

    share = count / groups
    return pl.pallas_call(
        body,
        grid=(count,),
        in_specs=in_specs,
        out_specs=[spec(kind) for kind, _ in outs],
        out_shape=out_shape,
        input_output_aliases=aliases,
        cost_estimate=pl.CostEstimate(
            flops=int(flops * share), transcendentals=int(exps * share), bytes_accessed=int(nbytes * share)
        ),
    )(*operands)


def on_device(query_rows, key_rows, value_rows, cotangent, log_decay, norm_gain):
    length = query_rows.shape[0]
    heads = log_decay.shape[1]
    f32 = jnp.float32
    bf16 = jnp.bfloat16
    t = lax.broadcasted_iota(jnp.int32, (length, length), 0)
    s = lax.broadcasted_iota(jnp.int32, (length, length), 1)
    lower = (t >= s).astype(f32)
    exact = lax.Precision.HIGHEST
    cum = jnp.dot(lower, log_decay, precision=exact)
    cum_t = lax.dot_general(log_decay, lower, (((0,), (1,)), ((), ())), precision=exact)
    final_log = cum[-1]
    gain_rows = norm_gain.reshape(heads, 1, DH)
    q, k, v, g = query_rows, key_rows, value_rows, cotangent
    big = length * length * DH * 2 * heads
    small = length * DH * DH * 2 * heads
    rows_bytes = length * heads * DH * 2
    (local_state,) = _per_head(
        local_state_kernel,
        [("rows", k), ("rows", v), ("cum", cum), ("cumt", cum_t)],
        [("square", f32)],
        heads, length, small, 2 * rows_bytes,
    )
    def intra_piece(part, done):
        return _per_head(
            intra_kernel,
            [("rows", q), ("rows", k), ("rows", v), ("cum", cum), ("cumt", cum_t)],
            [("rows", f32)],
            heads, length, 2 * big, 5 * rows_bytes, heads * length * length, part=part, into=done,
        )

    groups = heads // HB
    state_in, (intra,) = forward_states(
        local_state, final_log, [functools.partial(intra_piece, p) for p in range(groups)]
    )
    state_low = state_in.astype(bf16)
    out_grad, moment, gain_part = _per_head(
        norm_kernel,
        [("rows", q), ("rows", g), ("rows", intra), ("square", state_low), ("cum", cum), ("cumt", cum_t), ("gain", gain_rows)],
        [("rows", bf16), ("square", f32), ("gain", f32)],
        heads, length, 2 * small, 5 * rows_bytes,
    )
    def grads_piece(part, done):
        return _per_head(
            grads_kernel,
            [("rows", q), ("rows", k), ("rows", v), ("rows", out_grad), ("cum", cum), ("cumt", cum_t),
             ("square", state_low)],
            [("rows", bf16), ("rows", f32), ("rows", f32)],
            heads, length, 5 * big + small, 9 * rows_bytes, heads * length * length, part=part, into=done,
        )

    grad_state, gain_sum, (query_grad, key_part, value_part) = backward_states(
        moment, final_log, gain_part.reshape(heads * DH), [functools.partial(grads_piece, p) for p in range(groups)]
    )
    grad_low = grad_state.astype(bf16)
    key_grad, value_grad = _per_head(
        finish_kernel,
        [("rows", k), ("rows", v), ("rows", key_part), ("rows", value_part), ("square", grad_low),
         ("cum", cum), ("cumt", cum_t)],
        [("rows", bf16), ("rows", bf16)],
        heads, length, 2 * small, 8 * rows_bytes,
    )
    seq_total = length * lax.axis_size(("ctx", "dp"))
    gain_grad = gain_sum * (1.0 / math.sqrt(seq_total))
    return (query_grad, key_grad, value_grad, gain_grad)


def solution(mesh):
    return jax.shard_map(
        on_device,
        mesh=mesh,
        in_specs=(
            P(("groups", "ctx", "dp"), "head"),
            P(("groups", "ctx", "dp"), "head"),
            P(("groups", "ctx", "dp"), "head"),
            P(("groups", "ctx", "dp"), "head"),
            P(("groups", "ctx", "dp"), "head"),
            P("head"),
        ),
        out_specs=(
            P(("groups", "ctx", "dp"), "head"),
            P(("groups", "ctx", "dp"), "head"),
            P(("groups", "ctx", "dp"), "head"),
            P(("groups", "head")),
        ),
        check_vma=False,
    )
```

```python
import functools
import math

import jax
import jax.numpy as jnp
from jax import lax
from jax.experimental import pallas as pl
from jax.sharding import PartitionSpec as P

DH = 128
PAD = 8
CHUNKS = 4
HB = 4


epsilon = 1e-06


def swap_dp(x):
    return lax.ppermute(x, "dp", perm=[(0, 1), (1, 0)])


def pack_rows(core, *rows):
    heads = core.shape[0]
    pad = [jnp.broadcast_to(r.reshape(heads, 1, -1), (heads, 1, DH)) for r in rows]
    fill = jnp.zeros((heads, PAD - len(rows), DH), jnp.float32)
    return jnp.concatenate([core] + pad + [fill], axis=1)


def halves(x, c):
    half = x.shape[0] // 2
    return lax.dynamic_slice_in_dim(x, c * half, half, axis=0)


def join_halves(mine, other, c):
    first = jnp.where(c == 0, mine, other)
    second = jnp.where(c == 0, other, mine)
    return jnp.concatenate([first, second], axis=0)


def chain_scan(chip_state, chip_decay, later, pieces_of_cover, cover=None):
    chips = lax.axis_size("ctx")
    z = lax.axis_index("ctx")
    heads = chip_state.shape[0]
    count = min(CHUNKS, heads)
    size = heads // count
    pieces = chip_state.reshape(count, size, DH, DH)
    factor = jnp.exp(chip_decay).reshape(count, size, 1, 1)
    rank = (chips - 1 - z) if later else z
    if later:
        perm = [(i, i - 1) for i in range(1, chips)]
    else:
        perm = [(i, i + 1) for i in range(chips - 1)]
    prefix = jnp.zeros_like(pieces)
    steps = count + chips - 2
    for step in range(steps):
        send = jnp.clip(step - rank, 0, count - 1)
        outgoing = factor[send] * prefix[send] + pieces[send]
        arrived = lax.ppermute(outgoing, "ctx", perm=perm)
        where_to = step - rank + 1
        valid = (where_to >= 0) & (where_to < count) & (rank >= 1)
        slot = jnp.clip(where_to, 0, count - 1)
        prefix = prefix.at[slot].set(jnp.where(valid, arrived, prefix[slot]))
        if step < len(pieces_of_cover):
            cover = pieces_of_cover[step](cover)
            cover, prefix = lax.optimization_barrier((cover, prefix))
    for piece in pieces_of_cover[steps:]:
        cover = piece(cover)
    return prefix.reshape(heads, DH, DH), cover


def forward_states(local_state, final_log, cover):
    c = lax.axis_index("dp")
    message = pack_rows(local_state, final_log)
    other = swap_dp(message)
    own_state, other_state = local_state, other[:, :DH, :]
    own_fin, other_fin = final_log, other[:, DH, 0]
    first = jnp.where(c == 0, own_state, other_state)
    second = jnp.where(c == 0, other_state, own_state)
    fin_first = jnp.where(c == 0, own_fin, other_fin)
    fin_second = jnp.where(c == 0, other_fin, own_fin)
    chip_state = jnp.exp(fin_second)[:, None, None] * first + second
    chip_decay = fin_first + fin_second
    prefix_half, cover = chain_scan(halves(chip_state, c), halves(chip_decay, c), False, cover)
    prefix = join_halves(prefix_half, swap_dp(prefix_half), c)
    core_one = jnp.exp(fin_first)[:, None, None] * prefix + first
    return jnp.where(c == 0, prefix, core_one), cover


def backward_states(moment, final_log, gain_part, cover):
    c = lax.axis_index("dp")
    heads = moment.shape[0]
    gain_rows = gain_part.reshape(heads, DH)
    message = pack_rows(moment, final_log, gain_rows)
    other = swap_dp(message)
    own_m, other_m = moment, other[:, :DH, :]
    own_fin, other_fin = final_log, other[:, DH, 0]
    first = jnp.where(c == 0, own_m, other_m)
    second = jnp.where(c == 0, other_m, own_m)
    fin_first = jnp.where(c == 0, own_fin, other_fin)
    fin_second = jnp.where(c == 0, other_fin, own_fin)
    chip_gain = gain_rows + other[:, DH + 1, :]
    chip_state = first + jnp.exp(fin_first)[:, None, None] * second
    chip_decay = fin_first + fin_second
    chips = lax.axis_size("ctx")

    def grads_step(piece, both):
        return piece(both[0]), both[1]

    def gain_step(distance, both):
        partners = [(i, i ^ distance) for i in range(chips)]
        return both[0], both[1] + lax.ppermute(both[1], "ctx", perm=partners)

    steps = [functools.partial(grads_step, piece) for piece in cover]
    distance = 1
    while distance < chips:
        steps.append(functools.partial(gain_step, distance))
        distance *= 2
    suffix_half, (cover, gain_total) = chain_scan(
        halves(chip_state, c), halves(chip_decay, c), True, steps, (None, chip_gain)
    )
    suffix = join_halves(suffix_half, swap_dp(suffix_half), c)
    core_zero = second + jnp.exp(fin_second)[:, None, None] * suffix
    return jnp.where(c == 0, core_zero, suffix), gain_total.reshape(heads * DH), cover


def _dot(a, b, contract):
    return lax.dot_general(a, b, (contract, ((), ())), preferred_element_type=jnp.float32)


def _nn(a, b):
    return _dot(a, b, ((1,), (0,)))


def _nt(a, b):
    return _dot(a, b, ((1,), (1,)))


def _tn(a, b):
    return _dot(a, b, ((0,), (0,)))


def _decay(cum_col, cum_row):
    length = cum_col.shape[0]
    t = lax.broadcasted_iota(jnp.int32, (length, length), 0)
    s = lax.broadcasted_iota(jnp.int32, (length, length), 1)
    causal = t >= s
    spread = cum_col - cum_row
    return jnp.where(causal, jnp.exp(jnp.where(causal, spread, 0.0)), 0.0)


def _masked(q, k, decay):
    return (_nt(q, k) * decay).astype(jnp.bfloat16)


def _head_vectors(cum_ref, cumt_ref, j, first=0):
    h = (pl.program_id(0) + first) * HB + j
    full = cum_ref[...]
    lane = lax.broadcasted_iota(jnp.int32, full.shape, 1)
    col = jnp.sum(jnp.where(lane == h, full, 0.0), axis=1, keepdims=True)
    row = cumt_ref[pl.ds(h, 1), :]
    fin = col[col.shape[0] - 1 :, :]
    return col, row, jnp.exp(col), jnp.exp(fin - col)


def _lanes(j):
    return slice(j * DH, (j + 1) * DH)


def local_state_kernel(k_ref, v_ref, cum_ref, cumt_ref, s_ref):
    for j in range(HB):
        cols = _lanes(j)
        _, _, _, toend = _head_vectors(cum_ref, cumt_ref, j)
        scaled = (k_ref[:, cols].astype(jnp.float32) * toend).astype(jnp.bfloat16)
        s_ref[j] = _tn(scaled, v_ref[:, cols])


def intra_kernel(first, q_ref, k_ref, v_ref, cum_ref, cumt_ref, out_ref):
    for j in range(HB):
        cols = _lanes(j)
        col, row, _, _ = _head_vectors(cum_ref, cumt_ref, j, first)
        decay = _decay(col, row)
        out_ref[:, cols] = _nn(_masked(q_ref[:, cols], k_ref[:, cols], decay), v_ref[:, cols])


def norm_kernel(q_ref, g_ref, intra_ref, st_ref, cum_ref, cumt_ref, gain_ref, og_ref, m_ref, gp_ref):
    for j in range(HB):
        cols = _lanes(j)
        _, _, grow, _ = _head_vectors(cum_ref, cumt_ref, j)
        q = q_ref[:, cols]
        attended = intra_ref[:, cols] + grow * _nn(q, st_ref[j])
        width = attended.shape[-1]
        root_mean = jnp.sqrt(jnp.sum(attended * attended, axis=-1, keepdims=True) / width + epsilon)
        normed = attended / root_mean
        grad_f = g_ref[:, cols].astype(jnp.float32)
        scaled = gain_ref[j] * grad_f
        projected = jnp.sum(scaled * attended, axis=-1, keepdims=True)
        out_grad = ((scaled - attended * projected / (width * root_mean * root_mean)) / root_mean).astype(
            jnp.bfloat16
        )
        og_ref[:, cols] = out_grad
        gp_ref[j] = jnp.sum(grad_f * normed, axis=0, keepdims=True)
        q_scaled = (q.astype(jnp.float32) * grow).astype(jnp.bfloat16)
        m_ref[j] = _tn(q_scaled, out_grad)


def grads_kernel(first, q_ref, k_ref, v_ref, og_ref, cum_ref, cumt_ref, st_ref, qg_ref, kg_ref, vg_ref):
    for j in range(HB):
        cols = _lanes(j)
        col, row, grow, _ = _head_vectors(cum_ref, cumt_ref, j, first)
        decay = _decay(col, row)
        q, k, v, og = q_ref[:, cols], k_ref[:, cols], v_ref[:, cols], og_ref[:, cols]
        masked = _masked(q, k, decay)
        rgrad = (_nt(og, v) * decay).astype(jnp.bfloat16)
        qg_ref[:, cols] = (_nn(rgrad, k) + grow * _nt(og, st_ref[j])).astype(jnp.bfloat16)
        kg_ref[:, cols] = _tn(rgrad, q)
        vg_ref[:, cols] = _tn(masked, og)


def finish_kernel(k_ref, v_ref, kg_ref, vg_ref, gl_ref, cum_ref, cumt_ref, ko_ref, vo_ref):
    for j in range(HB):
        cols = _lanes(j)
        _, _, _, toend = _head_vectors(cum_ref, cumt_ref, j)
        grad_low = gl_ref[j]
        ko_ref[:, cols] = (kg_ref[:, cols] + toend * _nt(v_ref[:, cols], grad_low)).astype(jnp.bfloat16)
        vo_ref[:, cols] = (vg_ref[:, cols] + toend * _nn(k_ref[:, cols], grad_low)).astype(jnp.bfloat16)


def _per_head(kernel, ins, outs, heads, length, flops, nbytes, exps=0, part=None, into=None):
    groups = heads // HB
    first, count = (0, groups) if part is None else (part, 1)
    if part is not None:
        kernel = functools.partial(kernel, first)

    def spec(kind):
        if kind == "rows":
            return pl.BlockSpec((length, HB * DH), lambda i: (0, i + first))
        if kind == "cum":
            return pl.BlockSpec((length, heads), lambda i: (0, 0))
        if kind == "cumt":
            return pl.BlockSpec((heads, length), lambda i: (0, 0))
        if kind == "gain":
            return pl.BlockSpec((HB, 1, DH), lambda i: (i + first, 0, 0))
        return pl.BlockSpec((HB, DH, DH), lambda i: (i + first, 0, 0))

    shapes = {
        "rows": (length, heads * DH),
        "gain": (heads, 1, DH),
        "square": (heads, DH, DH),
    }
    out_shape = [jax.ShapeDtypeStruct(shapes[kind], dtype) for kind, dtype in outs]
    in_specs = [spec(kind) for kind, _ in ins]
    operands = [x for _, x in ins]
    aliases = {}
    body = kernel
    if into is not None:
        given = len(ins)
        in_specs += [pl.BlockSpec(memory_space=pl.ANY) for _ in into]
        operands += list(into)
        aliases = {given + i: i for i in range(len(into))}

        def body(*refs):
            kernel(*refs[:given], *refs[given + len(into) :])

    share = count / groups
    return pl.pallas_call(
        body,
        grid=(count,),
        in_specs=in_specs,
        out_specs=[spec(kind) for kind, _ in outs],
        out_shape=out_shape,
        input_output_aliases=aliases,
        cost_estimate=pl.CostEstimate(
            flops=int(flops * share), transcendentals=int(exps * share), bytes_accessed=int(nbytes * share)
        ),
    )(*operands)


def on_device(query_rows, key_rows, value_rows, cotangent, log_decay, norm_gain):
    length = query_rows.shape[0]
    heads = log_decay.shape[1]
    f32 = jnp.float32
    bf16 = jnp.bfloat16
    t = lax.broadcasted_iota(jnp.int32, (length, length), 0)
    s = lax.broadcasted_iota(jnp.int32, (length, length), 1)
    lower = (t >= s).astype(f32)
    exact = lax.Precision.HIGHEST
    cum = jnp.dot(lower, log_decay, precision=exact)
    cum_t = lax.dot_general(log_decay, lower, (((0,), (1,)), ((), ())), precision=exact)
    final_log = cum[-1]
    gain_rows = norm_gain.reshape(heads, 1, DH)
    q, k, v, g = query_rows, key_rows, value_rows, cotangent
    big = length * length * DH * 2 * heads
    small = length * DH * DH * 2 * heads
    rows_bytes = length * heads * DH * 2
    (local_state,) = _per_head(
        local_state_kernel,
        [("rows", k), ("rows", v), ("cum", cum), ("cumt", cum_t)],
        [("square", f32)],
        heads, length, small, 2 * rows_bytes,
    )
    def intra_piece(part, done):
        return _per_head(
            intra_kernel,
            [("rows", q), ("rows", k), ("rows", v), ("cum", cum), ("cumt", cum_t)],
            [("rows", f32)],
            heads, length, 2 * big, 5 * rows_bytes, heads * length * length, part=part, into=done,
        )

    groups = heads // HB
    state_in, (intra,) = forward_states(
        local_state, final_log, [functools.partial(intra_piece, p) for p in range(groups)]
    )
    state_low = state_in.astype(bf16)
    out_grad, moment, gain_part = _per_head(
        norm_kernel,
        [("rows", q), ("rows", g), ("rows", intra), ("square", state_low), ("cum", cum), ("cumt", cum_t), ("gain", gain_rows)],
        [("rows", bf16), ("square", f32), ("gain", f32)],
        heads, length, 2 * small, 5 * rows_bytes,
    )
    def grads_piece(part, done):
        return _per_head(
            grads_kernel,
            [("rows", q), ("rows", k), ("rows", v), ("rows", out_grad), ("cum", cum), ("cumt", cum_t),
             ("square", state_low)],
            [("rows", bf16), ("rows", f32), ("rows", f32)],
            heads, length, 5 * big + small, 9 * rows_bytes, heads * length * length, part=part, into=done,
        )

    grad_state, gain_sum, (query_grad, key_part, value_part) = backward_states(
        moment, final_log, gain_part.reshape(heads * DH), [functools.partial(grads_piece, p) for p in range(groups)]
    )
    grad_low = grad_state.astype(bf16)
    key_grad, value_grad = _per_head(
        finish_kernel,
        [("rows", k), ("rows", v), ("rows", key_part), ("rows", value_part), ("square", grad_low),
         ("cum", cum), ("cumt", cum_t)],
        [("rows", bf16), ("rows", bf16)],
        heads, length, 2 * small, 8 * rows_bytes,
    )
    seq_total = length * lax.axis_size(("ctx", "dp"))
    gain_grad = gain_sum * (1.0 / math.sqrt(seq_total))
    return (query_grad, key_grad, value_grad, gain_grad)


def solution(mesh):
    return jax.shard_map(
        on_device,
        mesh=mesh,
        in_specs=(
            P(("groups", "ctx", "dp"), "head"),
            P(("groups", "ctx", "dp"), "head"),
            P(("groups", "ctx", "dp"), "head"),
            P(("groups", "ctx", "dp"), "head"),
            P(("groups", "ctx", "dp"), "head"),
            P("head"),
        ),
        out_specs=(
            P(("groups", "ctx", "dp"), "head"),
            P(("groups", "ctx", "dp"), "head"),
            P(("groups", "ctx", "dp"), "head"),
            P(("groups", "head")),
        ),
        check_vma=False,
    )
```

```python
import functools
import math

import jax
import jax.numpy as jnp
from jax import lax
from jax.experimental import pallas as pl
from jax.sharding import PartitionSpec as P

DH = 128
PAD = 8
CHUNKS = 4
HB = 4


epsilon = 1e-06


def swap_dp(x):
    return lax.ppermute(x, "dp", perm=[(0, 1), (1, 0)])


def pack_rows(core, *rows):
    heads = core.shape[0]
    pad = [jnp.broadcast_to(r.reshape(heads, 1, -1), (heads, 1, DH)) for r in rows]
    fill = jnp.zeros((heads, PAD - len(rows), DH), jnp.float32)
    return jnp.concatenate([core] + pad + [fill], axis=1)


def halves(x, c):
    half = x.shape[0] // 2
    return lax.dynamic_slice_in_dim(x, c * half, half, axis=0)


def join_halves(mine, other, c):
    first = jnp.where(c == 0, mine, other)
    second = jnp.where(c == 0, other, mine)
    return jnp.concatenate([first, second], axis=0)


def chain_scan(chip_state, chip_decay, later, pieces_of_cover, cover=None):
    chips = lax.axis_size("ctx")
    z = lax.axis_index("ctx")
    heads = chip_state.shape[0]
    count = min(CHUNKS, heads)
    size = heads // count
    pieces = chip_state.reshape(count, size, DH, DH)
    factor = jnp.exp(chip_decay).reshape(count, size, 1, 1)
    rank = (chips - 1 - z) if later else z
    if later:
        perm = [(i, i - 1) for i in range(1, chips)]
    else:
        perm = [(i, i + 1) for i in range(chips - 1)]
    prefix = jnp.zeros_like(pieces)
    steps = count + chips - 2
    for step in range(steps):
        send = jnp.clip(step - rank, 0, count - 1)
        outgoing = factor[send] * prefix[send] + pieces[send]
        if step < len(pieces_of_cover):
            cover = pieces_of_cover[step](cover, outgoing)
        arrived = lax.ppermute(outgoing, "ctx", perm=perm)
        where_to = step - rank + 1
        valid = (where_to >= 0) & (where_to < count) & (rank >= 1)
        slot = jnp.clip(where_to, 0, count - 1)
        prefix = prefix.at[slot].set(jnp.where(valid, arrived, prefix[slot]))
        if step < len(pieces_of_cover):
            cover, prefix = lax.optimization_barrier((cover, prefix))
    for piece in pieces_of_cover[steps:]:
        cover = piece(cover, prefix)
    return prefix.reshape(heads, DH, DH), cover


def forward_states(local_state, final_log, cover):
    c = lax.axis_index("dp")
    message = pack_rows(local_state, final_log)
    other = swap_dp(message)
    own_state, other_state = local_state, other[:, :DH, :]
    own_fin, other_fin = final_log, other[:, DH, 0]
    first = jnp.where(c == 0, own_state, other_state)
    second = jnp.where(c == 0, other_state, own_state)
    fin_first = jnp.where(c == 0, own_fin, other_fin)
    fin_second = jnp.where(c == 0, other_fin, own_fin)
    chip_state = jnp.exp(fin_second)[:, None, None] * first + second
    chip_decay = fin_first + fin_second
    prefix_half, cover = chain_scan(halves(chip_state, c), halves(chip_decay, c), False, cover)
    prefix = join_halves(prefix_half, swap_dp(prefix_half), c)
    core_one = jnp.exp(fin_first)[:, None, None] * prefix + first
    return jnp.where(c == 0, prefix, core_one), cover


def backward_states(moment, final_log, gain_part, cover):
    c = lax.axis_index("dp")
    heads = moment.shape[0]
    gain_rows = gain_part.reshape(heads, DH)
    message = pack_rows(moment, final_log, gain_rows)
    other = swap_dp(message)
    own_m, other_m = moment, other[:, :DH, :]
    own_fin, other_fin = final_log, other[:, DH, 0]
    first = jnp.where(c == 0, own_m, other_m)
    second = jnp.where(c == 0, other_m, own_m)
    fin_first = jnp.where(c == 0, own_fin, other_fin)
    fin_second = jnp.where(c == 0, other_fin, own_fin)
    chip_gain = gain_rows + other[:, DH + 1, :]
    chip_state = first + jnp.exp(fin_first)[:, None, None] * second
    chip_decay = fin_first + fin_second
    chips = lax.axis_size("ctx")

    def grads_step(piece, both, anchor):
        return piece(both[0], anchor), both[1]

    def gain_step(distance, both, anchor):
        partners = [(i, i ^ distance) for i in range(chips)]
        return both[0], both[1] + lax.ppermute(both[1], "ctx", perm=partners)

    steps = [functools.partial(grads_step, piece) for piece in cover]
    distance = 1
    while distance < chips:
        steps.append(functools.partial(gain_step, distance))
        distance *= 2
    suffix_half, (cover, gain_total) = chain_scan(
        halves(chip_state, c), halves(chip_decay, c), True, steps, (None, chip_gain)
    )
    suffix = join_halves(suffix_half, swap_dp(suffix_half), c)
    core_zero = second + jnp.exp(fin_second)[:, None, None] * suffix
    return jnp.where(c == 0, core_zero, suffix), gain_total.reshape(heads * DH), cover


def _dot(a, b, contract):
    return lax.dot_general(a, b, (contract, ((), ())), preferred_element_type=jnp.float32)


def _nn(a, b):
    return _dot(a, b, ((1,), (0,)))


def _nt(a, b):
    return _dot(a, b, ((1,), (1,)))


def _tn(a, b):
    return _dot(a, b, ((0,), (0,)))


def _decay(cum_col, cum_row):
    length = cum_col.shape[0]
    t = lax.broadcasted_iota(jnp.int32, (length, length), 0)
    s = lax.broadcasted_iota(jnp.int32, (length, length), 1)
    causal = t >= s
    spread = cum_col - cum_row
    return jnp.where(causal, jnp.exp(jnp.where(causal, spread, 0.0)), 0.0)


def _masked(q, k, decay):
    return (_nt(q, k) * decay).astype(jnp.bfloat16)


def _head_vectors(cum_ref, cumt_ref, j, first=0):
    h = (pl.program_id(0) + first) * HB + j
    full = cum_ref[...]
    lane = lax.broadcasted_iota(jnp.int32, full.shape, 1)
    col = jnp.sum(jnp.where(lane == h, full, 0.0), axis=1, keepdims=True)
    row = cumt_ref[pl.ds(h, 1), :]
    fin = col[col.shape[0] - 1 :, :]
    return col, row, jnp.exp(col), jnp.exp(fin - col)


def _lanes(j):
    return slice(j * DH, (j + 1) * DH)


def local_state_kernel(k_ref, v_ref, cum_ref, cumt_ref, s_ref):
    for j in range(HB):
        cols = _lanes(j)
        _, _, _, toend = _head_vectors(cum_ref, cumt_ref, j)
        scaled = (k_ref[:, cols].astype(jnp.float32) * toend).astype(jnp.bfloat16)
        s_ref[j] = _tn(scaled, v_ref[:, cols])


def intra_kernel(first, q_ref, k_ref, v_ref, cum_ref, cumt_ref, out_ref):
    for j in range(HB):
        cols = _lanes(j)
        col, row, _, _ = _head_vectors(cum_ref, cumt_ref, j, first)
        decay = _decay(col, row)
        out_ref[:, cols] = _nn(_masked(q_ref[:, cols], k_ref[:, cols], decay), v_ref[:, cols])


def norm_kernel(q_ref, g_ref, intra_ref, st_ref, cum_ref, cumt_ref, gain_ref, og_ref, m_ref, gp_ref):
    for j in range(HB):
        cols = _lanes(j)
        _, _, grow, _ = _head_vectors(cum_ref, cumt_ref, j)
        q = q_ref[:, cols]
        attended = intra_ref[:, cols] + grow * _nn(q, st_ref[j])
        width = attended.shape[-1]
        root_mean = jnp.sqrt(jnp.sum(attended * attended, axis=-1, keepdims=True) / width + epsilon)
        normed = attended / root_mean
        grad_f = g_ref[:, cols].astype(jnp.float32)
        scaled = gain_ref[j] * grad_f
        projected = jnp.sum(scaled * attended, axis=-1, keepdims=True)
        out_grad = ((scaled - attended * projected / (width * root_mean * root_mean)) / root_mean).astype(
            jnp.bfloat16
        )
        og_ref[:, cols] = out_grad
        gp_ref[j] = jnp.sum(grad_f * normed, axis=0, keepdims=True)
        q_scaled = (q.astype(jnp.float32) * grow).astype(jnp.bfloat16)
        m_ref[j] = _tn(q_scaled, out_grad)


def grads_kernel(first, q_ref, k_ref, v_ref, og_ref, cum_ref, cumt_ref, st_ref, qg_ref, kg_ref, vg_ref):
    for j in range(HB):
        cols = _lanes(j)
        col, row, grow, _ = _head_vectors(cum_ref, cumt_ref, j, first)
        decay = _decay(col, row)
        q, k, v, og = q_ref[:, cols], k_ref[:, cols], v_ref[:, cols], og_ref[:, cols]
        masked = _masked(q, k, decay)
        rgrad = (_nt(og, v) * decay).astype(jnp.bfloat16)
        qg_ref[:, cols] = (_nn(rgrad, k) + grow * _nt(og, st_ref[j])).astype(jnp.bfloat16)
        kg_ref[:, cols] = _tn(rgrad, q)
        vg_ref[:, cols] = _tn(masked, og)


def finish_kernel(k_ref, v_ref, kg_ref, vg_ref, gl_ref, cum_ref, cumt_ref, ko_ref, vo_ref):
    for j in range(HB):
        cols = _lanes(j)
        _, _, _, toend = _head_vectors(cum_ref, cumt_ref, j)
        grad_low = gl_ref[j]
        ko_ref[:, cols] = (kg_ref[:, cols] + toend * _nt(v_ref[:, cols], grad_low)).astype(jnp.bfloat16)
        vo_ref[:, cols] = (vg_ref[:, cols] + toend * _nn(k_ref[:, cols], grad_low)).astype(jnp.bfloat16)


def _per_head(kernel, ins, outs, heads, length, flops, nbytes, exps=0, part=None, into=None):
    groups = heads // HB
    first, count = (0, groups) if part is None else (part, 1)
    if part is not None:
        kernel = functools.partial(kernel, first)

    def spec(kind):
        if kind == "rows":
            return pl.BlockSpec((length, HB * DH), lambda i: (0, i + first))
        if kind == "cum":
            return pl.BlockSpec((length, heads), lambda i: (0, 0))
        if kind == "cumt":
            return pl.BlockSpec((heads, length), lambda i: (0, 0))
        if kind == "gain":
            return pl.BlockSpec((HB, 1, DH), lambda i: (i + first, 0, 0))
        return pl.BlockSpec((HB, DH, DH), lambda i: (i + first, 0, 0))

    shapes = {
        "rows": (length, heads * DH),
        "gain": (heads, 1, DH),
        "square": (heads, DH, DH),
    }
    out_shape = [jax.ShapeDtypeStruct(shapes[kind], dtype) for kind, dtype in outs]
    in_specs = [spec(kind) for kind, _ in ins]
    operands = [x for _, x in ins]
    aliases = {}
    body = kernel
    if into is not None:
        given = len(ins)
        in_specs += [pl.BlockSpec(memory_space=pl.ANY) for _ in into]
        operands += list(into)
        aliases = {given + i: i for i in range(len(into))}

        def body(*refs):
            kernel(*refs[:given], *refs[given + len(into) :])

    share = count / groups
    return pl.pallas_call(
        body,
        grid=(count,),
        in_specs=in_specs,
        out_specs=[spec(kind) for kind, _ in outs],
        out_shape=out_shape,
        input_output_aliases=aliases,
        cost_estimate=pl.CostEstimate(
            flops=int(flops * share), transcendentals=int(exps * share), bytes_accessed=int(nbytes * share)
        ),
    )(*operands)


def on_device(query_rows, key_rows, value_rows, cotangent, log_decay, norm_gain):
    length = query_rows.shape[0]
    heads = log_decay.shape[1]
    f32 = jnp.float32
    bf16 = jnp.bfloat16
    t = lax.broadcasted_iota(jnp.int32, (length, length), 0)
    s = lax.broadcasted_iota(jnp.int32, (length, length), 1)
    lower = (t >= s).astype(f32)
    exact = lax.Precision.HIGHEST
    cum = jnp.dot(lower, log_decay, precision=exact)
    cum_t = lax.dot_general(log_decay, lower, (((0,), (1,)), ((), ())), precision=exact)
    final_log = cum[-1]
    gain_rows = norm_gain.reshape(heads, 1, DH)
    q, k, v, g = query_rows, key_rows, value_rows, cotangent
    big = length * length * DH * 2 * heads
    small = length * DH * DH * 2 * heads
    rows_bytes = length * heads * DH * 2
    (local_state,) = _per_head(
        local_state_kernel,
        [("rows", k), ("rows", v), ("cum", cum), ("cumt", cum_t)],
        [("square", f32)],
        heads, length, small, 2 * rows_bytes,
    )
    def intra_piece(part, done, anchor):
        q_tied, _ = lax.optimization_barrier((q, anchor))
        return _per_head(
            intra_kernel,
            [("rows", q_tied), ("rows", k), ("rows", v), ("cum", cum), ("cumt", cum_t)],
            [("rows", f32)],
            heads, length, 2 * big, 5 * rows_bytes, heads * length * length, part=part, into=done,
        )

    groups = heads // HB
    state_in, (intra,) = forward_states(
        local_state, final_log, [functools.partial(intra_piece, p) for p in range(groups)]
    )
    state_low = state_in.astype(bf16)
    out_grad, moment, gain_part = _per_head(
        norm_kernel,
        [("rows", q), ("rows", g), ("rows", intra), ("square", state_low), ("cum", cum), ("cumt", cum_t), ("gain", gain_rows)],
        [("rows", bf16), ("square", f32), ("gain", f32)],
        heads, length, 2 * small, 5 * rows_bytes,
    )
    def grads_piece(part, done, anchor):
        og_tied, _ = lax.optimization_barrier((out_grad, anchor))
        return _per_head(
            grads_kernel,
            [("rows", q), ("rows", k), ("rows", v), ("rows", og_tied), ("cum", cum), ("cumt", cum_t),
             ("square", state_low)],
            [("rows", bf16), ("rows", f32), ("rows", f32)],
            heads, length, 5 * big + small, 9 * rows_bytes, heads * length * length, part=part, into=done,
        )

    grad_state, gain_sum, (query_grad, key_part, value_part) = backward_states(
        moment, final_log, gain_part.reshape(heads * DH), [functools.partial(grads_piece, p) for p in range(groups)]
    )
    grad_low = grad_state.astype(bf16)
    key_grad, value_grad = _per_head(
        finish_kernel,
        [("rows", k), ("rows", v), ("rows", key_part), ("rows", value_part), ("square", grad_low),
         ("cum", cum), ("cumt", cum_t)],
        [("rows", bf16), ("rows", bf16)],
        heads, length, 2 * small, 8 * rows_bytes,
    )
    seq_total = length * lax.axis_size(("ctx", "dp"))
    gain_grad = gain_sum * (1.0 / math.sqrt(seq_total))
    return (query_grad, key_grad, value_grad, gain_grad)


def solution(mesh):
    return jax.shard_map(
        on_device,
        mesh=mesh,
        in_specs=(
            P(("groups", "ctx", "dp"), "head"),
            P(("groups", "ctx", "dp"), "head"),
            P(("groups", "ctx", "dp"), "head"),
            P(("groups", "ctx", "dp"), "head"),
            P(("groups", "ctx", "dp"), "head"),
            P("head"),
        ),
        out_specs=(
            P(("groups", "ctx", "dp"), "head"),
            P(("groups", "ctx", "dp"), "head"),
            P(("groups", "ctx", "dp"), "head"),
            P(("groups", "head")),
        ),
        check_vma=False,
    )
```

```python
import functools
import math

import jax
import jax.numpy as jnp
from jax import lax
from jax.experimental import pallas as pl
from jax.sharding import PartitionSpec as P

DH = 128
PAD = 8
CHUNKS = 4
HB = 4
PIECE_STEPS = 2


epsilon = 1e-06


def swap_dp(x):
    return lax.ppermute(x, "dp", perm=[(0, 1), (1, 0)])


def pack_rows(core, *rows):
    heads = core.shape[0]
    pad = [jnp.broadcast_to(r.reshape(heads, 1, -1), (heads, 1, DH)) for r in rows]
    fill = jnp.zeros((heads, PAD - len(rows), DH), jnp.float32)
    return jnp.concatenate([core] + pad + [fill], axis=1)


def halves(x, c):
    half = x.shape[0] // 2
    return lax.dynamic_slice_in_dim(x, c * half, half, axis=0)


def join_halves(mine, other, c):
    first = jnp.where(c == 0, mine, other)
    second = jnp.where(c == 0, other, mine)
    return jnp.concatenate([first, second], axis=0)


def chain_scan(chip_state, chip_decay, later, pieces_of_cover, cover=None):
    chips = lax.axis_size("ctx")
    z = lax.axis_index("ctx")
    heads = chip_state.shape[0]
    count = min(CHUNKS, heads)
    size = heads // count
    pieces = chip_state.reshape(count, size, DH, DH)
    factor = jnp.exp(chip_decay).reshape(count, size, 1, 1)
    rank = (chips - 1 - z) if later else z
    if later:
        perm = [(i, i - 1) for i in range(1, chips)]
    else:
        perm = [(i, i + 1) for i in range(chips - 1)]
    prefix = jnp.zeros_like(pieces)
    steps = count + chips - 2
    for step in range(steps):
        send = jnp.clip(step - rank, 0, count - 1)
        outgoing = factor[send] * prefix[send] + pieces[send]
        if step < len(pieces_of_cover):
            cover = pieces_of_cover[step](cover, outgoing)
        arrived = lax.ppermute(outgoing, "ctx", perm=perm)
        where_to = step - rank + 1
        valid = (where_to >= 0) & (where_to < count) & (rank >= 1)
        slot = jnp.clip(where_to, 0, count - 1)
        prefix = prefix.at[slot].set(jnp.where(valid, arrived, prefix[slot]))
        if step < len(pieces_of_cover):
            cover, prefix = lax.optimization_barrier((cover, prefix))
    for piece in pieces_of_cover[steps:]:
        cover = piece(cover, prefix)
    return prefix.reshape(heads, DH, DH), cover


def forward_states(local_state, final_log, cover):
    c = lax.axis_index("dp")
    message = pack_rows(local_state, final_log)
    other = swap_dp(message)
    own_state, other_state = local_state, other[:, :DH, :]
    own_fin, other_fin = final_log, other[:, DH, 0]
    first = jnp.where(c == 0, own_state, other_state)
    second = jnp.where(c == 0, other_state, own_state)
    fin_first = jnp.where(c == 0, own_fin, other_fin)
    fin_second = jnp.where(c == 0, other_fin, own_fin)
    chip_state = jnp.exp(fin_second)[:, None, None] * first + second
    chip_decay = fin_first + fin_second
    prefix_half, cover = chain_scan(halves(chip_state, c), halves(chip_decay, c), False, cover)
    prefix = join_halves(prefix_half, swap_dp(prefix_half), c)
    core_one = jnp.exp(fin_first)[:, None, None] * prefix + first
    return jnp.where(c == 0, prefix, core_one), cover


def backward_states(moment, final_log, gain_part, cover):
    c = lax.axis_index("dp")
    heads = moment.shape[0]
    gain_rows = gain_part.reshape(heads, DH)
    message = pack_rows(moment, final_log, gain_rows)
    other = swap_dp(message)
    own_m, other_m = moment, other[:, :DH, :]
    own_fin, other_fin = final_log, other[:, DH, 0]
    first = jnp.where(c == 0, own_m, other_m)
    second = jnp.where(c == 0, other_m, own_m)
    fin_first = jnp.where(c == 0, own_fin, other_fin)
    fin_second = jnp.where(c == 0, other_fin, own_fin)
    chip_gain = gain_rows + other[:, DH + 1, :]
    chip_state = first + jnp.exp(fin_first)[:, None, None] * second
    chip_decay = fin_first + fin_second
    chips = lax.axis_size("ctx")

    def grads_step(piece, both, anchor):
        return piece(both[0], anchor), both[1]

    def gain_step(distance, both, anchor):
        partners = [(i, i ^ distance) for i in range(chips)]
        return both[0], both[1] + lax.ppermute(both[1], "ctx", perm=partners)

    steps = [functools.partial(grads_step, piece) for piece in cover]
    distance = 1
    while distance < chips:
        steps.append(functools.partial(gain_step, distance))
        distance *= 2
    suffix_half, (cover, gain_total) = chain_scan(
        halves(chip_state, c), halves(chip_decay, c), True, steps, (None, chip_gain)
    )
    suffix = join_halves(suffix_half, swap_dp(suffix_half), c)
    core_zero = second + jnp.exp(fin_second)[:, None, None] * suffix
    return jnp.where(c == 0, core_zero, suffix), gain_total.reshape(heads * DH), cover


def _dot(a, b, contract):
    return lax.dot_general(a, b, (contract, ((), ())), preferred_element_type=jnp.float32)


def _nn(a, b):
    return _dot(a, b, ((1,), (0,)))


def _nt(a, b):
    return _dot(a, b, ((1,), (1,)))


def _tn(a, b):
    return _dot(a, b, ((0,), (0,)))


def _decay(cum_col, cum_row):
    length = cum_col.shape[0]
    t = lax.broadcasted_iota(jnp.int32, (length, length), 0)
    s = lax.broadcasted_iota(jnp.int32, (length, length), 1)
    causal = t >= s
    spread = cum_col - cum_row
    return jnp.where(causal, jnp.exp(jnp.where(causal, spread, 0.0)), 0.0)


def _masked(q, k, decay):
    return (_nt(q, k) * decay).astype(jnp.bfloat16)


def _head_vectors(cum_ref, cumt_ref, j, first=0, hb=None):
    h = (pl.program_id(0) + first) * (HB if hb is None else hb) + j
    full = cum_ref[...]
    lane = lax.broadcasted_iota(jnp.int32, full.shape, 1)
    col = jnp.sum(jnp.where(lane == h, full, 0.0), axis=1, keepdims=True)
    row = cumt_ref[pl.ds(h, 1), :]
    fin = col[col.shape[0] - 1 :, :]
    return col, row, jnp.exp(col), jnp.exp(fin - col)


def _lanes(j):
    return slice(j * DH, (j + 1) * DH)


def local_state_kernel(k_ref, v_ref, cum_ref, cumt_ref, s_ref):
    for j in range(HB):
        cols = _lanes(j)
        _, _, _, toend = _head_vectors(cum_ref, cumt_ref, j)
        scaled = (k_ref[:, cols].astype(jnp.float32) * toend).astype(jnp.bfloat16)
        s_ref[j] = _tn(scaled, v_ref[:, cols])


def intra_kernel(first, hb, q_ref, k_ref, v_ref, cum_ref, cumt_ref, out_ref):
    for j in range(hb):
        cols = _lanes(j)
        col, row, _, _ = _head_vectors(cum_ref, cumt_ref, j, first, hb)
        decay = _decay(col, row)
        out_ref[:, cols] = _nn(_masked(q_ref[:, cols], k_ref[:, cols], decay), v_ref[:, cols])


def norm_kernel(q_ref, g_ref, intra_ref, st_ref, cum_ref, cumt_ref, gain_ref, og_ref, m_ref, gp_ref):
    for j in range(HB):
        cols = _lanes(j)
        _, _, grow, _ = _head_vectors(cum_ref, cumt_ref, j)
        q = q_ref[:, cols]
        attended = intra_ref[:, cols] + grow * _nn(q, st_ref[j])
        width = attended.shape[-1]
        root_mean = jnp.sqrt(jnp.sum(attended * attended, axis=-1, keepdims=True) / width + epsilon)
        normed = attended / root_mean
        grad_f = g_ref[:, cols].astype(jnp.float32)
        scaled = gain_ref[j] * grad_f
        projected = jnp.sum(scaled * attended, axis=-1, keepdims=True)
        out_grad = ((scaled - attended * projected / (width * root_mean * root_mean)) / root_mean).astype(
            jnp.bfloat16
        )
        og_ref[:, cols] = out_grad
        gp_ref[j] = jnp.sum(grad_f * normed, axis=0, keepdims=True)
        q_scaled = (q.astype(jnp.float32) * grow).astype(jnp.bfloat16)
        m_ref[j] = _tn(q_scaled, out_grad)


def grads_kernel(first, hb, q_ref, k_ref, v_ref, og_ref, cum_ref, cumt_ref, st_ref, qg_ref, kg_ref, vg_ref):
    for j in range(hb):
        cols = _lanes(j)
        col, row, grow, _ = _head_vectors(cum_ref, cumt_ref, j, first, hb)
        decay = _decay(col, row)
        q, k, v, og = q_ref[:, cols], k_ref[:, cols], v_ref[:, cols], og_ref[:, cols]
        masked = _masked(q, k, decay)
        rgrad = (_nt(og, v) * decay).astype(jnp.bfloat16)
        qg_ref[:, cols] = (_nn(rgrad, k) + grow * _nt(og, st_ref[j])).astype(jnp.bfloat16)
        kg_ref[:, cols] = _tn(rgrad, q)
        vg_ref[:, cols] = _tn(masked, og)


def finish_kernel(k_ref, v_ref, kg_ref, vg_ref, gl_ref, cum_ref, cumt_ref, ko_ref, vo_ref):
    for j in range(HB):
        cols = _lanes(j)
        _, _, _, toend = _head_vectors(cum_ref, cumt_ref, j)
        grad_low = gl_ref[j]
        ko_ref[:, cols] = (kg_ref[:, cols] + toend * _nt(v_ref[:, cols], grad_low)).astype(jnp.bfloat16)
        vo_ref[:, cols] = (vg_ref[:, cols] + toend * _nn(k_ref[:, cols], grad_low)).astype(jnp.bfloat16)


def _per_head(kernel, ins, outs, heads, length, flops, nbytes, exps=0, part=None, into=None):
    hb = HB if part is None else HB // PIECE_STEPS
    groups = heads // hb
    first, count = (0, groups) if part is None else (part * PIECE_STEPS, PIECE_STEPS)
    if part is not None:
        kernel = functools.partial(kernel, first, hb)

    def spec(kind):
        if kind == "rows":
            return pl.BlockSpec((length, hb * DH), lambda i: (0, i + first))
        if kind == "cum":
            return pl.BlockSpec((length, heads), lambda i: (0, 0))
        if kind == "cumt":
            return pl.BlockSpec((heads, length), lambda i: (0, 0))
        if kind == "gain":
            return pl.BlockSpec((hb, 1, DH), lambda i: (i + first, 0, 0))
        return pl.BlockSpec((hb, DH, DH), lambda i: (i + first, 0, 0))

    shapes = {
        "rows": (length, heads * DH),
        "gain": (heads, 1, DH),
        "square": (heads, DH, DH),
    }
    out_shape = [jax.ShapeDtypeStruct(shapes[kind], dtype) for kind, dtype in outs]
    in_specs = [spec(kind) for kind, _ in ins]
    operands = [x for _, x in ins]
    aliases = {}
    body = kernel
    if into is not None:
        given = len(ins)
        in_specs += [pl.BlockSpec(memory_space=pl.ANY) for _ in into]
        operands += list(into)
        aliases = {given + i: i for i in range(len(into))}

        def body(*refs):
            kernel(*refs[:given], *refs[given + len(into) :])

    share = count / groups
    return pl.pallas_call(
        body,
        grid=(count,),
        in_specs=in_specs,
        out_specs=[spec(kind) for kind, _ in outs],
        out_shape=out_shape,
        input_output_aliases=aliases,
        cost_estimate=pl.CostEstimate(
            flops=int(flops * share), transcendentals=int(exps * share), bytes_accessed=int(nbytes * share)
        ),
    )(*operands)


def on_device(query_rows, key_rows, value_rows, cotangent, log_decay, norm_gain):
    length = query_rows.shape[0]
    heads = log_decay.shape[1]
    f32 = jnp.float32
    bf16 = jnp.bfloat16
    t = lax.broadcasted_iota(jnp.int32, (length, length), 0)
    s = lax.broadcasted_iota(jnp.int32, (length, length), 1)
    lower = (t >= s).astype(f32)
    exact = lax.Precision.HIGHEST
    cum = jnp.dot(lower, log_decay, precision=exact)
    cum_t = lax.dot_general(log_decay, lower, (((0,), (1,)), ((), ())), precision=exact)
    final_log = cum[-1]
    gain_rows = norm_gain.reshape(heads, 1, DH)
    q, k, v, g = query_rows, key_rows, value_rows, cotangent
    big = length * length * DH * 2 * heads
    small = length * DH * DH * 2 * heads
    rows_bytes = length * heads * DH * 2
    (local_state,) = _per_head(
        local_state_kernel,
        [("rows", k), ("rows", v), ("cum", cum), ("cumt", cum_t)],
        [("square", f32)],
        heads, length, small, 2 * rows_bytes,
    )
    def intra_piece(part, done, anchor):
        q_tied, _ = lax.optimization_barrier((q, anchor))
        return _per_head(
            intra_kernel,
            [("rows", q_tied), ("rows", k), ("rows", v), ("cum", cum), ("cumt", cum_t)],
            [("rows", f32)],
            heads, length, 2 * big, 5 * rows_bytes, heads * length * length, part=part, into=done,
        )

    groups = heads // HB
    state_in, (intra,) = forward_states(
        local_state, final_log, [functools.partial(intra_piece, p) for p in range(groups)]
    )
    state_low = state_in.astype(bf16)
    out_grad, moment, gain_part = _per_head(
        norm_kernel,
        [("rows", q), ("rows", g), ("rows", intra), ("square", state_low), ("cum", cum), ("cumt", cum_t), ("gain", gain_rows)],
        [("rows", bf16), ("square", f32), ("gain", f32)],
        heads, length, 2 * small, 5 * rows_bytes,
    )
    def grads_piece(part, done, anchor):
        og_tied, _ = lax.optimization_barrier((out_grad, anchor))
        return _per_head(
            grads_kernel,
            [("rows", q), ("rows", k), ("rows", v), ("rows", og_tied), ("cum", cum), ("cumt", cum_t),
             ("square", state_low)],
            [("rows", bf16), ("rows", f32), ("rows", f32)],
            heads, length, 5 * big + small, 9 * rows_bytes, heads * length * length, part=part, into=done,
        )

    grad_state, gain_sum, (query_grad, key_part, value_part) = backward_states(
        moment, final_log, gain_part.reshape(heads * DH), [functools.partial(grads_piece, p) for p in range(groups)]
    )
    grad_low = grad_state.astype(bf16)
    key_grad, value_grad = _per_head(
        finish_kernel,
        [("rows", k), ("rows", v), ("rows", key_part), ("rows", value_part), ("square", grad_low),
         ("cum", cum), ("cumt", cum_t)],
        [("rows", bf16), ("rows", bf16)],
        heads, length, 2 * small, 8 * rows_bytes,
    )
    seq_total = length * lax.axis_size(("ctx", "dp"))
    gain_grad = gain_sum * (1.0 / math.sqrt(seq_total))
    return (query_grad, key_grad, value_grad, gain_grad)


def solution(mesh):
    return jax.shard_map(
        on_device,
        mesh=mesh,
        in_specs=(
            P(("groups", "ctx", "dp"), "head"),
            P(("groups", "ctx", "dp"), "head"),
            P(("groups", "ctx", "dp"), "head"),
            P(("groups", "ctx", "dp"), "head"),
            P(("groups", "ctx", "dp"), "head"),
            P("head"),
        ),
        out_specs=(
            P(("groups", "ctx", "dp"), "head"),
            P(("groups", "ctx", "dp"), "head"),
            P(("groups", "ctx", "dp"), "head"),
            P(("groups", "head")),
        ),
        check_vma=False,
    )
```

```python
import functools
import math

import jax
import jax.numpy as jnp
from jax import lax
from jax.experimental import pallas as pl
from jax.sharding import PartitionSpec as P

DH = 128
PAD = 8
CHUNKS = 4
HB = 4
PIECE_STEPS = 2


epsilon = 1e-06


def swap_dp(x):
    return lax.ppermute(x, "dp", perm=[(0, 1), (1, 0)])


def pack_rows(core, *rows):
    heads = core.shape[0]
    pad = [jnp.broadcast_to(r.reshape(heads, 1, -1), (heads, 1, DH)) for r in rows]
    fill = jnp.zeros((heads, PAD - len(rows), DH), jnp.float32)
    return jnp.concatenate([core] + pad + [fill], axis=1)


def halves(x, c):
    half = x.shape[0] // 2
    return lax.dynamic_slice_in_dim(x, c * half, half, axis=0)


def join_halves(mine, other, c):
    first = jnp.where(c == 0, mine, other)
    second = jnp.where(c == 0, other, mine)
    return jnp.concatenate([first, second], axis=0)


def chain_scan(chip_state, chip_decay, later, pieces_of_cover, cover=None):
    chips = lax.axis_size("ctx")
    z = lax.axis_index("ctx")
    heads = chip_state.shape[0]
    count = min(CHUNKS, heads)
    size = heads // count
    pieces = chip_state.reshape(count, size, DH, DH)
    factor = jnp.exp(chip_decay).reshape(count, size, 1, 1)
    rank = (chips - 1 - z) if later else z
    if later:
        perm = [(i, i - 1) for i in range(1, chips)]
    else:
        perm = [(i, i + 1) for i in range(chips - 1)]
    prefix = jnp.zeros_like(pieces)
    steps = count + chips - 2
    for step in range(steps):
        send = jnp.clip(step - rank, 0, count - 1)
        outgoing = factor[send] * prefix[send] + pieces[send]
        if step < len(pieces_of_cover):
            cover = pieces_of_cover[step](cover, outgoing)
        arrived = lax.ppermute(outgoing, "ctx", perm=perm)
        where_to = step - rank + 1
        valid = (where_to >= 0) & (where_to < count) & (rank >= 1)
        slot = jnp.clip(where_to, 0, count - 1)
        prefix = prefix.at[slot].set(jnp.where(valid, arrived, prefix[slot]))
        if step < len(pieces_of_cover):
            cover, prefix = lax.optimization_barrier((cover, prefix))
    for piece in pieces_of_cover[steps:]:
        cover = piece(cover, prefix)
    return prefix.reshape(heads, DH, DH), cover


def forward_states(local_state, final_log, cover):
    c = lax.axis_index("dp")
    message = pack_rows(local_state, final_log)
    other = swap_dp(message)
    own_state, other_state = local_state, other[:, :DH, :]
    own_fin, other_fin = final_log, other[:, DH, 0]
    first = jnp.where(c == 0, own_state, other_state)
    second = jnp.where(c == 0, other_state, own_state)
    fin_first = jnp.where(c == 0, own_fin, other_fin)
    fin_second = jnp.where(c == 0, other_fin, own_fin)
    chip_state = jnp.exp(fin_second)[:, None, None] * first + second
    chip_decay = fin_first + fin_second
    prefix_half, cover = chain_scan(halves(chip_state, c), halves(chip_decay, c), False, cover)
    prefix = join_halves(prefix_half, swap_dp(prefix_half), c)
    core_one = jnp.exp(fin_first)[:, None, None] * prefix + first
    return jnp.where(c == 0, prefix, core_one), cover


def backward_states(moment, final_log, gain_part, cover):
    c = lax.axis_index("dp")
    heads = moment.shape[0]
    gain_rows = gain_part.reshape(heads, DH)
    message = pack_rows(moment, final_log, gain_rows)
    other = swap_dp(message)
    own_m, other_m = moment, other[:, :DH, :]
    own_fin, other_fin = final_log, other[:, DH, 0]
    first = jnp.where(c == 0, own_m, other_m)
    second = jnp.where(c == 0, other_m, own_m)
    fin_first = jnp.where(c == 0, own_fin, other_fin)
    fin_second = jnp.where(c == 0, other_fin, own_fin)
    chip_gain = gain_rows + other[:, DH + 1, :]
    chip_state = first + jnp.exp(fin_first)[:, None, None] * second
    chip_decay = fin_first + fin_second
    chips = lax.axis_size("ctx")

    def grads_step(piece, both, anchor):
        return piece(both[0], anchor), both[1]

    def gain_step(distance, both, anchor):
        partners = [(i, i ^ distance) for i in range(chips)]
        return both[0], both[1] + lax.ppermute(both[1], "ctx", perm=partners)

    steps = [functools.partial(grads_step, piece) for piece in cover]
    distance = 1
    while distance < chips:
        steps.append(functools.partial(gain_step, distance))
        distance *= 2
    suffix_half, (cover, gain_total) = chain_scan(
        halves(chip_state, c), halves(chip_decay, c), True, steps, (None, chip_gain)
    )
    suffix = join_halves(suffix_half, swap_dp(suffix_half), c)
    core_zero = second + jnp.exp(fin_second)[:, None, None] * suffix
    return jnp.where(c == 0, core_zero, suffix), gain_total.reshape(heads * DH), cover


def _dot(a, b, contract):
    return lax.dot_general(a, b, (contract, ((), ())), preferred_element_type=jnp.float32)


def _nn(a, b):
    return _dot(a, b, ((1,), (0,)))


def _nt(a, b):
    return _dot(a, b, ((1,), (1,)))


def _tn(a, b):
    return _dot(a, b, ((0,), (0,)))


def _decay(cum_col, cum_row):
    length = cum_col.shape[0]
    t = lax.broadcasted_iota(jnp.int32, (length, length), 0)
    s = lax.broadcasted_iota(jnp.int32, (length, length), 1)
    causal = t >= s
    spread = cum_col - cum_row
    return jnp.where(causal, jnp.exp(jnp.where(causal, spread, 0.0)), 0.0)


def _masked(q, k, decay):
    return (_nt(q, k) * decay).astype(jnp.bfloat16)


def _head_vectors(cum_ref, cumt_ref, j, first=0, hb=None):
    h = (pl.program_id(0) + first) * (HB if hb is None else hb) + j
    full = cum_ref[...]
    lane = lax.broadcasted_iota(jnp.int32, full.shape, 1)
    col = jnp.sum(jnp.where(lane == h, full, 0.0), axis=1, keepdims=True)
    row = cumt_ref[pl.ds(h, 1), :]
    fin = col[col.shape[0] - 1 :, :]
    return col, row, jnp.exp(col), jnp.exp(fin - col)


def _lanes(j):
    return slice(j * DH, (j + 1) * DH)


def local_state_kernel(k_ref, v_ref, cum_ref, cumt_ref, s_ref):
    for j in range(HB):
        cols = _lanes(j)
        _, _, _, toend = _head_vectors(cum_ref, cumt_ref, j)
        scaled = (k_ref[:, cols].astype(jnp.float32) * toend).astype(jnp.bfloat16)
        s_ref[j] = _tn(scaled, v_ref[:, cols])


def _tile_decays(col, row):
    size = col.shape[0] // 2
    tiles = {}
    for i in range(2):
        for j in range(i + 1):
            c = col[i * size : (i + 1) * size]
            r = row[:, j * size : (j + 1) * size]
            tiles[i, j] = _decay(c, r) if i == j else jnp.exp(c - r)
    return tiles, size


def intra_kernel(first, hb, q_ref, k_ref, v_ref, cum_ref, cumt_ref, out_ref):
    for j in range(hb):
        cols = _lanes(j)
        col, row, _, _ = _head_vectors(cum_ref, cumt_ref, j, first, hb)
        tiles, size = _tile_decays(col, row)
        q, k, v = q_ref[:, cols], k_ref[:, cols], v_ref[:, cols]
        for a in range(2):
            qa = q[a * size : (a + 1) * size]
            total = None
            for b in range(a + 1):
                part = _nn(_masked(qa, k[b * size : (b + 1) * size], tiles[a, b]), v[b * size : (b + 1) * size])
                total = part if total is None else total + part
            out_ref[a * size : (a + 1) * size, cols] = total


def norm_kernel(q_ref, g_ref, intra_ref, st_ref, cum_ref, cumt_ref, gain_ref, og_ref, m_ref, gp_ref):
    for j in range(HB):
        cols = _lanes(j)
        _, _, grow, _ = _head_vectors(cum_ref, cumt_ref, j)
        q = q_ref[:, cols]
        attended = intra_ref[:, cols] + grow * _nn(q, st_ref[j])
        width = attended.shape[-1]
        root_mean = jnp.sqrt(jnp.sum(attended * attended, axis=-1, keepdims=True) / width + epsilon)
        normed = attended / root_mean
        grad_f = g_ref[:, cols].astype(jnp.float32)
        scaled = gain_ref[j] * grad_f
        projected = jnp.sum(scaled * attended, axis=-1, keepdims=True)
        out_grad = ((scaled - attended * projected / (width * root_mean * root_mean)) / root_mean).astype(
            jnp.bfloat16
        )
        og_ref[:, cols] = out_grad
        gp_ref[j] = jnp.sum(grad_f * normed, axis=0, keepdims=True)
        q_scaled = (q.astype(jnp.float32) * grow).astype(jnp.bfloat16)
        m_ref[j] = _tn(q_scaled, out_grad)


def grads_kernel(first, hb, q_ref, k_ref, v_ref, og_ref, cum_ref, cumt_ref, st_ref, qg_ref, kg_ref, vg_ref):
    for j in range(hb):
        cols = _lanes(j)
        col, row, grow, _ = _head_vectors(cum_ref, cumt_ref, j, first, hb)
        tiles, size = _tile_decays(col, row)
        q, k, v, og = q_ref[:, cols], k_ref[:, cols], v_ref[:, cols], og_ref[:, cols]
        part = lambda x, i: x[i * size : (i + 1) * size]
        qg = [None, None]
        kg = [None, None]
        vg = [None, None]

        def add(acc, i, value):
            acc[i] = value if acc[i] is None else acc[i] + value

        for a in range(2):
            for b in range(a + 1):
                masked = _masked(part(q, a), part(k, b), tiles[a, b])
                rgrad = (_nt(part(og, a), part(v, b)) * tiles[a, b]).astype(jnp.bfloat16)
                add(qg, a, _nn(rgrad, part(k, b)))
                add(kg, b, _tn(rgrad, part(q, a)))
                add(vg, b, _tn(masked, part(og, a)))
        state_part = grow * _nt(og, st_ref[j])
        for a in range(2):
            rows = slice(a * size, (a + 1) * size)
            qg_ref[rows, cols] = (qg[a] + state_part[rows]).astype(jnp.bfloat16)
            kg_ref[rows, cols] = kg[a]
            vg_ref[rows, cols] = vg[a]


def finish_kernel(k_ref, v_ref, kg_ref, vg_ref, gl_ref, cum_ref, cumt_ref, ko_ref, vo_ref):
    for j in range(HB):
        cols = _lanes(j)
        _, _, _, toend = _head_vectors(cum_ref, cumt_ref, j)
        grad_low = gl_ref[j]
        ko_ref[:, cols] = (kg_ref[:, cols] + toend * _nt(v_ref[:, cols], grad_low)).astype(jnp.bfloat16)
        vo_ref[:, cols] = (vg_ref[:, cols] + toend * _nn(k_ref[:, cols], grad_low)).astype(jnp.bfloat16)


def _per_head(kernel, ins, outs, heads, length, flops, nbytes, exps=0, part=None, into=None):
    hb = HB if part is None else HB // PIECE_STEPS
    groups = heads // hb
    first, count = (0, groups) if part is None else (part * PIECE_STEPS, PIECE_STEPS)
    if part is not None:
        kernel = functools.partial(kernel, first, hb)

    def spec(kind):
        if kind == "rows":
            return pl.BlockSpec((length, hb * DH), lambda i: (0, i + first))
        if kind == "cum":
            return pl.BlockSpec((length, heads), lambda i: (0, 0))
        if kind == "cumt":
            return pl.BlockSpec((heads, length), lambda i: (0, 0))
        if kind == "gain":
            return pl.BlockSpec((hb, 1, DH), lambda i: (i + first, 0, 0))
        return pl.BlockSpec((hb, DH, DH), lambda i: (i + first, 0, 0))

    shapes = {
        "rows": (length, heads * DH),
        "gain": (heads, 1, DH),
        "square": (heads, DH, DH),
    }
    out_shape = [jax.ShapeDtypeStruct(shapes[kind], dtype) for kind, dtype in outs]
    in_specs = [spec(kind) for kind, _ in ins]
    operands = [x for _, x in ins]
    aliases = {}
    body = kernel
    if into is not None:
        given = len(ins)
        in_specs += [pl.BlockSpec(memory_space=pl.ANY) for _ in into]
        operands += list(into)
        aliases = {given + i: i for i in range(len(into))}

        def body(*refs):
            kernel(*refs[:given], *refs[given + len(into) :])

    share = count / groups
    return pl.pallas_call(
        body,
        grid=(count,),
        in_specs=in_specs,
        out_specs=[spec(kind) for kind, _ in outs],
        out_shape=out_shape,
        input_output_aliases=aliases,
        cost_estimate=pl.CostEstimate(
            flops=int(flops * share), transcendentals=int(exps * share), bytes_accessed=int(nbytes * share)
        ),
    )(*operands)


def on_device(query_rows, key_rows, value_rows, cotangent, log_decay, norm_gain):
    length = query_rows.shape[0]
    heads = log_decay.shape[1]
    f32 = jnp.float32
    bf16 = jnp.bfloat16
    t = lax.broadcasted_iota(jnp.int32, (length, length), 0)
    s = lax.broadcasted_iota(jnp.int32, (length, length), 1)
    lower = (t >= s).astype(f32)
    exact = lax.Precision.HIGHEST
    cum = jnp.dot(lower, log_decay, precision=exact)
    cum_t = lax.dot_general(log_decay, lower, (((0,), (1,)), ((), ())), precision=exact)
    final_log = cum[-1]
    gain_rows = norm_gain.reshape(heads, 1, DH)
    q, k, v, g = query_rows, key_rows, value_rows, cotangent
    big = length * length * DH * 2 * heads
    small = length * DH * DH * 2 * heads
    rows_bytes = length * heads * DH * 2
    (local_state,) = _per_head(
        local_state_kernel,
        [("rows", k), ("rows", v), ("cum", cum), ("cumt", cum_t)],
        [("square", f32)],
        heads, length, small, 2 * rows_bytes,
    )
    def intra_piece(part, done, anchor):
        q_tied, _ = lax.optimization_barrier((q, anchor))
        return _per_head(
            intra_kernel,
            [("rows", q_tied), ("rows", k), ("rows", v), ("cum", cum), ("cumt", cum_t)],
            [("rows", f32)],
            heads, length, 2 * big, 5 * rows_bytes, heads * length * length, part=part, into=done,
        )

    groups = heads // HB
    state_in, (intra,) = forward_states(
        local_state, final_log, [functools.partial(intra_piece, p) for p in range(groups)]
    )
    state_low = state_in.astype(bf16)
    out_grad, moment, gain_part = _per_head(
        norm_kernel,
        [("rows", q), ("rows", g), ("rows", intra), ("square", state_low), ("cum", cum), ("cumt", cum_t), ("gain", gain_rows)],
        [("rows", bf16), ("square", f32), ("gain", f32)],
        heads, length, 2 * small, 5 * rows_bytes,
    )
    def grads_piece(part, done, anchor):
        og_tied, _ = lax.optimization_barrier((out_grad, anchor))
        return _per_head(
            grads_kernel,
            [("rows", q), ("rows", k), ("rows", v), ("rows", og_tied), ("cum", cum), ("cumt", cum_t),
             ("square", state_low)],
            [("rows", bf16), ("rows", f32), ("rows", f32)],
            heads, length, 5 * big + small, 9 * rows_bytes, heads * length * length, part=part, into=done,
        )

    grad_state, gain_sum, (query_grad, key_part, value_part) = backward_states(
        moment, final_log, gain_part.reshape(heads * DH), [functools.partial(grads_piece, p) for p in range(groups)]
    )
    grad_low = grad_state.astype(bf16)
    key_grad, value_grad = _per_head(
        finish_kernel,
        [("rows", k), ("rows", v), ("rows", key_part), ("rows", value_part), ("square", grad_low),
         ("cum", cum), ("cumt", cum_t)],
        [("rows", bf16), ("rows", bf16)],
        heads, length, 2 * small, 8 * rows_bytes,
    )
    seq_total = length * lax.axis_size(("ctx", "dp"))
    gain_grad = gain_sum * (1.0 / math.sqrt(seq_total))
    return (query_grad, key_grad, value_grad, gain_grad)


def solution(mesh):
    return jax.shard_map(
        on_device,
        mesh=mesh,
        in_specs=(
            P(("groups", "ctx", "dp"), "head"),
            P(("groups", "ctx", "dp"), "head"),
            P(("groups", "ctx", "dp"), "head"),
            P(("groups", "ctx", "dp"), "head"),
            P(("groups", "ctx", "dp"), "head"),
            P("head"),
        ),
        out_specs=(
            P(("groups", "ctx", "dp"), "head"),
            P(("groups", "ctx", "dp"), "head"),
            P(("groups", "ctx", "dp"), "head"),
            P(("groups", "head")),
        ),
        check_vma=False,
    )
```

```python
import functools
import math

import jax
import jax.numpy as jnp
from jax import lax
from jax.experimental import pallas as pl
from jax.sharding import PartitionSpec as P

DH = 128
PAD = 8
CHUNKS = 2
HB = 4
PIECE_STEPS = 2


epsilon = 1e-06


def swap_dp(x):
    return lax.ppermute(x, "dp", perm=[(0, 1), (1, 0)])


def pack_rows(core, *rows):
    heads = core.shape[0]
    pad = [jnp.broadcast_to(r.reshape(heads, 1, -1), (heads, 1, DH)) for r in rows]
    fill = jnp.zeros((heads, PAD - len(rows), DH), jnp.float32)
    return jnp.concatenate([core] + pad + [fill], axis=1)


def halves(x, c):
    half = x.shape[0] // 2
    return lax.dynamic_slice_in_dim(x, c * half, half, axis=0)


def join_halves(mine, other, c):
    first = jnp.where(c == 0, mine, other)
    second = jnp.where(c == 0, other, mine)
    return jnp.concatenate([first, second], axis=0)


def chain_scan(chip_state, chip_decay, later, pieces_of_cover, cover=None):
    chips = lax.axis_size("ctx")
    z = lax.axis_index("ctx")
    heads = chip_state.shape[0]
    count = min(CHUNKS, heads)
    size = heads // count
    pieces = chip_state.reshape(count, size, DH, DH)
    factor = jnp.exp(chip_decay).reshape(count, size, 1, 1)
    rank = (chips - 1 - z) if later else z
    if later:
        perm = [(i, i - 1) for i in range(1, chips)]
    else:
        perm = [(i, i + 1) for i in range(chips - 1)]
    prefix = jnp.zeros_like(pieces)
    steps = count + chips - 2
    for step in range(steps):
        send = jnp.clip(step - rank, 0, count - 1)
        outgoing = factor[send] * prefix[send] + pieces[send]
        if step < len(pieces_of_cover):
            cover = pieces_of_cover[step](cover, outgoing)
        arrived = lax.ppermute(outgoing, "ctx", perm=perm)
        where_to = step - rank + 1
        valid = (where_to >= 0) & (where_to < count) & (rank >= 1)
        slot = jnp.clip(where_to, 0, count - 1)
        prefix = prefix.at[slot].set(jnp.where(valid, arrived, prefix[slot]))
        if step < len(pieces_of_cover):
            cover, prefix = lax.optimization_barrier((cover, prefix))
    for piece in pieces_of_cover[steps:]:
        cover = piece(cover, prefix)
    return prefix.reshape(heads, DH, DH), cover


def forward_states(local_state, final_log, cover):
    c = lax.axis_index("dp")
    message = pack_rows(local_state, final_log)
    other = swap_dp(message)
    own_state, other_state = local_state, other[:, :DH, :]
    own_fin, other_fin = final_log, other[:, DH, 0]
    first = jnp.where(c == 0, own_state, other_state)
    second = jnp.where(c == 0, other_state, own_state)
    fin_first = jnp.where(c == 0, own_fin, other_fin)
    fin_second = jnp.where(c == 0, other_fin, own_fin)
    chip_state = jnp.exp(fin_second)[:, None, None] * first + second
    chip_decay = fin_first + fin_second
    prefix_half, cover = chain_scan(halves(chip_state, c), halves(chip_decay, c), False, cover)
    prefix = join_halves(prefix_half, swap_dp(prefix_half), c)
    core_one = jnp.exp(fin_first)[:, None, None] * prefix + first
    return jnp.where(c == 0, prefix, core_one), cover


def backward_states(moment, final_log, gain_part, cover):
    c = lax.axis_index("dp")
    heads = moment.shape[0]
    gain_rows = gain_part.reshape(heads, DH)
    message = pack_rows(moment, final_log, gain_rows)
    other = swap_dp(message)
    own_m, other_m = moment, other[:, :DH, :]
    own_fin, other_fin = final_log, other[:, DH, 0]
    first = jnp.where(c == 0, own_m, other_m)
    second = jnp.where(c == 0, other_m, own_m)
    fin_first = jnp.where(c == 0, own_fin, other_fin)
    fin_second = jnp.where(c == 0, other_fin, own_fin)
    chip_gain = gain_rows + other[:, DH + 1, :]
    chip_state = first + jnp.exp(fin_first)[:, None, None] * second
    chip_decay = fin_first + fin_second
    chips = lax.axis_size("ctx")

    def grads_step(piece, both, anchor):
        return piece(both[0], anchor), both[1]

    def both_steps(first, second, both, anchor):
        return second(first(both, anchor), anchor)

    def gain_step(distance, both, anchor):
        partners = [(i, i ^ distance) for i in range(chips)]
        return both[0], both[1] + lax.ppermute(both[1], "ctx", perm=partners)

    rounds = []
    distance = 1
    while distance < chips:
        rounds.append(functools.partial(gain_step, distance))
        distance *= 2
    steps = [functools.partial(grads_step, piece) for piece in cover]
    for index, gain_round in enumerate(rounds):
        if index < len(steps):
            steps[index] = functools.partial(both_steps, steps[index], gain_round)
        else:
            steps.append(gain_round)
    suffix_half, (cover, gain_total) = chain_scan(
        halves(chip_state, c), halves(chip_decay, c), True, steps, (None, chip_gain)
    )
    suffix = join_halves(suffix_half, swap_dp(suffix_half), c)
    core_zero = second + jnp.exp(fin_second)[:, None, None] * suffix
    return jnp.where(c == 0, core_zero, suffix), gain_total.reshape(heads * DH), cover


def _dot(a, b, contract):
    return lax.dot_general(a, b, (contract, ((), ())), preferred_element_type=jnp.float32)


def _nn(a, b):
    return _dot(a, b, ((1,), (0,)))


def _nt(a, b):
    return _dot(a, b, ((1,), (1,)))


def _tn(a, b):
    return _dot(a, b, ((0,), (0,)))


def _decay(cum_col, cum_row):
    length = cum_col.shape[0]
    t = lax.broadcasted_iota(jnp.int32, (length, length), 0)
    s = lax.broadcasted_iota(jnp.int32, (length, length), 1)
    causal = t >= s
    spread = cum_col - cum_row
    return jnp.where(causal, jnp.exp(jnp.where(causal, spread, 0.0)), 0.0)


def _masked(q, k, decay):
    return (_nt(q, k) * decay).astype(jnp.bfloat16)


def _head_vectors(cum_ref, cumt_ref, j, first=0, hb=None):
    h = (pl.program_id(0) + first) * (HB if hb is None else hb) + j
    full = cum_ref[...]
    lane = lax.broadcasted_iota(jnp.int32, full.shape, 1)
    col = jnp.sum(jnp.where(lane == h, full, 0.0), axis=1, keepdims=True)
    row = cumt_ref[pl.ds(h, 1), :]
    fin = col[col.shape[0] - 1 :, :]
    return col, row, jnp.exp(col), jnp.exp(fin - col)


def _lanes(j):
    return slice(j * DH, (j + 1) * DH)


def local_state_kernel(k_ref, v_ref, cum_ref, cumt_ref, s_ref):
    for j in range(HB):
        cols = _lanes(j)
        _, _, _, toend = _head_vectors(cum_ref, cumt_ref, j)
        scaled = (k_ref[:, cols].astype(jnp.float32) * toend).astype(jnp.bfloat16)
        s_ref[j] = _tn(scaled, v_ref[:, cols])


def _tile_decays(col, row):
    size = col.shape[0] // 2
    tiles = {}
    for i in range(2):
        for j in range(i + 1):
            c = col[i * size : (i + 1) * size]
            r = row[:, j * size : (j + 1) * size]
            tiles[i, j] = _decay(c, r) if i == j else jnp.exp(c - r)
    return tiles, size


def intra_kernel(first, hb, q_ref, k_ref, v_ref, cum_ref, cumt_ref, out_ref):
    for j in range(hb):
        cols = _lanes(j)
        col, row, _, _ = _head_vectors(cum_ref, cumt_ref, j, first, hb)
        tiles, size = _tile_decays(col, row)
        q, k, v = q_ref[:, cols], k_ref[:, cols], v_ref[:, cols]
        for a in range(2):
            qa = q[a * size : (a + 1) * size]
            total = None
            for b in range(a + 1):
                part = _nn(_masked(qa, k[b * size : (b + 1) * size], tiles[a, b]), v[b * size : (b + 1) * size])
                total = part if total is None else total + part
            out_ref[a * size : (a + 1) * size, cols] = total


def norm_kernel(q_ref, g_ref, intra_ref, st_ref, cum_ref, cumt_ref, gain_ref, og_ref, m_ref, gp_ref):
    for j in range(HB):
        cols = _lanes(j)
        _, _, grow, _ = _head_vectors(cum_ref, cumt_ref, j)
        q = q_ref[:, cols]
        attended = intra_ref[:, cols] + grow * _nn(q, st_ref[j])
        width = attended.shape[-1]
        root_mean = jnp.sqrt(jnp.sum(attended * attended, axis=-1, keepdims=True) / width + epsilon)
        normed = attended / root_mean
        grad_f = g_ref[:, cols].astype(jnp.float32)
        scaled = gain_ref[j] * grad_f
        projected = jnp.sum(scaled * attended, axis=-1, keepdims=True)
        out_grad = ((scaled - attended * projected / (width * root_mean * root_mean)) / root_mean).astype(
            jnp.bfloat16
        )
        og_ref[:, cols] = out_grad
        gp_ref[j] = jnp.sum(grad_f * normed, axis=0, keepdims=True)
        q_scaled = (q.astype(jnp.float32) * grow).astype(jnp.bfloat16)
        m_ref[j] = _tn(q_scaled, out_grad)


def grads_kernel(first, hb, q_ref, k_ref, v_ref, og_ref, cum_ref, cumt_ref, st_ref, qg_ref, kg_ref, vg_ref):
    for j in range(hb):
        cols = _lanes(j)
        col, row, grow, _ = _head_vectors(cum_ref, cumt_ref, j, first, hb)
        tiles, size = _tile_decays(col, row)
        q, k, v, og = q_ref[:, cols], k_ref[:, cols], v_ref[:, cols], og_ref[:, cols]
        part = lambda x, i: x[i * size : (i + 1) * size]
        qg = [None, None]
        kg = [None, None]
        vg = [None, None]

        def add(acc, i, value):
            acc[i] = value if acc[i] is None else acc[i] + value

        for a in range(2):
            for b in range(a + 1):
                masked = _masked(part(q, a), part(k, b), tiles[a, b])
                rgrad = (_nt(part(og, a), part(v, b)) * tiles[a, b]).astype(jnp.bfloat16)
                add(qg, a, _nn(rgrad, part(k, b)))
                add(kg, b, _tn(rgrad, part(q, a)))
                add(vg, b, _tn(masked, part(og, a)))
        state_part = grow * _nt(og, st_ref[j])
        for a in range(2):
            rows = slice(a * size, (a + 1) * size)
            qg_ref[rows, cols] = (qg[a] + state_part[rows]).astype(jnp.bfloat16)
            kg_ref[rows, cols] = kg[a]
            vg_ref[rows, cols] = vg[a]


def finish_kernel(k_ref, v_ref, kg_ref, vg_ref, gl_ref, cum_ref, cumt_ref, ko_ref, vo_ref):
    for j in range(HB):
        cols = _lanes(j)
        _, _, _, toend = _head_vectors(cum_ref, cumt_ref, j)
        grad_low = gl_ref[j]
        ko_ref[:, cols] = (kg_ref[:, cols] + toend * _nt(v_ref[:, cols], grad_low)).astype(jnp.bfloat16)
        vo_ref[:, cols] = (vg_ref[:, cols] + toend * _nn(k_ref[:, cols], grad_low)).astype(jnp.bfloat16)


def _per_head(kernel, ins, outs, heads, length, flops, nbytes, exps=0, part=None, into=None):
    hb = HB if part is None else HB // PIECE_STEPS
    groups = heads // hb
    first, count = (0, groups) if part is None else (part * PIECE_STEPS, PIECE_STEPS)
    if part is not None:
        kernel = functools.partial(kernel, first, hb)

    def spec(kind):
        if kind == "rows":
            return pl.BlockSpec((length, hb * DH), lambda i: (0, i + first))
        if kind == "cum":
            return pl.BlockSpec((length, heads), lambda i: (0, 0))
        if kind == "cumt":
            return pl.BlockSpec((heads, length), lambda i: (0, 0))
        if kind == "gain":
            return pl.BlockSpec((hb, 1, DH), lambda i: (i + first, 0, 0))
        return pl.BlockSpec((hb, DH, DH), lambda i: (i + first, 0, 0))

    shapes = {
        "rows": (length, heads * DH),
        "gain": (heads, 1, DH),
        "square": (heads, DH, DH),
    }
    out_shape = [jax.ShapeDtypeStruct(shapes[kind], dtype) for kind, dtype in outs]
    in_specs = [spec(kind) for kind, _ in ins]
    operands = [x for _, x in ins]
    aliases = {}
    body = kernel
    if into is not None:
        given = len(ins)
        in_specs += [pl.BlockSpec(memory_space=pl.ANY) for _ in into]
        operands += list(into)
        aliases = {given + i: i for i in range(len(into))}

        def body(*refs):
            kernel(*refs[:given], *refs[given + len(into) :])

    share = count / groups
    return pl.pallas_call(
        body,
        grid=(count,),
        in_specs=in_specs,
        out_specs=[spec(kind) for kind, _ in outs],
        out_shape=out_shape,
        input_output_aliases=aliases,
        cost_estimate=pl.CostEstimate(
            flops=int(flops * share), transcendentals=int(exps * share), bytes_accessed=int(nbytes * share)
        ),
    )(*operands)


def on_device(query_rows, key_rows, value_rows, cotangent, log_decay, norm_gain):
    length = query_rows.shape[0]
    heads = log_decay.shape[1]
    f32 = jnp.float32
    bf16 = jnp.bfloat16
    t = lax.broadcasted_iota(jnp.int32, (length, length), 0)
    s = lax.broadcasted_iota(jnp.int32, (length, length), 1)
    lower = (t >= s).astype(f32)
    exact = lax.Precision.HIGHEST
    cum = jnp.dot(lower, log_decay, precision=exact)
    cum_t = lax.dot_general(log_decay, lower, (((0,), (1,)), ((), ())), precision=exact)
    final_log = cum[-1]
    gain_rows = norm_gain.reshape(heads, 1, DH)
    q, k, v, g = query_rows, key_rows, value_rows, cotangent
    big = length * length * DH * 2 * heads
    small = length * DH * DH * 2 * heads
    rows_bytes = length * heads * DH * 2
    (local_state,) = _per_head(
        local_state_kernel,
        [("rows", k), ("rows", v), ("cum", cum), ("cumt", cum_t)],
        [("square", f32)],
        heads, length, small, 2 * rows_bytes,
    )
    def intra_piece(part, done, anchor):
        q_tied, _ = lax.optimization_barrier((q, anchor))
        return _per_head(
            intra_kernel,
            [("rows", q_tied), ("rows", k), ("rows", v), ("cum", cum), ("cumt", cum_t)],
            [("rows", f32)],
            heads, length, 2 * big, 5 * rows_bytes, heads * length * length, part=part, into=done,
        )

    groups = heads // HB
    state_in, (intra,) = forward_states(
        local_state, final_log, [functools.partial(intra_piece, p) for p in range(groups)]
    )
    state_low = state_in.astype(bf16)
    out_grad, moment, gain_part = _per_head(
        norm_kernel,
        [("rows", q), ("rows", g), ("rows", intra), ("square", state_low), ("cum", cum), ("cumt", cum_t), ("gain", gain_rows)],
        [("rows", bf16), ("square", f32), ("gain", f32)],
        heads, length, 2 * small, 5 * rows_bytes,
    )
    def grads_piece(part, done, anchor):
        og_tied, _ = lax.optimization_barrier((out_grad, anchor))
        return _per_head(
            grads_kernel,
            [("rows", q), ("rows", k), ("rows", v), ("rows", og_tied), ("cum", cum), ("cumt", cum_t),
             ("square", state_low)],
            [("rows", bf16), ("rows", f32), ("rows", f32)],
            heads, length, 5 * big + small, 9 * rows_bytes, heads * length * length, part=part, into=done,
        )

    grad_state, gain_sum, (query_grad, key_part, value_part) = backward_states(
        moment, final_log, gain_part.reshape(heads * DH), [functools.partial(grads_piece, p) for p in range(groups)]
    )
    grad_low = grad_state.astype(bf16)
    key_grad, value_grad = _per_head(
        finish_kernel,
        [("rows", k), ("rows", v), ("rows", key_part), ("rows", value_part), ("square", grad_low),
         ("cum", cum), ("cumt", cum_t)],
        [("rows", bf16), ("rows", bf16)],
        heads, length, 2 * small, 8 * rows_bytes,
    )
    seq_total = length * lax.axis_size(("ctx", "dp"))
    gain_grad = gain_sum * (1.0 / math.sqrt(seq_total))
    return (query_grad, key_grad, value_grad, gain_grad)


def solution(mesh):
    return jax.shard_map(
        on_device,
        mesh=mesh,
        in_specs=(
            P(("groups", "ctx", "dp"), "head"),
            P(("groups", "ctx", "dp"), "head"),
            P(("groups", "ctx", "dp"), "head"),
            P(("groups", "ctx", "dp"), "head"),
            P(("groups", "ctx", "dp"), "head"),
            P("head"),
        ),
        out_specs=(
            P(("groups", "ctx", "dp"), "head"),
            P(("groups", "ctx", "dp"), "head"),
            P(("groups", "ctx", "dp"), "head"),
            P(("groups", "head")),
        ),
        check_vma=False,
    )
```

```python
import functools
import math

import jax
import jax.numpy as jnp
from jax import lax
from jax.experimental import pallas as pl
from jax.sharding import PartitionSpec as P

DH = 128
PAD = 8
CHUNKS = 2
HB = 4
PIECE_STEPS = 2


epsilon = 1e-06


def swap_dp(x):
    return lax.ppermute(x, "dp", perm=[(0, 1), (1, 0)])


def pack_rows(core, *rows):
    heads = core.shape[0]
    pad = [jnp.broadcast_to(r.reshape(heads, 1, -1), (heads, 1, DH)) for r in rows]
    fill = jnp.zeros((heads, PAD - len(rows), DH), jnp.float32)
    return jnp.concatenate([core] + pad + [fill], axis=1)


def halves(x, c):
    half = x.shape[0] // 2
    return lax.dynamic_slice_in_dim(x, c * half, half, axis=0)


def join_halves(mine, other, c):
    first = jnp.where(c == 0, mine, other)
    second = jnp.where(c == 0, other, mine)
    return jnp.concatenate([first, second], axis=0)


def chain_scan(chip_state, chip_decay, later, pieces_of_cover, cover=None):
    chips = lax.axis_size("ctx")
    z = lax.axis_index("ctx")
    heads = chip_state.shape[0]
    count = min(CHUNKS, heads)
    size = heads // count
    pieces = chip_state.reshape(count, size, DH, DH)
    factor = jnp.exp(chip_decay).reshape(count, size, 1, 1)
    rank = (chips - 1 - z) if later else z
    if later:
        perm = [(i, i - 1) for i in range(1, chips)]
    else:
        perm = [(i, i + 1) for i in range(chips - 1)]
    prefix = jnp.zeros_like(pieces)
    steps = count + chips - 2
    for step in range(steps):
        send = jnp.clip(step - rank, 0, count - 1)
        outgoing = factor[send] * prefix[send] + pieces[send]
        if step < len(pieces_of_cover):
            cover = pieces_of_cover[step](cover, outgoing)
        arrived = lax.ppermute(outgoing, "ctx", perm=perm)
        where_to = step - rank + 1
        valid = (where_to >= 0) & (where_to < count) & (rank >= 1)
        slot = jnp.clip(where_to, 0, count - 1)
        prefix = prefix.at[slot].set(jnp.where(valid, arrived, prefix[slot]))
        if step < len(pieces_of_cover):
            cover, prefix = lax.optimization_barrier((cover, prefix))
    for piece in pieces_of_cover[steps:]:
        cover = piece(cover, prefix)
    return prefix.reshape(heads, DH, DH), cover


def forward_states(message, final_log, cover):
    c = lax.axis_index("dp")
    local_state = message[:, :DH, :]
    other = swap_dp(message)
    own_state, other_state = local_state, other[:, :DH, :]
    own_fin, other_fin = final_log, other[:, DH, 0]
    first = jnp.where(c == 0, own_state, other_state)
    second = jnp.where(c == 0, other_state, own_state)
    fin_first = jnp.where(c == 0, own_fin, other_fin)
    fin_second = jnp.where(c == 0, other_fin, own_fin)
    chip_state = jnp.exp(fin_second)[:, None, None] * first + second
    chip_decay = fin_first + fin_second
    prefix_half, cover = chain_scan(halves(chip_state, c), halves(chip_decay, c), False, cover)
    prefix = join_halves(prefix_half, swap_dp(prefix_half), c)
    core_one = jnp.exp(fin_first)[:, None, None] * prefix + first
    return jnp.where(c == 0, prefix, core_one), cover


def backward_states(message, final_log, cover):
    c = lax.axis_index("dp")
    heads = message.shape[0]
    moment = message[:, :DH, :]
    gain_rows = message[:, DH + 1, :]
    other = swap_dp(message)
    own_m, other_m = moment, other[:, :DH, :]
    own_fin, other_fin = final_log, other[:, DH, 0]
    first = jnp.where(c == 0, own_m, other_m)
    second = jnp.where(c == 0, other_m, own_m)
    fin_first = jnp.where(c == 0, own_fin, other_fin)
    fin_second = jnp.where(c == 0, other_fin, own_fin)
    chip_gain = gain_rows + other[:, DH + 1, :]
    chip_state = first + jnp.exp(fin_first)[:, None, None] * second
    chip_decay = fin_first + fin_second
    chips = lax.axis_size("ctx")

    def grads_step(piece, both, anchor):
        return piece(both[0], anchor), both[1]

    def both_steps(first, second, both, anchor):
        return second(first(both, anchor), anchor)

    def gain_step(distance, both, anchor):
        partners = [(i, i ^ distance) for i in range(chips)]
        return both[0], both[1] + lax.ppermute(both[1], "ctx", perm=partners)

    rounds = []
    distance = 1
    while distance < chips:
        rounds.append(functools.partial(gain_step, distance))
        distance *= 2
    steps = [functools.partial(grads_step, piece) for piece in cover]
    for index, gain_round in enumerate(rounds):
        if index < len(steps):
            steps[index] = functools.partial(both_steps, steps[index], gain_round)
        else:
            steps.append(gain_round)
    suffix_half, (cover, gain_total) = chain_scan(
        halves(chip_state, c), halves(chip_decay, c), True, steps, (None, chip_gain)
    )
    suffix = join_halves(suffix_half, swap_dp(suffix_half), c)
    core_zero = second + jnp.exp(fin_second)[:, None, None] * suffix
    return jnp.where(c == 0, core_zero, suffix), gain_total.reshape(heads * DH), cover


def _dot(a, b, contract):
    return lax.dot_general(a, b, (contract, ((), ())), preferred_element_type=jnp.float32)


def _nn(a, b):
    return _dot(a, b, ((1,), (0,)))


def _nt(a, b):
    return _dot(a, b, ((1,), (1,)))


def _tn(a, b):
    return _dot(a, b, ((0,), (0,)))


def _decay(cum_col, cum_row):
    length = cum_col.shape[0]
    t = lax.broadcasted_iota(jnp.int32, (length, length), 0)
    s = lax.broadcasted_iota(jnp.int32, (length, length), 1)
    causal = t >= s
    spread = cum_col - cum_row
    return jnp.where(causal, jnp.exp(jnp.where(causal, spread, 0.0)), 0.0)


def _masked(q, k, decay):
    return (_nt(q, k) * decay).astype(jnp.bfloat16)


def _head_vectors(cum_ref, cumt_ref, j, first=0, hb=None):
    h = (pl.program_id(0) + first) * (HB if hb is None else hb) + j
    full = cum_ref[...]
    lane = lax.broadcasted_iota(jnp.int32, full.shape, 1)
    col = jnp.sum(jnp.where(lane == h, full, 0.0), axis=1, keepdims=True)
    row = cumt_ref[pl.ds(h, 1), :]
    fin = col[col.shape[0] - 1 :, :]
    return col, row, jnp.exp(col), jnp.exp(fin - col)


def _lanes(j):
    return slice(j * DH, (j + 1) * DH)


def _pad_rows(*rows):
    slot = lax.broadcasted_iota(jnp.int32, (PAD, DH), 0)
    block = jnp.zeros((PAD, DH), jnp.float32)
    for index, value in enumerate(rows):
        block = jnp.where(slot == index, jnp.broadcast_to(value, (PAD, DH)), block)
    return block


def local_state_kernel(k_ref, v_ref, cum_ref, cumt_ref, s_ref):
    for j in range(HB):
        cols = _lanes(j)
        col, _, _, toend = _head_vectors(cum_ref, cumt_ref, j)
        scaled = (k_ref[:, cols].astype(jnp.float32) * toend).astype(jnp.bfloat16)
        s_ref[j, :DH, :] = _tn(scaled, v_ref[:, cols])
        s_ref[j, DH:, :] = _pad_rows(col[col.shape[0] - 1 :, :])


def _tile_decays(col, row):
    size = col.shape[0] // 2
    tiles = {}
    for i in range(2):
        for j in range(i + 1):
            c = col[i * size : (i + 1) * size]
            r = row[:, j * size : (j + 1) * size]
            tiles[i, j] = _decay(c, r) if i == j else jnp.exp(c - r)
    return tiles, size


def intra_kernel(first, hb, q_ref, k_ref, v_ref, cum_ref, cumt_ref, out_ref):
    for j in range(hb):
        cols = _lanes(j)
        col, row, _, _ = _head_vectors(cum_ref, cumt_ref, j, first, hb)
        tiles, size = _tile_decays(col, row)
        q, k, v = q_ref[:, cols], k_ref[:, cols], v_ref[:, cols]
        for a in range(2):
            qa = q[a * size : (a + 1) * size]
            total = None
            for b in range(a + 1):
                part = _nn(_masked(qa, k[b * size : (b + 1) * size], tiles[a, b]), v[b * size : (b + 1) * size])
                total = part if total is None else total + part
            out_ref[a * size : (a + 1) * size, cols] = total


def norm_kernel(q_ref, g_ref, intra_ref, st_ref, cum_ref, cumt_ref, gain_ref, og_ref, m_ref):
    for j in range(HB):
        cols = _lanes(j)
        col, _, grow, _ = _head_vectors(cum_ref, cumt_ref, j)
        q = q_ref[:, cols]
        attended = intra_ref[:, cols] + grow * _nn(q, st_ref[j])
        width = attended.shape[-1]
        root_mean = jnp.sqrt(jnp.sum(attended * attended, axis=-1, keepdims=True) / width + epsilon)
        normed = attended / root_mean
        grad_f = g_ref[:, cols].astype(jnp.float32)
        scaled = gain_ref[j] * grad_f
        projected = jnp.sum(scaled * attended, axis=-1, keepdims=True)
        out_grad = ((scaled - attended * projected / (width * root_mean * root_mean)) / root_mean).astype(
            jnp.bfloat16
        )
        og_ref[:, cols] = out_grad
        q_scaled = (q.astype(jnp.float32) * grow).astype(jnp.bfloat16)
        m_ref[j, :DH, :] = _tn(q_scaled, out_grad)
        m_ref[j, DH:, :] = _pad_rows(col[col.shape[0] - 1 :, :], jnp.sum(grad_f * normed, axis=0, keepdims=True))


def grads_kernel(first, hb, q_ref, k_ref, v_ref, og_ref, cum_ref, cumt_ref, st_ref, qg_ref, kg_ref, vg_ref):
    for j in range(hb):
        cols = _lanes(j)
        col, row, grow, _ = _head_vectors(cum_ref, cumt_ref, j, first, hb)
        tiles, size = _tile_decays(col, row)
        q, k, v, og = q_ref[:, cols], k_ref[:, cols], v_ref[:, cols], og_ref[:, cols]
        part = lambda x, i: x[i * size : (i + 1) * size]
        qg = [None, None]
        kg = [None, None]
        vg = [None, None]

        def add(acc, i, value):
            acc[i] = value if acc[i] is None else acc[i] + value

        for a in range(2):
            for b in range(a + 1):
                masked = _masked(part(q, a), part(k, b), tiles[a, b])
                rgrad = (_nt(part(og, a), part(v, b)) * tiles[a, b]).astype(jnp.bfloat16)
                add(qg, a, _nn(rgrad, part(k, b)))
                add(kg, b, _tn(rgrad, part(q, a)))
                add(vg, b, _tn(masked, part(og, a)))
        state_part = grow * _nt(og, st_ref[j])
        for a in range(2):
            rows = slice(a * size, (a + 1) * size)
            qg_ref[rows, cols] = (qg[a] + state_part[rows]).astype(jnp.bfloat16)
            kg_ref[rows, cols] = kg[a]
            vg_ref[rows, cols] = vg[a]


def finish_kernel(k_ref, v_ref, kg_ref, vg_ref, gl_ref, cum_ref, cumt_ref, ko_ref, vo_ref):
    for j in range(HB):
        cols = _lanes(j)
        _, _, _, toend = _head_vectors(cum_ref, cumt_ref, j)
        grad_low = gl_ref[j]
        ko_ref[:, cols] = (kg_ref[:, cols] + toend * _nt(v_ref[:, cols], grad_low)).astype(jnp.bfloat16)
        vo_ref[:, cols] = (vg_ref[:, cols] + toend * _nn(k_ref[:, cols], grad_low)).astype(jnp.bfloat16)


def _per_head(kernel, ins, outs, heads, length, flops, nbytes, exps=0, part=None, into=None):
    hb = HB if part is None else HB // PIECE_STEPS
    groups = heads // hb
    first, count = (0, groups) if part is None else (part * PIECE_STEPS, PIECE_STEPS)
    if part is not None:
        kernel = functools.partial(kernel, first, hb)

    def spec(kind):
        if kind == "rows":
            return pl.BlockSpec((length, hb * DH), lambda i: (0, i + first))
        if kind == "cum":
            return pl.BlockSpec((length, heads), lambda i: (0, 0))
        if kind == "cumt":
            return pl.BlockSpec((heads, length), lambda i: (0, 0))
        if kind == "gain":
            return pl.BlockSpec((hb, 1, DH), lambda i: (i + first, 0, 0))
        if kind == "message":
            return pl.BlockSpec((hb, DH + PAD, DH), lambda i: (i + first, 0, 0))
        return pl.BlockSpec((hb, DH, DH), lambda i: (i + first, 0, 0))

    shapes = {
        "rows": (length, heads * DH),
        "gain": (heads, 1, DH),
        "square": (heads, DH, DH),
        "message": (heads, DH + PAD, DH),
    }
    out_shape = [jax.ShapeDtypeStruct(shapes[kind], dtype) for kind, dtype in outs]
    in_specs = [spec(kind) for kind, _ in ins]
    operands = [x for _, x in ins]
    aliases = {}
    body = kernel
    if into is not None:
        given = len(ins)
        in_specs += [pl.BlockSpec(memory_space=pl.ANY) for _ in into]
        operands += list(into)
        aliases = {given + i: i for i in range(len(into))}

        def body(*refs):
            kernel(*refs[:given], *refs[given + len(into) :])

    share = count / groups
    return pl.pallas_call(
        body,
        grid=(count,),
        in_specs=in_specs,
        out_specs=[spec(kind) for kind, _ in outs],
        out_shape=out_shape,
        input_output_aliases=aliases,
        cost_estimate=pl.CostEstimate(
            flops=int(flops * share), transcendentals=int(exps * share), bytes_accessed=int(nbytes * share)
        ),
    )(*operands)


def on_device(query_rows, key_rows, value_rows, cotangent, log_decay, norm_gain):
    length = query_rows.shape[0]
    heads = log_decay.shape[1]
    f32 = jnp.float32
    bf16 = jnp.bfloat16
    t = lax.broadcasted_iota(jnp.int32, (length, length), 0)
    s = lax.broadcasted_iota(jnp.int32, (length, length), 1)
    lower = (t >= s).astype(f32)
    exact = lax.Precision.HIGHEST
    cum = jnp.dot(lower, log_decay, precision=exact)
    cum_t = lax.dot_general(log_decay, lower, (((0,), (1,)), ((), ())), precision=exact)
    final_log = cum[-1]
    gain_rows = norm_gain.reshape(heads, 1, DH)
    q, k, v, g = query_rows, key_rows, value_rows, cotangent
    big = length * length * DH * 2 * heads
    small = length * DH * DH * 2 * heads
    rows_bytes = length * heads * DH * 2
    (local_state,) = _per_head(
        local_state_kernel,
        [("rows", k), ("rows", v), ("cum", cum), ("cumt", cum_t)],
        [("message", f32)],
        heads, length, small, 2 * rows_bytes,
    )
    def intra_piece(part, done, anchor):
        q_tied, _ = lax.optimization_barrier((q, anchor))
        return _per_head(
            intra_kernel,
            [("rows", q_tied), ("rows", k), ("rows", v), ("cum", cum), ("cumt", cum_t)],
            [("rows", f32)],
            heads, length, 2 * big, 5 * rows_bytes, heads * length * length, part=part, into=done,
        )

    groups = heads // HB
    state_in, (intra,) = forward_states(
        local_state, final_log, [functools.partial(intra_piece, p) for p in range(groups)]
    )
    state_low = state_in.astype(bf16)
    out_grad, moment = _per_head(
        norm_kernel,
        [("rows", q), ("rows", g), ("rows", intra), ("square", state_low), ("cum", cum), ("cumt", cum_t), ("gain", gain_rows)],
        [("rows", bf16), ("message", f32)],
        heads, length, 2 * small, 5 * rows_bytes,
    )
    def grads_piece(part, done, anchor):
        og_tied, _ = lax.optimization_barrier((out_grad, anchor))
        return _per_head(
            grads_kernel,
            [("rows", q), ("rows", k), ("rows", v), ("rows", og_tied), ("cum", cum), ("cumt", cum_t),
             ("square", state_low)],
            [("rows", bf16), ("rows", f32), ("rows", f32)],
            heads, length, 5 * big + small, 9 * rows_bytes, heads * length * length, part=part, into=done,
        )

    grad_state, gain_sum, (query_grad, key_part, value_part) = backward_states(
        moment, final_log, [functools.partial(grads_piece, p) for p in range(groups)]
    )
    grad_low = grad_state.astype(bf16)
    key_grad, value_grad = _per_head(
        finish_kernel,
        [("rows", k), ("rows", v), ("rows", key_part), ("rows", value_part), ("square", grad_low),
         ("cum", cum), ("cumt", cum_t)],
        [("rows", bf16), ("rows", bf16)],
        heads, length, 2 * small, 8 * rows_bytes,
    )
    seq_total = length * lax.axis_size(("ctx", "dp"))
    gain_grad = gain_sum * (1.0 / math.sqrt(seq_total))
    return (query_grad, key_grad, value_grad, gain_grad)


def solution(mesh):
    return jax.shard_map(
        on_device,
        mesh=mesh,
        in_specs=(
            P(("groups", "ctx", "dp"), "head"),
            P(("groups", "ctx", "dp"), "head"),
            P(("groups", "ctx", "dp"), "head"),
            P(("groups", "ctx", "dp"), "head"),
            P(("groups", "ctx", "dp"), "head"),
            P("head"),
        ),
        out_specs=(
            P(("groups", "ctx", "dp"), "head"),
            P(("groups", "ctx", "dp"), "head"),
            P(("groups", "ctx", "dp"), "head"),
            P(("groups", "head")),
        ),
        check_vma=False,
    )
```

```python
import functools
import math

import jax
import jax.numpy as jnp
from jax import lax
from jax.experimental import pallas as pl
from jax.sharding import PartitionSpec as P

DH = 128
PAD = 8
CHUNKS = 2
HB = 4
PIECE_STEPS = 2


epsilon = 1e-06


def swap_dp(x):
    return lax.ppermute(x, "dp", perm=[(0, 1), (1, 0)])


def pack_rows(core, *rows):
    heads = core.shape[0]
    pad = [jnp.broadcast_to(r.reshape(heads, 1, -1), (heads, 1, DH)) for r in rows]
    fill = jnp.zeros((heads, PAD - len(rows), DH), jnp.float32)
    return jnp.concatenate([core] + pad + [fill], axis=1)


def halves(x, c):
    half = x.shape[0] // 2
    return lax.dynamic_slice_in_dim(x, c * half, half, axis=0)


def join_halves(mine, other, c):
    first = jnp.where(c == 0, mine, other)
    second = jnp.where(c == 0, other, mine)
    return jnp.concatenate([first, second], axis=0)


def chain_scan(chip_state, chip_decay, later, pieces_of_cover, cover=None):
    chips = lax.axis_size("ctx")
    z = lax.axis_index("ctx")
    heads = chip_state.shape[0]
    count = min(CHUNKS, heads)
    size = heads // count
    pieces = chip_state.reshape(count, size, DH, DH)
    factor = jnp.exp(chip_decay).reshape(count, size, 1, 1)
    rank = (chips - 1 - z) if later else z
    if later:
        perm = [(i, i - 1) for i in range(1, chips)]
    else:
        perm = [(i, i + 1) for i in range(chips - 1)]
    prefix = jnp.zeros_like(pieces)
    steps = count + chips - 2
    for step in range(steps):
        send = jnp.clip(step - rank, 0, count - 1)
        outgoing = factor[send] * prefix[send] + pieces[send]
        if step < len(pieces_of_cover):
            cover = pieces_of_cover[step](cover, outgoing)
        arrived = lax.ppermute(outgoing, "ctx", perm=perm)
        where_to = step - rank + 1
        valid = (where_to >= 0) & (where_to < count) & (rank >= 1)
        slot = jnp.clip(where_to, 0, count - 1)
        prefix = prefix.at[slot].set(jnp.where(valid, arrived, prefix[slot]))
        if step < len(pieces_of_cover):
            cover, prefix = lax.optimization_barrier((cover, prefix))
    for piece in pieces_of_cover[steps:]:
        cover = piece(cover, prefix)
    return prefix.reshape(heads, DH, DH), cover


def forward_states(message, final_log, cover):
    c = lax.axis_index("dp")
    local_state = message[:, :DH, :]
    other = swap_dp(message)
    own_state, other_state = local_state, other[:, :DH, :]
    own_fin, other_fin = final_log, other[:, DH, 0]
    first = jnp.where(c == 0, own_state, other_state)
    second = jnp.where(c == 0, other_state, own_state)
    fin_first = jnp.where(c == 0, own_fin, other_fin)
    fin_second = jnp.where(c == 0, other_fin, own_fin)
    chip_state = jnp.exp(fin_second)[:, None, None] * first + second
    chip_decay = fin_first + fin_second
    prefix_half, cover = chain_scan(halves(chip_state, c), halves(chip_decay, c), False, cover)
    prefix = join_halves(prefix_half, swap_dp(prefix_half), c)
    core_one = jnp.exp(fin_first)[:, None, None] * prefix + first
    return jnp.where(c == 0, prefix, core_one), cover


def backward_states(message, final_log, cover):
    c = lax.axis_index("dp")
    heads = message.shape[0]
    moment = message[:, :DH, :]
    gain_rows = message[:, DH + 1, :]
    other = swap_dp(message)
    own_m, other_m = moment, other[:, :DH, :]
    own_fin, other_fin = final_log, other[:, DH, 0]
    first = jnp.where(c == 0, own_m, other_m)
    second = jnp.where(c == 0, other_m, own_m)
    fin_first = jnp.where(c == 0, own_fin, other_fin)
    fin_second = jnp.where(c == 0, other_fin, own_fin)
    chip_gain = gain_rows + other[:, DH + 1, :]
    chip_state = first + jnp.exp(fin_first)[:, None, None] * second
    chip_decay = fin_first + fin_second
    chips = lax.axis_size("ctx")

    def grads_step(piece, both, anchor):
        return piece(both[0], anchor), both[1]

    def both_steps(first, second, both, anchor):
        return second(first(both, anchor), anchor)

    def gain_step(distance, both, anchor):
        partners = [(i, i ^ distance) for i in range(chips)]
        return both[0], both[1] + lax.ppermute(both[1], "ctx", perm=partners)

    rounds = []
    distance = 1
    while distance < chips:
        rounds.append(functools.partial(gain_step, distance))
        distance *= 2
    steps = [functools.partial(grads_step, piece) for piece in cover]
    for index, gain_round in enumerate(rounds):
        if index < len(steps):
            steps[index] = functools.partial(both_steps, steps[index], gain_round)
        else:
            steps.append(gain_round)
    suffix_half, (cover, gain_total) = chain_scan(
        halves(chip_state, c), halves(chip_decay, c), True, steps, (None, chip_gain)
    )
    suffix = join_halves(suffix_half, swap_dp(suffix_half), c)
    core_zero = second + jnp.exp(fin_second)[:, None, None] * suffix
    return jnp.where(c == 0, core_zero, suffix), gain_total.reshape(heads * DH), cover


def _dot(a, b, contract):
    return lax.dot_general(a, b, (contract, ((), ())), preferred_element_type=jnp.float32)


def _nn(a, b):
    return _dot(a, b, ((1,), (0,)))


def _nt(a, b):
    return _dot(a, b, ((1,), (1,)))


def _tn(a, b):
    return _dot(a, b, ((0,), (0,)))


def _decay(cum_col, cum_row):
    length = cum_col.shape[0]
    t = lax.broadcasted_iota(jnp.int32, (length, length), 0)
    s = lax.broadcasted_iota(jnp.int32, (length, length), 1)
    causal = t >= s
    spread = cum_col - cum_row
    return jnp.where(causal, jnp.exp(jnp.where(causal, spread, 0.0)), 0.0)


def _masked(q, k, decay):
    return (_nt(q, k) * decay).astype(jnp.bfloat16)


def _head_vectors(cum_ref, cumt_ref, j, first=0, hb=None):
    h = (pl.program_id(0) + first) * (HB if hb is None else hb) + j
    full = cum_ref[...]
    lane = lax.broadcasted_iota(jnp.int32, full.shape, 1)
    col = jnp.sum(jnp.where(lane == h, full, 0.0), axis=1, keepdims=True)
    row = cumt_ref[pl.ds(h, 1), :]
    fin = col[col.shape[0] - 1 :, :]
    return col, row, jnp.exp(col), jnp.exp(fin - col)


def _lanes(j):
    return slice(j * DH, (j + 1) * DH)


def _pad_rows(*rows):
    slot = lax.broadcasted_iota(jnp.int32, (PAD, DH), 0)
    block = jnp.zeros((PAD, DH), jnp.float32)
    for index, value in enumerate(rows):
        block = jnp.where(slot == index, jnp.broadcast_to(value, (PAD, DH)), block)
    return block


def local_state_kernel(hb, k_ref, v_ref, cum_ref, cumt_ref, s_ref):
    for j in range(hb):
        cols = _lanes(j)
        col, _, _, toend = _head_vectors(cum_ref, cumt_ref, j, 0, hb)
        scaled = (k_ref[:, cols].astype(jnp.float32) * toend).astype(jnp.bfloat16)
        s_ref[j, :DH, :] = _tn(scaled, v_ref[:, cols])
        s_ref[j, DH:, :] = _pad_rows(col[col.shape[0] - 1 :, :])


def _tile_decays(col, row):
    size = col.shape[0] // 2
    tiles = {}
    for i in range(2):
        for j in range(i + 1):
            c = col[i * size : (i + 1) * size]
            r = row[:, j * size : (j + 1) * size]
            tiles[i, j] = _decay(c, r) if i == j else jnp.exp(c - r)
    return tiles, size


def intra_kernel(first, hb, q_ref, k_ref, v_ref, cum_ref, cumt_ref, out_ref):
    for j in range(hb):
        cols = _lanes(j)
        col, row, _, _ = _head_vectors(cum_ref, cumt_ref, j, first, hb)
        tiles, size = _tile_decays(col, row)
        q, k, v = q_ref[:, cols], k_ref[:, cols], v_ref[:, cols]
        for a in range(2):
            qa = q[a * size : (a + 1) * size]
            total = None
            for b in range(a + 1):
                part = _nn(_masked(qa, k[b * size : (b + 1) * size], tiles[a, b]), v[b * size : (b + 1) * size])
                total = part if total is None else total + part
            out_ref[a * size : (a + 1) * size, cols] = total


def norm_kernel(q_ref, g_ref, intra_ref, st_ref, cum_ref, cumt_ref, gain_ref, og_ref, m_ref):
    for j in range(HB):
        cols = _lanes(j)
        col, _, grow, _ = _head_vectors(cum_ref, cumt_ref, j)
        q = q_ref[:, cols]
        attended = intra_ref[:, cols] + grow * _nn(q, st_ref[j])
        width = attended.shape[-1]
        root_mean = jnp.sqrt(jnp.sum(attended * attended, axis=-1, keepdims=True) / width + epsilon)
        normed = attended / root_mean
        grad_f = g_ref[:, cols].astype(jnp.float32)
        scaled = gain_ref[j] * grad_f
        projected = jnp.sum(scaled * attended, axis=-1, keepdims=True)
        out_grad = ((scaled - attended * projected / (width * root_mean * root_mean)) / root_mean).astype(
            jnp.bfloat16
        )
        og_ref[:, cols] = out_grad
        q_scaled = (q.astype(jnp.float32) * grow).astype(jnp.bfloat16)
        m_ref[j, :DH, :] = _tn(q_scaled, out_grad)
        m_ref[j, DH:, :] = _pad_rows(col[col.shape[0] - 1 :, :], jnp.sum(grad_f * normed, axis=0, keepdims=True))


def grads_kernel(first, hb, q_ref, k_ref, v_ref, og_ref, cum_ref, cumt_ref, st_ref, qg_ref, kg_ref, vg_ref):
    for j in range(hb):
        cols = _lanes(j)
        col, row, grow, _ = _head_vectors(cum_ref, cumt_ref, j, first, hb)
        tiles, size = _tile_decays(col, row)
        q, k, v, og = q_ref[:, cols], k_ref[:, cols], v_ref[:, cols], og_ref[:, cols]
        part = lambda x, i: x[i * size : (i + 1) * size]
        qg = [None, None]
        kg = [None, None]
        vg = [None, None]

        def add(acc, i, value):
            acc[i] = value if acc[i] is None else acc[i] + value

        for a in range(2):
            for b in range(a + 1):
                masked = _masked(part(q, a), part(k, b), tiles[a, b])
                rgrad = (_nt(part(og, a), part(v, b)) * tiles[a, b]).astype(jnp.bfloat16)
                add(qg, a, _nn(rgrad, part(k, b)))
                add(kg, b, _tn(rgrad, part(q, a)))
                add(vg, b, _tn(masked, part(og, a)))
        state_part = grow * _nt(og, st_ref[j])
        for a in range(2):
            rows = slice(a * size, (a + 1) * size)
            qg_ref[rows, cols] = (qg[a] + state_part[rows]).astype(jnp.bfloat16)
            kg_ref[rows, cols] = kg[a]
            vg_ref[rows, cols] = vg[a]


def finish_kernel(k_ref, v_ref, kg_ref, vg_ref, gl_ref, cum_ref, cumt_ref, ko_ref, vo_ref):
    for j in range(HB):
        cols = _lanes(j)
        _, _, _, toend = _head_vectors(cum_ref, cumt_ref, j)
        grad_low = gl_ref[j]
        ko_ref[:, cols] = (kg_ref[:, cols] + toend * _nt(v_ref[:, cols], grad_low)).astype(jnp.bfloat16)
        vo_ref[:, cols] = (vg_ref[:, cols] + toend * _nn(k_ref[:, cols], grad_low)).astype(jnp.bfloat16)


def _per_head(kernel, ins, outs, heads, length, flops, nbytes, exps=0, part=None, into=None, wide=False):
    hb = HB if part is None else HB // PIECE_STEPS
    if wide:
        hb = min(2 * HB, heads)
        kernel = functools.partial(kernel, hb)
    groups = heads // hb
    first, count = (0, groups) if part is None else (part * PIECE_STEPS, PIECE_STEPS)
    if part is not None:
        kernel = functools.partial(kernel, first, hb)

    def spec(kind):
        if kind == "rows":
            return pl.BlockSpec((length, hb * DH), lambda i: (0, i + first))
        if kind == "cum":
            return pl.BlockSpec((length, heads), lambda i: (0, 0))
        if kind == "cumt":
            return pl.BlockSpec((heads, length), lambda i: (0, 0))
        if kind == "gain":
            return pl.BlockSpec((hb, 1, DH), lambda i: (i + first, 0, 0))
        if kind == "message":
            return pl.BlockSpec((hb, DH + PAD, DH), lambda i: (i + first, 0, 0))
        return pl.BlockSpec((hb, DH, DH), lambda i: (i + first, 0, 0))

    shapes = {
        "rows": (length, heads * DH),
        "gain": (heads, 1, DH),
        "square": (heads, DH, DH),
        "message": (heads, DH + PAD, DH),
    }
    out_shape = [jax.ShapeDtypeStruct(shapes[kind], dtype) for kind, dtype in outs]
    in_specs = [spec(kind) for kind, _ in ins]
    operands = [x for _, x in ins]
    aliases = {}
    body = kernel
    if into is not None:
        given = len(ins)
        in_specs += [pl.BlockSpec(memory_space=pl.ANY) for _ in into]
        operands += list(into)
        aliases = {given + i: i for i in range(len(into))}

        def body(*refs):
            kernel(*refs[:given], *refs[given + len(into) :])

    share = count / groups
    return pl.pallas_call(
        body,
        grid=(count,),
        in_specs=in_specs,
        out_specs=[spec(kind) for kind, _ in outs],
        out_shape=out_shape,
        input_output_aliases=aliases,
        cost_estimate=pl.CostEstimate(
            flops=int(flops * share), transcendentals=int(exps * share), bytes_accessed=int(nbytes * share)
        ),
    )(*operands)


def on_device(query_rows, key_rows, value_rows, cotangent, log_decay, norm_gain):
    length = query_rows.shape[0]
    heads = log_decay.shape[1]
    f32 = jnp.float32
    bf16 = jnp.bfloat16
    t = lax.broadcasted_iota(jnp.int32, (length, length), 0)
    s = lax.broadcasted_iota(jnp.int32, (length, length), 1)
    lower = (t >= s).astype(f32)
    exact = lax.Precision.HIGHEST
    cum = jnp.dot(lower, log_decay, precision=exact)
    cum_t = lax.dot_general(log_decay, lower, (((0,), (1,)), ((), ())), precision=exact)
    final_log = cum[-1]
    gain_rows = norm_gain.reshape(heads, 1, DH)
    q, k, v, g = query_rows, key_rows, value_rows, cotangent
    big = length * length * DH * 2 * heads
    small = length * DH * DH * 2 * heads
    rows_bytes = length * heads * DH * 2
    (local_state,) = _per_head(
        local_state_kernel,
        [("rows", k), ("rows", v), ("cum", cum), ("cumt", cum_t)],
        [("message", f32)],
        heads, length, small, 2 * rows_bytes, wide=True,
    )
    def intra_piece(part, done, anchor):
        q_tied, _ = lax.optimization_barrier((q, anchor))
        return _per_head(
            intra_kernel,
            [("rows", q_tied), ("rows", k), ("rows", v), ("cum", cum), ("cumt", cum_t)],
            [("rows", f32)],
            heads, length, 2 * big, 5 * rows_bytes, heads * length * length, part=part, into=done,
        )

    groups = heads // HB
    state_in, (intra,) = forward_states(
        local_state, final_log, [functools.partial(intra_piece, p) for p in range(groups)]
    )
    state_low = state_in.astype(bf16)
    out_grad, moment = _per_head(
        norm_kernel,
        [("rows", q), ("rows", g), ("rows", intra), ("square", state_low), ("cum", cum), ("cumt", cum_t), ("gain", gain_rows)],
        [("rows", bf16), ("message", f32)],
        heads, length, 2 * small, 5 * rows_bytes,
    )
    def grads_piece(part, done, anchor):
        og_tied, _ = lax.optimization_barrier((out_grad, anchor))
        return _per_head(
            grads_kernel,
            [("rows", q), ("rows", k), ("rows", v), ("rows", og_tied), ("cum", cum), ("cumt", cum_t),
             ("square", state_low)],
            [("rows", bf16), ("rows", f32), ("rows", f32)],
            heads, length, 5 * big + small, 9 * rows_bytes, heads * length * length, part=part, into=done,
        )

    grad_state, gain_sum, (query_grad, key_part, value_part) = backward_states(
        moment, final_log, [functools.partial(grads_piece, p) for p in range(groups)]
    )
    grad_low = grad_state.astype(bf16)
    key_grad, value_grad = _per_head(
        finish_kernel,
        [("rows", k), ("rows", v), ("rows", key_part), ("rows", value_part), ("square", grad_low),
         ("cum", cum), ("cumt", cum_t)],
        [("rows", bf16), ("rows", bf16)],
        heads, length, 2 * small, 8 * rows_bytes,
    )
    seq_total = length * lax.axis_size(("ctx", "dp"))
    gain_grad = gain_sum * (1.0 / math.sqrt(seq_total))
    return (query_grad, key_grad, value_grad, gain_grad)


def solution(mesh):
    return jax.shard_map(
        on_device,
        mesh=mesh,
        in_specs=(
            P(("groups", "ctx", "dp"), "head"),
            P(("groups", "ctx", "dp"), "head"),
            P(("groups", "ctx", "dp"), "head"),
            P(("groups", "ctx", "dp"), "head"),
            P(("groups", "ctx", "dp"), "head"),
            P("head"),
        ),
        out_specs=(
            P(("groups", "ctx", "dp"), "head"),
            P(("groups", "ctx", "dp"), "head"),
            P(("groups", "ctx", "dp"), "head"),
            P(("groups", "head")),
        ),
        check_vma=False,
    )
```

```python
import functools
import math

import jax
import jax.numpy as jnp
from jax import lax
from jax.experimental import pallas as pl
from jax.sharding import PartitionSpec as P

DH = 128
PAD = 8
CHUNKS = 2
HB = 4
PIECE_STEPS = 2


epsilon = 1e-06


def swap_dp(x):
    return lax.ppermute(x, "dp", perm=[(0, 1), (1, 0)])


def pack_rows(core, *rows):
    heads = core.shape[0]
    pad = [jnp.broadcast_to(r.reshape(heads, 1, -1), (heads, 1, DH)) for r in rows]
    fill = jnp.zeros((heads, PAD - len(rows), DH), jnp.float32)
    return jnp.concatenate([core] + pad + [fill], axis=1)


def halves(x, c):
    half = x.shape[0] // 2
    return lax.dynamic_slice_in_dim(x, c * half, half, axis=0)


def join_halves(mine, other, c):
    first = jnp.where(c == 0, mine, other)
    second = jnp.where(c == 0, other, mine)
    return jnp.concatenate([first, second], axis=0)


def chain_scan(chip_state, chip_decay, later, pieces_of_cover, cover=None):
    chips = lax.axis_size("ctx")
    z = lax.axis_index("ctx")
    heads = chip_state.shape[0]
    count = min(CHUNKS, heads)
    size = heads // count
    pieces = chip_state.reshape(count, size, DH, DH)
    factor = jnp.exp(chip_decay).reshape(count, size, 1, 1)
    rank = (chips - 1 - z) if later else z
    if later:
        perm = [(i, i - 1) for i in range(1, chips)]
    else:
        perm = [(i, i + 1) for i in range(chips - 1)]
    prefix = jnp.zeros_like(pieces)
    steps = count + chips - 2
    for step in range(steps):
        send = jnp.clip(step - rank, 0, count - 1)
        outgoing = factor[send] * prefix[send] + pieces[send]
        if step < len(pieces_of_cover):
            cover = pieces_of_cover[step](cover, outgoing)
        arrived = lax.ppermute(outgoing, "ctx", perm=perm)
        where_to = step - rank + 1
        valid = (where_to >= 0) & (where_to < count) & (rank >= 1)
        slot = jnp.clip(where_to, 0, count - 1)
        prefix = prefix.at[slot].set(jnp.where(valid, arrived, prefix[slot]))
        if step < len(pieces_of_cover):
            cover, prefix = lax.optimization_barrier((cover, prefix))
    for piece in pieces_of_cover[steps:]:
        cover = piece(cover, prefix)
    return prefix.reshape(heads, DH, DH), cover


def forward_states(message, final_log, cover):
    c = lax.axis_index("dp")
    local_state = message[:, :DH, :]
    other = swap_dp(message)
    own_state, other_state = local_state, other[:, :DH, :]
    own_fin, other_fin = final_log, other[:, DH, 0]
    first = jnp.where(c == 0, own_state, other_state)
    second = jnp.where(c == 0, other_state, own_state)
    fin_first = jnp.where(c == 0, own_fin, other_fin)
    fin_second = jnp.where(c == 0, other_fin, own_fin)
    chip_half = jnp.exp(halves(fin_second, c))[:, None, None] * halves(first, c) + halves(second, c)
    decay_half = halves(fin_first, c) + halves(fin_second, c)
    prefix_half, cover = chain_scan(chip_half, decay_half, False, cover)
    prefix = join_halves(prefix_half, swap_dp(prefix_half), c)
    core_one = jnp.exp(fin_first)[:, None, None] * prefix + first
    return jnp.where(c == 0, prefix, core_one), cover


def backward_states(message, final_log, cover):
    c = lax.axis_index("dp")
    heads = message.shape[0]
    moment = message[:, :DH, :]
    gain_rows = message[:, DH + 1, :]
    other = swap_dp(message)
    own_m, other_m = moment, other[:, :DH, :]
    own_fin, other_fin = final_log, other[:, DH, 0]
    first = jnp.where(c == 0, own_m, other_m)
    second = jnp.where(c == 0, other_m, own_m)
    fin_first = jnp.where(c == 0, own_fin, other_fin)
    fin_second = jnp.where(c == 0, other_fin, own_fin)
    chip_gain = gain_rows + other[:, DH + 1, :]
    chip_half = halves(first, c) + jnp.exp(halves(fin_first, c))[:, None, None] * halves(second, c)
    decay_half = halves(fin_first, c) + halves(fin_second, c)
    chips = lax.axis_size("ctx")

    def grads_step(piece, both, anchor):
        return piece(both[0], anchor), both[1]

    def both_steps(first, second, both, anchor):
        return second(first(both, anchor), anchor)

    def gain_step(distance, both, anchor):
        partners = [(i, i ^ distance) for i in range(chips)]
        return both[0], both[1] + lax.ppermute(both[1], "ctx", perm=partners)

    rounds = []
    distance = 1
    while distance < chips:
        rounds.append(functools.partial(gain_step, distance))
        distance *= 2
    steps = [functools.partial(grads_step, piece) for piece in cover]
    for index, gain_round in enumerate(rounds):
        if index < len(steps):
            steps[index] = functools.partial(both_steps, steps[index], gain_round)
        else:
            steps.append(gain_round)
    suffix_half, (cover, gain_total) = chain_scan(
        chip_half, decay_half, True, steps, (None, chip_gain)
    )
    suffix = join_halves(suffix_half, swap_dp(suffix_half), c)
    core_zero = second + jnp.exp(fin_second)[:, None, None] * suffix
    return jnp.where(c == 0, core_zero, suffix), gain_total.reshape(heads * DH), cover


def _dot(a, b, contract):
    return lax.dot_general(a, b, (contract, ((), ())), preferred_element_type=jnp.float32)


def _nn(a, b):
    return _dot(a, b, ((1,), (0,)))


def _nt(a, b):
    return _dot(a, b, ((1,), (1,)))


def _tn(a, b):
    return _dot(a, b, ((0,), (0,)))


def _decay(cum_col, cum_row):
    length = cum_col.shape[0]
    t = lax.broadcasted_iota(jnp.int32, (length, length), 0)
    s = lax.broadcasted_iota(jnp.int32, (length, length), 1)
    causal = t >= s
    spread = cum_col - cum_row
    return jnp.where(causal, jnp.exp(jnp.where(causal, spread, 0.0)), 0.0)


def _masked(q, k, decay):
    return (_nt(q, k) * decay).astype(jnp.bfloat16)


def _head_vectors(cum_ref, cumt_ref, j, first=0, hb=None):
    h = (pl.program_id(0) + first) * (HB if hb is None else hb) + j
    full = cum_ref[...]
    lane = lax.broadcasted_iota(jnp.int32, full.shape, 1)
    col = jnp.sum(jnp.where(lane == h, full, 0.0), axis=1, keepdims=True)
    row = cumt_ref[pl.ds(h, 1), :]
    fin = col[col.shape[0] - 1 :, :]
    return col, row, jnp.exp(col), jnp.exp(fin - col)


def _lanes(j):
    return slice(j * DH, (j + 1) * DH)


def _pad_rows(*rows):
    slot = lax.broadcasted_iota(jnp.int32, (PAD, DH), 0)
    block = jnp.zeros((PAD, DH), jnp.float32)
    for index, value in enumerate(rows):
        block = jnp.where(slot == index, jnp.broadcast_to(value, (PAD, DH)), block)
    return block


def local_state_kernel(hb, k_ref, v_ref, cum_ref, cumt_ref, s_ref):
    for j in range(hb):
        cols = _lanes(j)
        col, _, _, toend = _head_vectors(cum_ref, cumt_ref, j, 0, hb)
        scaled = (k_ref[:, cols].astype(jnp.float32) * toend).astype(jnp.bfloat16)
        s_ref[j, :DH, :] = _tn(scaled, v_ref[:, cols])
        s_ref[j, DH:, :] = _pad_rows(col[col.shape[0] - 1 :, :])


def _tile_decays(col, row):
    size = col.shape[0] // 2
    tiles = {}
    for i in range(2):
        for j in range(i + 1):
            c = col[i * size : (i + 1) * size]
            r = row[:, j * size : (j + 1) * size]
            tiles[i, j] = _decay(c, r) if i == j else jnp.exp(c - r)
    return tiles, size


def intra_kernel(first, hb, q_ref, k_ref, v_ref, cum_ref, cumt_ref, out_ref):
    for j in range(hb):
        cols = _lanes(j)
        col, row, _, _ = _head_vectors(cum_ref, cumt_ref, j, first, hb)
        tiles, size = _tile_decays(col, row)
        q, k, v = q_ref[:, cols], k_ref[:, cols], v_ref[:, cols]
        for a in range(2):
            qa = q[a * size : (a + 1) * size]
            total = None
            for b in range(a + 1):
                part = _nn(_masked(qa, k[b * size : (b + 1) * size], tiles[a, b]), v[b * size : (b + 1) * size])
                total = part if total is None else total + part
            out_ref[a * size : (a + 1) * size, cols] = total


def norm_kernel(q_ref, g_ref, intra_ref, st_ref, cum_ref, cumt_ref, gain_ref, og_ref, m_ref):
    for j in range(HB):
        cols = _lanes(j)
        col, _, grow, _ = _head_vectors(cum_ref, cumt_ref, j)
        q = q_ref[:, cols]
        attended = intra_ref[:, cols] + grow * _nn(q, st_ref[j])
        width = attended.shape[-1]
        root_mean = jnp.sqrt(jnp.sum(attended * attended, axis=-1, keepdims=True) / width + epsilon)
        normed = attended / root_mean
        grad_f = g_ref[:, cols].astype(jnp.float32)
        scaled = gain_ref[j] * grad_f
        projected = jnp.sum(scaled * attended, axis=-1, keepdims=True)
        out_grad = ((scaled - attended * projected / (width * root_mean * root_mean)) / root_mean).astype(
            jnp.bfloat16
        )
        og_ref[:, cols] = out_grad
        q_scaled = (q.astype(jnp.float32) * grow).astype(jnp.bfloat16)
        m_ref[j, :DH, :] = _tn(q_scaled, out_grad)
        m_ref[j, DH:, :] = _pad_rows(col[col.shape[0] - 1 :, :], jnp.sum(grad_f * normed, axis=0, keepdims=True))


def grads_kernel(first, hb, q_ref, k_ref, v_ref, og_ref, cum_ref, cumt_ref, st_ref, qg_ref, kg_ref, vg_ref):
    for j in range(hb):
        cols = _lanes(j)
        col, row, grow, _ = _head_vectors(cum_ref, cumt_ref, j, first, hb)
        tiles, size = _tile_decays(col, row)
        q, k, v, og = q_ref[:, cols], k_ref[:, cols], v_ref[:, cols], og_ref[:, cols]
        part = lambda x, i: x[i * size : (i + 1) * size]
        qg = [None, None]
        kg = [None, None]
        vg = [None, None]

        def add(acc, i, value):
            acc[i] = value if acc[i] is None else acc[i] + value

        for a in range(2):
            for b in range(a + 1):
                masked = _masked(part(q, a), part(k, b), tiles[a, b])
                rgrad = (_nt(part(og, a), part(v, b)) * tiles[a, b]).astype(jnp.bfloat16)
                add(qg, a, _nn(rgrad, part(k, b)))
                add(kg, b, _tn(rgrad, part(q, a)))
                add(vg, b, _tn(masked, part(og, a)))
        state_part = grow * _nt(og, st_ref[j])
        for a in range(2):
            rows = slice(a * size, (a + 1) * size)
            qg_ref[rows, cols] = (qg[a] + state_part[rows]).astype(jnp.bfloat16)
            kg_ref[rows, cols] = kg[a]
            vg_ref[rows, cols] = vg[a]


def finish_kernel(k_ref, v_ref, kg_ref, vg_ref, gl_ref, cum_ref, cumt_ref, ko_ref, vo_ref):
    for j in range(HB):
        cols = _lanes(j)
        _, _, _, toend = _head_vectors(cum_ref, cumt_ref, j)
        grad_low = gl_ref[j]
        ko_ref[:, cols] = (kg_ref[:, cols] + toend * _nt(v_ref[:, cols], grad_low)).astype(jnp.bfloat16)
        vo_ref[:, cols] = (vg_ref[:, cols] + toend * _nn(k_ref[:, cols], grad_low)).astype(jnp.bfloat16)


def _per_head(kernel, ins, outs, heads, length, flops, nbytes, exps=0, part=None, into=None, wide=False):
    hb = HB if part is None else HB // PIECE_STEPS
    if wide:
        hb = min(2 * HB, heads)
        kernel = functools.partial(kernel, hb)
    groups = heads // hb
    first, count = (0, groups) if part is None else (part * PIECE_STEPS, PIECE_STEPS)
    if part is not None:
        kernel = functools.partial(kernel, first, hb)

    def spec(kind):
        if kind == "rows":
            return pl.BlockSpec((length, hb * DH), lambda i: (0, i + first))
        if kind == "cum":
            return pl.BlockSpec((length, heads), lambda i: (0, 0))
        if kind == "cumt":
            return pl.BlockSpec((heads, length), lambda i: (0, 0))
        if kind == "gain":
            return pl.BlockSpec((hb, 1, DH), lambda i: (i + first, 0, 0))
        if kind == "message":
            return pl.BlockSpec((hb, DH + PAD, DH), lambda i: (i + first, 0, 0))
        return pl.BlockSpec((hb, DH, DH), lambda i: (i + first, 0, 0))

    shapes = {
        "rows": (length, heads * DH),
        "gain": (heads, 1, DH),
        "square": (heads, DH, DH),
        "message": (heads, DH + PAD, DH),
    }
    out_shape = [jax.ShapeDtypeStruct(shapes[kind], dtype) for kind, dtype in outs]
    in_specs = [spec(kind) for kind, _ in ins]
    operands = [x for _, x in ins]
    aliases = {}
    body = kernel
    if into is not None:
        given = len(ins)
        in_specs += [pl.BlockSpec(memory_space=pl.ANY) for _ in into]
        operands += list(into)
        aliases = {given + i: i for i in range(len(into))}

        def body(*refs):
            kernel(*refs[:given], *refs[given + len(into) :])

    share = count / groups
    return pl.pallas_call(
        body,
        grid=(count,),
        in_specs=in_specs,
        out_specs=[spec(kind) for kind, _ in outs],
        out_shape=out_shape,
        input_output_aliases=aliases,
        cost_estimate=pl.CostEstimate(
            flops=int(flops * share), transcendentals=int(exps * share), bytes_accessed=int(nbytes * share)
        ),
    )(*operands)


def on_device(query_rows, key_rows, value_rows, cotangent, log_decay, norm_gain):
    length = query_rows.shape[0]
    heads = log_decay.shape[1]
    f32 = jnp.float32
    bf16 = jnp.bfloat16
    t = lax.broadcasted_iota(jnp.int32, (length, length), 0)
    s = lax.broadcasted_iota(jnp.int32, (length, length), 1)
    lower = (t >= s).astype(f32)
    exact = lax.Precision.HIGHEST
    cum = jnp.dot(lower, log_decay, precision=exact)
    cum_t = lax.dot_general(log_decay, lower, (((0,), (1,)), ((), ())), precision=exact)
    final_log = cum[-1]
    gain_rows = norm_gain.reshape(heads, 1, DH)
    q, k, v, g = query_rows, key_rows, value_rows, cotangent
    big = length * length * DH * 2 * heads
    small = length * DH * DH * 2 * heads
    rows_bytes = length * heads * DH * 2
    (local_state,) = _per_head(
        local_state_kernel,
        [("rows", k), ("rows", v), ("cum", cum), ("cumt", cum_t)],
        [("message", f32)],
        heads, length, small, 2 * rows_bytes, wide=True,
    )
    def intra_piece(part, done, anchor):
        q_tied, _ = lax.optimization_barrier((q, anchor))
        return _per_head(
            intra_kernel,
            [("rows", q_tied), ("rows", k), ("rows", v), ("cum", cum), ("cumt", cum_t)],
            [("rows", f32)],
            heads, length, 2 * big, 5 * rows_bytes, heads * length * length, part=part, into=done,
        )

    groups = heads // HB
    state_in, (intra,) = forward_states(
        local_state, final_log, [functools.partial(intra_piece, p) for p in range(groups)]
    )
    state_low = state_in.astype(bf16)
    out_grad, moment = _per_head(
        norm_kernel,
        [("rows", q), ("rows", g), ("rows", intra), ("square", state_low), ("cum", cum), ("cumt", cum_t), ("gain", gain_rows)],
        [("rows", bf16), ("message", f32)],
        heads, length, 2 * small, 5 * rows_bytes,
    )
    def grads_piece(part, done, anchor):
        og_tied, _ = lax.optimization_barrier((out_grad, anchor))
        return _per_head(
            grads_kernel,
            [("rows", q), ("rows", k), ("rows", v), ("rows", og_tied), ("cum", cum), ("cumt", cum_t),
             ("square", state_low)],
            [("rows", bf16), ("rows", f32), ("rows", f32)],
            heads, length, 5 * big + small, 9 * rows_bytes, heads * length * length, part=part, into=done,
        )

    grad_state, gain_sum, (query_grad, key_part, value_part) = backward_states(
        moment, final_log, [functools.partial(grads_piece, p) for p in range(groups)]
    )
    grad_low = grad_state.astype(bf16)
    key_grad, value_grad = _per_head(
        finish_kernel,
        [("rows", k), ("rows", v), ("rows", key_part), ("rows", value_part), ("square", grad_low),
         ("cum", cum), ("cumt", cum_t)],
        [("rows", bf16), ("rows", bf16)],
        heads, length, 2 * small, 8 * rows_bytes,
    )
    seq_total = length * lax.axis_size(("ctx", "dp"))
    gain_grad = gain_sum * (1.0 / math.sqrt(seq_total))
    return (query_grad, key_grad, value_grad, gain_grad)


def solution(mesh):
    return jax.shard_map(
        on_device,
        mesh=mesh,
        in_specs=(
            P(("groups", "ctx", "dp"), "head"),
            P(("groups", "ctx", "dp"), "head"),
            P(("groups", "ctx", "dp"), "head"),
            P(("groups", "ctx", "dp"), "head"),
            P(("groups", "ctx", "dp"), "head"),
            P("head"),
        ),
        out_specs=(
            P(("groups", "ctx", "dp"), "head"),
            P(("groups", "ctx", "dp"), "head"),
            P(("groups", "ctx", "dp"), "head"),
            P(("groups", "head")),
        ),
        check_vma=False,
    )
```

```python
import functools
import math

import jax
import jax.numpy as jnp
from jax import lax
from jax.experimental import pallas as pl
from jax.sharding import PartitionSpec as P

DH = 128
PAD = 8
CHUNKS = 2
HB = 4
PIECE_STEPS = 2


epsilon = 1e-06


def swap_dp(x):
    return lax.ppermute(x, "dp", perm=[(0, 1), (1, 0)])


def pack_rows(core, *rows):
    heads = core.shape[0]
    pad = [jnp.broadcast_to(r.reshape(heads, 1, -1), (heads, 1, DH)) for r in rows]
    fill = jnp.zeros((heads, PAD - len(rows), DH), jnp.float32)
    return jnp.concatenate([core] + pad + [fill], axis=1)


def halves(x, c):
    half = x.shape[0] // 2
    return lax.dynamic_slice_in_dim(x, c * half, half, axis=0)


def join_halves(mine, other, c):
    first = jnp.where(c == 0, mine, other)
    second = jnp.where(c == 0, other, mine)
    return jnp.concatenate([first, second], axis=0)


def chain_scan(chip_state, chip_decay, later, pieces_of_cover, cover=None):
    chips = lax.axis_size("ctx")
    z = lax.axis_index("ctx")
    heads = chip_state.shape[0]
    count = min(CHUNKS, heads)
    size = heads // count
    pieces = chip_state.reshape(count, size, DH, DH)
    factor = jnp.exp(chip_decay).reshape(count, size, 1, 1)
    rank = (chips - 1 - z) if later else z
    if later:
        perm = [(i, i - 1) for i in range(1, chips)]
    else:
        perm = [(i, i + 1) for i in range(chips - 1)]
    prefix = jnp.zeros_like(pieces)
    steps = count + chips - 2
    for step in range(steps):
        send = jnp.clip(step - rank, 0, count - 1)
        outgoing = factor[send] * prefix[send] + pieces[send]
        if step < len(pieces_of_cover):
            cover = pieces_of_cover[step](cover, outgoing)
        arrived = lax.ppermute(outgoing, "ctx", perm=perm)
        where_to = step - rank + 1
        valid = (where_to >= 0) & (where_to < count) & (rank >= 1)
        slot = jnp.clip(where_to, 0, count - 1)
        prefix = prefix.at[slot].set(jnp.where(valid, arrived, prefix[slot]))
        if step < len(pieces_of_cover):
            cover, prefix = lax.optimization_barrier((cover, prefix))
    for piece in pieces_of_cover[steps:]:
        cover = piece(cover, prefix)
    return prefix.reshape(heads, DH, DH), cover


def forward_states(message, final_log, cover):
    c = lax.axis_index("dp")
    local_state = message[:, :DH, :]
    other = swap_dp(message)
    own_state, other_state = local_state, other[:, :DH, :]
    own_fin, other_fin = final_log, other[:, DH, 0]
    first = jnp.where(c == 0, own_state, other_state)
    second = jnp.where(c == 0, other_state, own_state)
    fin_first = jnp.where(c == 0, own_fin, other_fin)
    fin_second = jnp.where(c == 0, other_fin, own_fin)
    chip_state = jnp.exp(fin_second)[:, None, None] * first + second
    chip_decay = fin_first + fin_second
    prefix_half, cover = chain_scan(halves(chip_state, c), halves(chip_decay, c), False, cover)
    prefix = join_halves(prefix_half, swap_dp(prefix_half), c)
    core_one = jnp.exp(fin_first)[:, None, None] * prefix + first
    return jnp.where(c == 0, prefix, core_one), cover


def backward_states(message, final_log, cover):
    c = lax.axis_index("dp")
    heads = message.shape[0]
    moment = message[:, :DH, :]
    gain_rows = message[:, DH + 1, :]
    other = swap_dp(message)
    own_m, other_m = moment, other[:, :DH, :]
    own_fin, other_fin = final_log, other[:, DH, 0]
    first = jnp.where(c == 0, own_m, other_m)
    second = jnp.where(c == 0, other_m, own_m)
    fin_first = jnp.where(c == 0, own_fin, other_fin)
    fin_second = jnp.where(c == 0, other_fin, own_fin)
    chip_gain = gain_rows + other[:, DH + 1, :]
    chip_state = first + jnp.exp(fin_first)[:, None, None] * second
    chip_decay = fin_first + fin_second
    chips = lax.axis_size("ctx")

    def grads_step(piece, both, anchor):
        return piece(both[0], anchor), both[1]

    def both_steps(first, second, both, anchor):
        return second(first(both, anchor), anchor)

    def gain_step(distance, both, anchor):
        partners = [(i, i ^ distance) for i in range(chips)]
        return both[0], both[1] + lax.ppermute(both[1], "ctx", perm=partners)

    rounds = []
    distance = 1
    while distance < chips:
        rounds.append(functools.partial(gain_step, distance))
        distance *= 2
    steps = [functools.partial(grads_step, piece) for piece in cover]
    for index, gain_round in enumerate(rounds):
        if index < len(steps):
            steps[index] = functools.partial(both_steps, steps[index], gain_round)
        else:
            steps.append(gain_round)
    suffix_half, (cover, gain_total) = chain_scan(
        halves(chip_state, c), halves(chip_decay, c), True, steps, (None, chip_gain)
    )
    suffix = join_halves(suffix_half, swap_dp(suffix_half), c)
    core_zero = second + jnp.exp(fin_second)[:, None, None] * suffix
    return jnp.where(c == 0, core_zero, suffix), gain_total.reshape(heads * DH), cover


def _dot(a, b, contract):
    return lax.dot_general(a, b, (contract, ((), ())), preferred_element_type=jnp.float32)


def _nn(a, b):
    return _dot(a, b, ((1,), (0,)))


def _nt(a, b):
    return _dot(a, b, ((1,), (1,)))


def _tn(a, b):
    return _dot(a, b, ((0,), (0,)))


def _decay(cum_col, cum_row):
    length = cum_col.shape[0]
    t = lax.broadcasted_iota(jnp.int32, (length, length), 0)
    s = lax.broadcasted_iota(jnp.int32, (length, length), 1)
    causal = t >= s
    spread = cum_col - cum_row
    return jnp.where(causal, jnp.exp(jnp.where(causal, spread, 0.0)), 0.0)


def _masked(q, k, decay):
    return (_nt(q, k) * decay).astype(jnp.bfloat16)


def _head_vectors(cum_ref, cumt_ref, j, first=0, hb=None):
    h = (pl.program_id(0) + first) * (HB if hb is None else hb) + j
    full = cum_ref[...]
    lane = lax.broadcasted_iota(jnp.int32, full.shape, 1)
    col = jnp.sum(jnp.where(lane == h, full, 0.0), axis=1, keepdims=True)
    row = cumt_ref[pl.ds(h, 1), :]
    fin = col[col.shape[0] - 1 :, :]
    return col, row, jnp.exp(col), jnp.exp(fin - col)


def _lanes(j):
    return slice(j * DH, (j + 1) * DH)


def _pad_rows(*rows):
    slot = lax.broadcasted_iota(jnp.int32, (PAD, DH), 0)
    block = jnp.zeros((PAD, DH), jnp.float32)
    for index, value in enumerate(rows):
        block = jnp.where(slot == index, jnp.broadcast_to(value, (PAD, DH)), block)
    return block


def local_state_kernel(hb, k_ref, v_ref, cum_ref, cumt_ref, s_ref):
    for j in range(hb):
        cols = _lanes(j)
        col, _, _, toend = _head_vectors(cum_ref, cumt_ref, j, 0, hb)
        scaled = (k_ref[:, cols].astype(jnp.float32) * toend).astype(jnp.bfloat16)
        s_ref[j, :DH, :] = _tn(scaled, v_ref[:, cols])
        s_ref[j, DH:, :] = _pad_rows(col[col.shape[0] - 1 :, :])


def _tile_decays(col, row):
    size = col.shape[0] // 2
    tiles = {}
    for i in range(2):
        for j in range(i + 1):
            c = col[i * size : (i + 1) * size]
            r = row[:, j * size : (j + 1) * size]
            tiles[i, j] = _decay(c, r) if i == j else jnp.exp(c - r)
    return tiles, size


def intra_kernel(first, hb, q_ref, k_ref, v_ref, cum_ref, cumt_ref, out_ref):
    for j in range(hb):
        cols = _lanes(j)
        col, row, _, _ = _head_vectors(cum_ref, cumt_ref, j, first, hb)
        tiles, size = _tile_decays(col, row)
        q, k, v = q_ref[:, cols], k_ref[:, cols], v_ref[:, cols]
        for a in range(2):
            qa = q[a * size : (a + 1) * size]
            total = None
            for b in range(a + 1):
                part = _nn(_masked(qa, k[b * size : (b + 1) * size], tiles[a, b]), v[b * size : (b + 1) * size])
                total = part if total is None else total + part
            out_ref[a * size : (a + 1) * size, cols] = total


def norm_kernel(q_ref, g_ref, intra_ref, st_ref, cum_ref, cumt_ref, gain_ref, og_ref, m_ref):
    for j in range(HB):
        cols = _lanes(j)
        col, _, grow, _ = _head_vectors(cum_ref, cumt_ref, j)
        q = q_ref[:, cols]
        attended = intra_ref[:, cols] + grow * _nn(q, st_ref[j])
        width = attended.shape[-1]
        root_mean = jnp.sqrt(jnp.sum(attended * attended, axis=-1, keepdims=True) / width + epsilon)
        normed = attended / root_mean
        grad_f = g_ref[:, cols].astype(jnp.float32)
        scaled = gain_ref[j] * grad_f
        projected = jnp.sum(scaled * attended, axis=-1, keepdims=True)
        out_grad = ((scaled - attended * projected / (width * root_mean * root_mean)) / root_mean).astype(
            jnp.bfloat16
        )
        og_ref[:, cols] = out_grad
        q_scaled = (q.astype(jnp.float32) * grow).astype(jnp.bfloat16)
        m_ref[j, :DH, :] = _tn(q_scaled, out_grad)
        m_ref[j, DH:, :] = _pad_rows(col[col.shape[0] - 1 :, :], jnp.sum(grad_f * normed, axis=0, keepdims=True))


def grads_kernel(first, hb, q_ref, k_ref, v_ref, og_ref, cum_ref, cumt_ref, st_ref, qg_ref, kg_ref, vg_ref):
    for j in range(hb):
        cols = _lanes(j)
        col, row, grow, _ = _head_vectors(cum_ref, cumt_ref, j, first, hb)
        tiles, size = _tile_decays(col, row)
        q, k, v, og = q_ref[:, cols], k_ref[:, cols], v_ref[:, cols], og_ref[:, cols]
        part = lambda x, i: x[i * size : (i + 1) * size]
        qg = [None, None]
        kg = [None, None]
        vg = [None, None]

        def add(acc, i, value):
            acc[i] = value if acc[i] is None else acc[i] + value

        for a in range(2):
            for b in range(a + 1):
                masked = _masked(part(q, a), part(k, b), tiles[a, b])
                rgrad = (_nt(part(og, a), part(v, b)) * tiles[a, b]).astype(jnp.bfloat16)
                add(qg, a, _nn(rgrad, part(k, b)))
                add(kg, b, _tn(rgrad, part(q, a)))
                add(vg, b, _tn(masked, part(og, a)))
        state_part = grow * _nt(og, st_ref[j])
        for a in range(2):
            rows = slice(a * size, (a + 1) * size)
            qg_ref[rows, cols] = (qg[a] + state_part[rows]).astype(jnp.bfloat16)
            kg_ref[rows, cols] = kg[a]
            vg_ref[rows, cols] = vg[a]


def finish_kernel(k_ref, v_ref, kg_ref, vg_ref, gl_ref, cum_ref, cumt_ref, ko_ref, vo_ref):
    for j in range(HB):
        cols = _lanes(j)
        _, _, _, toend = _head_vectors(cum_ref, cumt_ref, j)
        grad_low = gl_ref[j]
        ko_ref[:, cols] = (kg_ref[:, cols] + toend * _nt(v_ref[:, cols], grad_low)).astype(jnp.bfloat16)
        vo_ref[:, cols] = (vg_ref[:, cols] + toend * _nn(k_ref[:, cols], grad_low)).astype(jnp.bfloat16)


def _per_head(kernel, ins, outs, heads, length, flops, nbytes, exps=0, part=None, into=None, wide=False):
    hb = HB if part is None else HB // PIECE_STEPS
    if wide:
        hb = min(4 * HB, heads)
        kernel = functools.partial(kernel, hb)
    groups = heads // hb
    first, count = (0, groups) if part is None else (part * PIECE_STEPS, PIECE_STEPS)
    if part is not None:
        kernel = functools.partial(kernel, first, hb)

    def spec(kind):
        if kind == "rows":
            return pl.BlockSpec((length, hb * DH), lambda i: (0, i + first))
        if kind == "cum":
            return pl.BlockSpec((length, heads), lambda i: (0, 0))
        if kind == "cumt":
            return pl.BlockSpec((heads, length), lambda i: (0, 0))
        if kind == "gain":
            return pl.BlockSpec((hb, 1, DH), lambda i: (i + first, 0, 0))
        if kind == "message":
            return pl.BlockSpec((hb, DH + PAD, DH), lambda i: (i + first, 0, 0))
        return pl.BlockSpec((hb, DH, DH), lambda i: (i + first, 0, 0))

    shapes = {
        "rows": (length, heads * DH),
        "gain": (heads, 1, DH),
        "square": (heads, DH, DH),
        "message": (heads, DH + PAD, DH),
    }
    out_shape = [jax.ShapeDtypeStruct(shapes[kind], dtype) for kind, dtype in outs]
    in_specs = [spec(kind) for kind, _ in ins]
    operands = [x for _, x in ins]
    aliases = {}
    body = kernel
    if into is not None:
        given = len(ins)
        in_specs += [pl.BlockSpec(memory_space=pl.ANY) for _ in into]
        operands += list(into)
        aliases = {given + i: i for i in range(len(into))}

        def body(*refs):
            kernel(*refs[:given], *refs[given + len(into) :])

    share = count / groups
    return pl.pallas_call(
        body,
        grid=(count,),
        in_specs=in_specs,
        out_specs=[spec(kind) for kind, _ in outs],
        out_shape=out_shape,
        input_output_aliases=aliases,
        cost_estimate=pl.CostEstimate(
            flops=int(flops * share), transcendentals=int(exps * share), bytes_accessed=int(nbytes * share)
        ),
    )(*operands)


def on_device(query_rows, key_rows, value_rows, cotangent, log_decay, norm_gain):
    length = query_rows.shape[0]
    heads = log_decay.shape[1]
    f32 = jnp.float32
    bf16 = jnp.bfloat16
    t = lax.broadcasted_iota(jnp.int32, (length, length), 0)
    s = lax.broadcasted_iota(jnp.int32, (length, length), 1)
    lower = (t >= s).astype(f32)
    exact = lax.Precision.HIGHEST
    cum = jnp.dot(lower, log_decay, precision=exact)
    cum_t = lax.dot_general(log_decay, lower, (((0,), (1,)), ((), ())), precision=exact)
    final_log = cum[-1]
    gain_rows = norm_gain.reshape(heads, 1, DH)
    q, k, v, g = query_rows, key_rows, value_rows, cotangent
    big = length * length * DH * 2 * heads
    small = length * DH * DH * 2 * heads
    rows_bytes = length * heads * DH * 2
    (local_state,) = _per_head(
        local_state_kernel,
        [("rows", k), ("rows", v), ("cum", cum), ("cumt", cum_t)],
        [("message", f32)],
        heads, length, small, 2 * rows_bytes, wide=True,
    )
    def intra_piece(part, done, anchor):
        q_tied, _ = lax.optimization_barrier((q, anchor))
        return _per_head(
            intra_kernel,
            [("rows", q_tied), ("rows", k), ("rows", v), ("cum", cum), ("cumt", cum_t)],
            [("rows", f32)],
            heads, length, 2 * big, 5 * rows_bytes, heads * length * length, part=part, into=done,
        )

    groups = heads // HB
    state_in, (intra,) = forward_states(
        local_state, final_log, [functools.partial(intra_piece, p) for p in range(groups)]
    )
    state_low = state_in.astype(bf16)
    out_grad, moment = _per_head(
        norm_kernel,
        [("rows", q), ("rows", g), ("rows", intra), ("square", state_low), ("cum", cum), ("cumt", cum_t), ("gain", gain_rows)],
        [("rows", bf16), ("message", f32)],
        heads, length, 2 * small, 5 * rows_bytes,
    )
    def grads_piece(part, done, anchor):
        og_tied, _ = lax.optimization_barrier((out_grad, anchor))
        return _per_head(
            grads_kernel,
            [("rows", q), ("rows", k), ("rows", v), ("rows", og_tied), ("cum", cum), ("cumt", cum_t),
             ("square", state_low)],
            [("rows", bf16), ("rows", f32), ("rows", f32)],
            heads, length, 5 * big + small, 9 * rows_bytes, heads * length * length, part=part, into=done,
        )

    grad_state, gain_sum, (query_grad, key_part, value_part) = backward_states(
        moment, final_log, [functools.partial(grads_piece, p) for p in range(groups)]
    )
    grad_low = grad_state.astype(bf16)
    key_grad, value_grad = _per_head(
        finish_kernel,
        [("rows", k), ("rows", v), ("rows", key_part), ("rows", value_part), ("square", grad_low),
         ("cum", cum), ("cumt", cum_t)],
        [("rows", bf16), ("rows", bf16)],
        heads, length, 2 * small, 8 * rows_bytes,
    )
    seq_total = length * lax.axis_size(("ctx", "dp"))
    gain_grad = gain_sum * (1.0 / math.sqrt(seq_total))
    return (query_grad, key_grad, value_grad, gain_grad)


def solution(mesh):
    return jax.shard_map(
        on_device,
        mesh=mesh,
        in_specs=(
            P(("groups", "ctx", "dp"), "head"),
            P(("groups", "ctx", "dp"), "head"),
            P(("groups", "ctx", "dp"), "head"),
            P(("groups", "ctx", "dp"), "head"),
            P(("groups", "ctx", "dp"), "head"),
            P("head"),
        ),
        out_specs=(
            P(("groups", "ctx", "dp"), "head"),
            P(("groups", "ctx", "dp"), "head"),
            P(("groups", "ctx", "dp"), "head"),
            P(("groups", "head")),
        ),
        check_vma=False,
    )
```
